256 devices in a mesh: group: 8 (over x, core), dev: 32 (over y, z).
Axes of the slice: x: 4, y: 4, z: 8, core: 2. Of those that a mesh axis runs over, the one named last changes fastest.
Arguments:
- em_image: bfloat16 [256, 1024, 512], P('group', 'dev'), may hold values from -6 to 6
- level_set: float32 [256, 1024, 512], P('group', 'dev'), may hold values from -6 to 6
- speeds: float32 [8], replicated, may hold values from -1 to 1.5
- brick_of_band: int32 [2048], P(('group', 'dev')), may hold values from 0 to 4095, as said below
- neighbours: int32 [4096, 6], P(('group', 'dev')), may hold values from -1 to 2047, as said below
- speed_index: int32 [4096], P(('group', 'dev')), may hold values from 0 to 7
Outputs:
- level_out: float32 [2048, 16, 16, 128], P(('group', 'dev'))
The draws below stay inside these ranges and needn't reach their ends.
Inputs may be any that keep to these rules, and one draw needn't show every extreme that they name: `brick_of_band`: bricks are numbered as in the reference program. No brick is named twice. Band index j names a brick of the slab group of device j // 8. No device holds two bricks named by band indices that go to the same device j // 8. `neighbours`: entry k of brick b's list (sides x-, x+, y-, y+, z-, z+) is the band index j with brick_of_band[j] equal to the brick beside b on side k, or -1 where that side is the volume's boundary or the brick beside has no band index.
All inputs are finite; a program needn't handle non-finite values.
Results may differ from the reference program's by a relative error of at most 0.0003.
Values may be sent and summed in bfloat16 or wider, within the bound.
No kernel may reach another device: no remote copies, remote signals or barrier semaphores. Data moves between devices by JAX's collectives and lax.ppermute only.
A program may use at most 64 MiB of HBM per device.

```python
import math
import jax
import jax.numpy as jnp
import numpy as np
from jax import lax

BX = 16
BY = 16
BZ = 128
BXN = 2
BYN = 2
BZN = 4
K = 8
STEPS = 4
NSPEED = 8
GROUPS = 8
PEERS = 32
ZB = 16
NX = 256
NY = 1024
NZ = 512
NBRICKS = 4096
NBAND = 2048
DEVICES = 256


def layer_counts():
    plane_bricks = BXN * BYN
    total_layers = PEERS * K // plane_bricks
    deepest = min(BZN, PEERS // plane_bricks)
    profile = [0] * PEERS
    remain = total_layers
    for position in range(PEERS):
        take_now = min(max(1, deepest - position // 2), remain)
        profile[position] = take_now
        remain = remain - take_now
    for position in range(PEERS):
        extra_layers = min(deepest - profile[position], remain)
        profile[position] = profile[position] + extra_layers
        remain = remain - extra_layers
    visit_order = [0]
    step_out = 1
    while len(visit_order) < PEERS:
        for direction in (1, -1):
            offset = direction * step_out % PEERS
            if offset not in visit_order and len(visit_order) < PEERS:
                visit_order.append(offset)
        step_out = step_out + 1
    counts_table = np.zeros(PEERS, np.int32)
    for position in range(PEERS):
        counts_table[visit_order[position]] = profile[position]
    return counts_table


def band_layout(key):
    base_key = jax.random.fold_in(key, 7)
    key_centre, key_base, key_jitter = jax.random.split(base_key, 3)
    bricks_dev = BXN * BYN * BZN
    centre = jax.random.randint(key_centre, (GROUPS,), 0, PEERS)
    counts_table = jnp.asarray(layer_counts())
    offset_rows = (jnp.arange(PEERS)[None, :] - centre[:, None]) % PEERS
    layers = counts_table[offset_rows]
    base_layer = jax.random.randint(key_base, (GROUPS, 1), 0, BZN)
    jitter = jax.random.randint(key_jitter, (GROUPS, PEERS), -1, 2)
    first_layer = jnp.clip(base_layer + jitter, 0, BZN - layers)
    brick_depth = jnp.arange(bricks_dev) % BZN
    chosen = (brick_depth[None, None, :] >= first_layer[:, :, None]) & (brick_depth[None, None, :] < (first_layer + layers)[:, :, None])
    band_flags = chosen.reshape(GROUPS, PEERS * bricks_dev).astype(jnp.int32)
    band_rank = jnp.cumsum(band_flags, axis=1) - band_flags
    group_start = jnp.arange(GROUPS)[:, None] * (PEERS * K)
    band_index = group_start + band_rank % PEERS * K + band_rank // PEERS
    return jnp.where(band_flags > 0, band_index, -1).reshape(-1).astype(jnp.int32)


def draw_brick_of_band(key, part):
    band_index = band_layout(key)
    target = jnp.where(band_index >= 0, band_index, NBAND)
    filled = jnp.zeros((NBAND + 1,), jnp.int32).at[target].set(jnp.arange(NBRICKS, dtype=jnp.int32))
    return filled[:NBAND]


def draw_neighbours(key, part):
    band_index = band_layout(key)
    bricks_dev = BXN * BYN * BZN
    brick_ids = jnp.arange(NBRICKS, dtype=jnp.int32)
    device = brick_ids // bricks_dev
    inside = brick_ids % bricks_dev
    across_x = device // PEERS * BXN + inside // (BYN * BZN)
    across_y = device % PEERS * BYN + inside // BZN % BYN
    across_z = inside % BZN
    columns = []
    for move_x, move_y, move_z in ((-1, 0, 0), (1, 0, 0), (0, -1, 0), (0, 1, 0), (0, 0, -1), (0, 0, 1)):
        pos_x = across_x + move_x
        pos_y = across_y + move_y
        pos_z = across_z + move_z
        inside_grid = (pos_x >= 0) & (pos_x < GROUPS * BXN) & (pos_y >= 0) & (pos_y < PEERS * BYN) & (pos_z >= 0) & (pos_z < BZN)
        beside_id = (pos_x // BXN * PEERS + pos_y // BYN) * bricks_dev + (pos_x % BXN * BYN + pos_y % BYN) * BZN + pos_z
        beside_id = jnp.clip(beside_id, 0, NBRICKS - 1)
        columns.append(jnp.where(inside_grid, band_index[beside_id], -1))
    return jnp.stack(columns, axis=1).astype(jnp.int32)


def touch_ends(values, stream_key, least, top_value):
    dims = values.shape
    index_at = [jax.random.randint(jax.random.fold_in(stream_key, axis), (), 0, dims[axis]) for axis in range(len(dims))]
    values = values.at[tuple(index_at)].set(least)
    longest = dims.index(max(dims))
    index_at[longest] = (index_at[longest] + 1) % dims[longest]
    return values.at[tuple(index_at)].set(top_value)


def block_levels(key, shape, cuts, low, largest):
    def one(dim, parts):
        heights = jax.random.uniform(jax.random.fold_in(jax.random.fold_in(key, 6), dim), (parts,), jnp.float32, low / len(cuts), largest / len(cuts))
        return jnp.repeat(jnp.exp(heights), shape[dim] // parts).reshape((-1,) + (1,) * (len(shape) - dim - 1))

    level = one(*cuts[0])
    for cut in cuts[1:]:
        level = level * one(*cut)
    return level


def gaussian(rng, extent, width, most, cuts=(), kind=jnp.bfloat16):
    values = width * jax.random.normal(rng, extent, jnp.float32)
    if cuts:
        values = values * block_levels(rng, extent, cuts, -0.22, 0.18)
    return jnp.clip(values, -most, most).astype(kind)


def setup_inputs(seed: int = 0) -> dict:
    key_list = jax.random.split(jax.random.key(seed), 7)
    return {
        "em_image": gaussian(key_list[0], (NX, NY, NZ), 1.0, 6.0, ((0, 8), (1, 32))),
        "level_set": gaussian(key_list[1], (NX, NY, NZ), 1.0, 6.0, ((0, 8), (1, 32)), jnp.float32),
        "speeds": jnp.clip(jax.random.uniform(key_list[2], (NSPEED,), jnp.float32, -1.0, 1.5), -1.0, 1.5),
        "brick_of_band": draw_brick_of_band(jax.random.fold_in(key_list[6], 71), 0),
        "neighbours": draw_neighbours(jax.random.fold_in(key_list[6], 71), 0),
        "speed_index": touch_ends(jax.random.randint(key_list[5], (NBRICKS,), 0, NSPEED), jax.random.fold_in(key_list[5], 1), 0, NSPEED - 1).astype(jnp.int32),
    }


gauss_raw = [math.exp(-0.5 * position * position) for position in range(-2, 3)]
gauss_taps = [weight / sum(gauss_raw) for weight in gauss_raw]
time_step = 0.2
smoothing = 0.15
contrast = 0.02

def smooth_axis(values, along):
    length = values.shape[along] - 4
    summed = gauss_taps[0] * lax.slice_in_dim(values, 0, length, axis=along)
    for offset in range(1, 5):
        summed = summed + gauss_taps[offset] * lax.slice_in_dim(values, offset, offset + length, axis=along)
    return summed

def edge_map(window):
    smoothed = smooth_axis(smooth_axis(smooth_axis(window, 0), 1), 2)
    grad_x = (smoothed[2:, 1:-1, 1:-1] - smoothed[:-2, 1:-1, 1:-1]) * 0.5
    grad_y = (smoothed[1:-1, 2:, 1:-1] - smoothed[1:-1, :-2, 1:-1]) * 0.5
    grad_z = (smoothed[1:-1, 1:-1, 2:] - smoothed[1:-1, 1:-1, :-2]) * 0.5
    return 1.0 / (1.0 + (grad_x * grad_x + grad_y * grad_y + grad_z * grad_z) / contrast)

def own_faces(levels):
    side_faces = jnp.stack([levels[:, 0], levels[:, -1], levels[:, :, 0], levels[:, :, -1]], axis=1)
    end_faces = jnp.stack([levels[:, :, :, 0], levels[:, :, :, -1]], axis=1)
    return (side_faces, end_faces)

def advance(levels, side_ghost, end_ghost, edge_maps, speed_rows):
    with_z = jnp.concatenate([end_ghost[:, 0][..., None], levels, end_ghost[:, 1][..., None]], axis=3)
    y_faces = jnp.pad(side_ghost[:, 2:4], ((0, 0), (0, 0), (0, 0), (1, 1)))
    with_y = jnp.concatenate([y_faces[:, 0][:, :, None, :], with_z, y_faces[:, 1][:, :, None, :]], axis=2)
    x_faces = jnp.pad(side_ghost[:, 0:2], ((0, 0), (0, 0), (1, 1), (1, 1)))
    padded = jnp.concatenate([x_faces[:, 0][:, None], with_y, x_faces[:, 1][:, None]], axis=1)
    centre = padded[:, 1:-1, 1:-1, 1:-1]
    minus_x = padded[:, :-2, 1:-1, 1:-1]
    plus_x = padded[:, 2:, 1:-1, 1:-1]
    minus_y = padded[:, 1:-1, :-2, 1:-1]
    plus_y = padded[:, 1:-1, 2:, 1:-1]
    minus_z = padded[:, 1:-1, 1:-1, :-2]
    plus_z = padded[:, 1:-1, 1:-1, 2:]
    laplace = plus_x + minus_x + (plus_y + minus_y) + (plus_z + minus_z) - 6.0 * centre
    diff_x = (plus_x - minus_x) * 0.5
    diff_y = (plus_y - minus_y) * 0.5
    diff_z = (plus_z - minus_z) * 0.5
    gradient = diff_x * diff_x + diff_y * diff_y + diff_z * diff_z
    force = smoothing * laplace + speed_rows[:, None, None, None]
    return centre + time_step * edge_maps * force * jnp.sqrt(1.0 + gradient)

def ghost_layer(faces, links, which, opposite):
    found = faces[jnp.maximum(links, 0), opposite]
    return jnp.where((links >= 0)[:, None, None], found, faces[:, which])

def advance_items(items):
    return advance(items[0], items[1], items[2], items[3], items[4])

def reference(em_image, level_set, speeds, brick_of_band, neighbours, speed_index):
    padded_image = jnp.pad(em_image, 3)

    def start_brick(brick_id):
        device = brick_id // ZB
        inside = brick_id % ZB
        group_no = device // PEERS
        dev_no = device % PEERS
        start_x = (group_no * BXN + inside // (BYN * BZN)) * BX
        start_y = (dev_no * BYN + inside // BZN % BYN) * BY
        start_z = inside % BZN * BZ
        corner = (start_x.astype(jnp.int32), start_y.astype(jnp.int32), start_z.astype(jnp.int32))
        level = lax.dynamic_slice(level_set, corner, (BX, BY, BZ))
        window = lax.dynamic_slice(padded_image, corner, (BX + 6, BY + 6, BZ + 6)).astype(jnp.float32)
        return (level, edge_map(window))
    levels, edge_maps = lax.map(start_brick, brick_of_band)
    beside_lists = neighbours[brick_of_band]
    speed_rows = speeds[speed_index[brick_of_band]]
    for repeat in range(STEPS):
        side_faces, end_faces = own_faces(levels)
        side_ghost = jnp.stack([ghost_layer(side_faces, beside_lists[:, side_no], side_no, (1, 0, 3, 2)[side_no]) for side_no in range(4)], axis=1)
        end_ghost = jnp.stack([ghost_layer(end_faces, beside_lists[:, 4 + side_no], side_no, 1 - side_no) for side_no in range(2)], axis=1)
        shaped = tuple((array.reshape((DEVICES, K) + array.shape[1:]) for array in (levels, side_ghost, end_ghost, edge_maps, speed_rows)))
        levels = lax.map(advance_items, shaped).reshape(levels.shape)
    return levels
```

```python
import math

import jax
import jax.numpy as jnp
from jax import lax
from jax.sharding import PartitionSpec as P

BX = 16
BY = 16
BZ = 128
BXN = 2
BYN = 2
BZN = 4
STEPS = 4


gauss_raw = [math.exp(-0.5 * position * position) for position in range(-2, 3)]
gauss_taps = [weight / sum(gauss_raw) for weight in gauss_raw]
time_step = 0.2
smoothing = 0.15
contrast = 0.02


def shortened(value):
    return jax.tree.map(lambda a: a.astype(jnp.bfloat16) if a.dtype == jnp.float32 else a, value)


def extended(cells, sides, width):
    for axis, dim in sides:
        count = lax.axis_size(axis)
        ends = count - 1
        head = lax.slice_in_dim(cells, 0, width, axis=dim)
        tail = lax.slice_in_dim(cells, cells.shape[dim] - width, cells.shape[dim], axis=dim)
        cells = jnp.concatenate(
            [
                lax.ppermute(tail, axis, [(i, (i + 1) % count) for i in range(ends)]),
                cells,
                lax.ppermute(head, axis, [((i + 1) % count, i) for i in range(ends)]),
            ],
            axis=dim,
        )
    return cells


def smooth_axis(values, along):
    length = values.shape[along] - 4
    summed = gauss_taps[0] * lax.slice_in_dim(values, 0, length, axis=along)
    for offset in range(1, 5):
        summed = summed + gauss_taps[offset] * lax.slice_in_dim(
            values, offset, offset + length, axis=along
        )
    return summed


def edge_map(window):
    smoothed = smooth_axis(smooth_axis(smooth_axis(window, 0), 1), 2)
    grad_x = (smoothed[2:, 1:-1, 1:-1] - smoothed[:-2, 1:-1, 1:-1]) * 0.5
    grad_y = (smoothed[1:-1, 2:, 1:-1] - smoothed[1:-1, :-2, 1:-1]) * 0.5
    grad_z = (smoothed[1:-1, 1:-1, 2:] - smoothed[1:-1, 1:-1, :-2]) * 0.5
    return 1.0 / (1.0 + (grad_x * grad_x + grad_y * grad_y + grad_z * grad_z) / contrast)


def to_bricks(block):
    shaped = block.reshape(BXN, BX, BYN, BY, BZN, BZ)
    return shaped.transpose(0, 2, 4, 1, 3, 5).reshape(BXN * BYN * BZN, BX, BY, BZ)


def own_faces(levels):
    side_faces = jnp.stack([levels[:, 0], levels[:, -1], levels[:, :, 0], levels[:, :, -1]], axis=1)
    end_faces = jnp.stack([levels[:, :, :, 0], levels[:, :, :, -1]], axis=1)
    return (side_faces, end_faces)


def advance(levels, side_ghost, end_ghost, edge_maps, speed_rows):
    with_z = jnp.concatenate(
        [end_ghost[:, 0][..., None], levels, end_ghost[:, 1][..., None]], axis=3
    )
    y_faces = jnp.pad(side_ghost[:, 2:4], ((0, 0), (0, 0), (0, 0), (1, 1)))
    with_y = jnp.concatenate(
        [y_faces[:, 0][:, :, None, :], with_z, y_faces[:, 1][:, :, None, :]], axis=2
    )
    x_faces = jnp.pad(side_ghost[:, 0:2], ((0, 0), (0, 0), (1, 1), (1, 1)))
    padded = jnp.concatenate([x_faces[:, 0][:, None], with_y, x_faces[:, 1][:, None]], axis=1)
    centre = padded[:, 1:-1, 1:-1, 1:-1]
    minus_x = padded[:, :-2, 1:-1, 1:-1]
    plus_x = padded[:, 2:, 1:-1, 1:-1]
    minus_y = padded[:, 1:-1, :-2, 1:-1]
    plus_y = padded[:, 1:-1, 2:, 1:-1]
    minus_z = padded[:, 1:-1, 1:-1, :-2]
    plus_z = padded[:, 1:-1, 1:-1, 2:]
    laplace = plus_x + minus_x + (plus_y + minus_y) + (plus_z + minus_z) - 6.0 * centre
    diff_x = (plus_x - minus_x) * 0.5
    diff_y = (plus_y - minus_y) * 0.5
    diff_z = (plus_z - minus_z) * 0.5
    gradient = diff_x * diff_x + diff_y * diff_y + diff_z * diff_z
    force = smoothing * laplace + speed_rows[:, None, None, None]
    return centre + time_step * edge_maps * force * jnp.sqrt(1.0 + gradient)


def assemble_ghosts(side_faces, end_faces, beside_lists):
    face_grid = side_faces.reshape((BXN, BYN, BZN) + side_faces.shape[1:])
    widened = extended(shortened(face_grid), (("group", 0), ("dev", 1)), 1).astype(face_grid.dtype)
    from_side = jnp.stack(
        [
            widened[:-2, 1:-1, :, 1],
            widened[2:, 1:-1, :, 0],
            widened[1:-1, :-2, :, 3],
            widened[1:-1, 2:, :, 2],
        ],
        axis=3,
    ).reshape(side_faces.shape)
    end_grid = end_faces.reshape((BXN, BYN, BZN) + end_faces.shape[1:])
    zero_faces = jnp.zeros_like(end_grid[:, :, :1, 0])
    lower_ghost = jnp.concatenate([zero_faces, end_grid[:, :, :-1, 1]], axis=2)
    upper_ghost = jnp.concatenate([end_grid[:, :, 1:, 0], zero_faces], axis=2)
    from_ends = jnp.stack([lower_ghost, upper_ghost], axis=3).reshape(end_faces.shape)
    linked = beside_lists >= 0
    side_ghost = jnp.where(linked[:, :4, None, None], from_side, side_faces)
    end_ghost = jnp.where(linked[:, 4:, None, None], from_ends, end_faces)
    return (side_ghost, end_ghost)


def place_rows(values, target, usable, partners):
    items = values.shape[0]
    matches = (target[None, :] == jnp.arange(partners)[:, None]) & usable[None, :]
    chosen = jnp.sum(jnp.where(matches, jnp.arange(items)[None, :], 0), axis=1)
    present = jnp.any(matches, axis=1)
    picked = jnp.take(values, chosen, axis=0)
    return jnp.where(
        present.reshape((partners,) + (1,) * (values.ndim - 1)), picked, jnp.zeros((), values.dtype)
    )


def halo_planes(cells, axis, dim):
    count = lax.axis_size(axis)
    ends = count - 1
    head = lax.slice_in_dim(cells, 0, 1, axis=dim)
    tail = lax.slice_in_dim(cells, cells.shape[dim] - 1, cells.shape[dim], axis=dim)
    from_below = lax.ppermute(tail, axis, [(i, i + 1) for i in range(ends)])
    from_above = lax.ppermute(head, axis, [(i + 1, i) for i in range(ends)])
    return from_below, from_above


def brick_field(per_brick, shape):
    grid = per_brick.reshape(BXN, 1, BYN, 1, BZN, 1)
    grid = jnp.broadcast_to(grid, (BXN, BX, BYN, BY, BZN, BZ))
    return grid.reshape(shape)


def dense_step(lvl, edge, rate, uses):
    below_x, above_x = halo_planes(lvl, "group", 0)
    below_y, above_y = halo_planes(lvl, "dev", 1)
    zero_z = jnp.zeros_like(lvl[:, :, :1])
    shifted = (
        jnp.concatenate([below_x, lvl[:-1]], axis=0),
        jnp.concatenate([lvl[1:], above_x], axis=0),
        jnp.concatenate([below_y, lvl[:, :-1]], axis=1),
        jnp.concatenate([lvl[:, 1:], above_y], axis=1),
        jnp.concatenate([zero_z, lvl[:, :, :-1]], axis=2),
        jnp.concatenate([lvl[:, :, 1:], zero_z], axis=2),
    )
    minus_x, plus_x, minus_y, plus_y, minus_z, plus_z = (
        jnp.where(use, value, lvl) for use, value in zip(uses, shifted)
    )
    centre = lvl
    laplace = plus_x + minus_x + (plus_y + minus_y) + (plus_z + minus_z) - 6.0 * centre
    diff_x = (plus_x - minus_x) * 0.5
    diff_y = (plus_y - minus_y) * 0.5
    diff_z = (plus_z - minus_z) * 0.5
    gradient = diff_x * diff_x + diff_y * diff_y + diff_z * diff_z
    force = smoothing * laplace + rate
    return centre + time_step * edge * force * jnp.sqrt(1.0 + gradient)


def per_device(em_image, level_set, speeds, brick_of_band, neighbours, speed_index):
    partners = lax.axis_size("dev")
    margin = extended(em_image, (("group", 0), ("dev", 1)), 3)
    window = jnp.pad(margin.astype(jnp.float32), ((0, 0), (0, 0), (3, 3)))
    edge = edge_map(window)
    shape = level_set.shape
    bricks_here = BXN * BYN * BZN
    choose = speed_index[:, None] == jnp.arange(speeds.shape[0])[None, :]
    rates_here = jnp.sum(jnp.where(choose, speeds[None, :], 0.0), axis=1)
    rate = brick_field(rates_here, shape)
    linked = neighbours >= 0
    sizes = (BX, BX, BY, BY, BZ, BZ)
    axes = (0, 0, 1, 1, 2, 2)
    uses = []
    for side in range(6):
        link = brick_field(linked[:, side], shape)
        pos = lax.broadcasted_iota(jnp.int32, shape, axes[side]) % sizes[side]
        inner = pos != (0 if side % 2 == 0 else sizes[side] - 1)
        uses.append(inner | link)
    lvl = level_set
    for repeat in range(STEPS):
        lvl = dense_step(lvl, edge, rate, uses)
    level_bricks = to_bricks(lvl)
    band_here = brick_of_band.shape[0]
    group_bands = lax.all_gather(brick_of_band, "dev", axis=0, tiled=True)
    device_here = lax.axis_index("group") * partners + lax.axis_index("dev")
    local_ids = device_here * bricks_here + jnp.arange(bricks_here, dtype=jnp.int32)
    found = group_bands[None, :] == local_ids[:, None]
    in_band = jnp.any(found, axis=1)
    band_place = jnp.sum(
        jnp.where(found, jnp.arange(group_bands.shape[0], dtype=jnp.int32)[None, :], 0), axis=1
    )
    owner_dev = band_place // band_here
    source_dev = brick_of_band // bricks_here % partners
    arrived = lax.all_to_all(
        place_rows(level_bricks, owner_dev, in_band, partners),
        "dev",
        split_axis=0,
        concat_axis=0,
        tiled=True,
    )
    return jnp.take(arrived, source_dev, axis=0)


def solution(mesh):
    placed = (
        P("group", "dev", None),
        P("group", "dev", None),
        P(),
        P(("group", "dev")),
        P(("group", "dev"), None),
        P(("group", "dev")),
    )
    return jax.shard_map(
        per_device,
        mesh=mesh,
        in_specs=placed,
        out_specs=P(("group", "dev"), None, None, None),
        check_vma=False,
    )
```

```python
import math

import jax
import jax.numpy as jnp
from jax import lax
from jax.sharding import PartitionSpec as P

BX = 16
BY = 16
BZ = 128
BXN = 2
BYN = 2
BZN = 4
STEPS = 4


gauss_raw = [math.exp(-0.5 * position * position) for position in range(-2, 3)]
gauss_taps = [weight / sum(gauss_raw) for weight in gauss_raw]
time_step = 0.2
smoothing = 0.15
contrast = 0.02


def shortened(value):
    return jax.tree.map(lambda a: a.astype(jnp.bfloat16) if a.dtype == jnp.float32 else a, value)


def extended(cells, sides, width):
    for axis, dim in sides:
        count = lax.axis_size(axis)
        ends = count - 1
        head = lax.slice_in_dim(cells, 0, width, axis=dim)
        tail = lax.slice_in_dim(cells, cells.shape[dim] - width, cells.shape[dim], axis=dim)
        cells = jnp.concatenate(
            [
                lax.ppermute(tail, axis, [(i, (i + 1) % count) for i in range(ends)]),
                cells,
                lax.ppermute(head, axis, [((i + 1) % count, i) for i in range(ends)]),
            ],
            axis=dim,
        )
    return cells


def smooth_axis(values, along):
    length = values.shape[along] - 4
    summed = gauss_taps[0] * lax.slice_in_dim(values, 0, length, axis=along)
    for offset in range(1, 5):
        summed = summed + gauss_taps[offset] * lax.slice_in_dim(
            values, offset, offset + length, axis=along
        )
    return summed


def edge_map(window):
    smoothed = smooth_axis(smooth_axis(smooth_axis(window, 0), 1), 2)
    grad_x = (smoothed[2:, 1:-1, 1:-1] - smoothed[:-2, 1:-1, 1:-1]) * 0.5
    grad_y = (smoothed[1:-1, 2:, 1:-1] - smoothed[1:-1, :-2, 1:-1]) * 0.5
    grad_z = (smoothed[1:-1, 1:-1, 2:] - smoothed[1:-1, 1:-1, :-2]) * 0.5
    return 1.0 / (1.0 + (grad_x * grad_x + grad_y * grad_y + grad_z * grad_z) / contrast)


def to_bricks(block):
    shaped = block.reshape(BXN, BX, BYN, BY, BZN, BZ)
    return shaped.transpose(0, 2, 4, 1, 3, 5).reshape(BXN * BYN * BZN, BX, BY, BZ)


def own_faces(levels):
    side_faces = jnp.stack([levels[:, 0], levels[:, -1], levels[:, :, 0], levels[:, :, -1]], axis=1)
    end_faces = jnp.stack([levels[:, :, :, 0], levels[:, :, :, -1]], axis=1)
    return (side_faces, end_faces)


def advance(levels, side_ghost, end_ghost, edge_maps, speed_rows):
    with_z = jnp.concatenate(
        [end_ghost[:, 0][..., None], levels, end_ghost[:, 1][..., None]], axis=3
    )
    y_faces = jnp.pad(side_ghost[:, 2:4], ((0, 0), (0, 0), (0, 0), (1, 1)))
    with_y = jnp.concatenate(
        [y_faces[:, 0][:, :, None, :], with_z, y_faces[:, 1][:, :, None, :]], axis=2
    )
    x_faces = jnp.pad(side_ghost[:, 0:2], ((0, 0), (0, 0), (1, 1), (1, 1)))
    padded = jnp.concatenate([x_faces[:, 0][:, None], with_y, x_faces[:, 1][:, None]], axis=1)
    centre = padded[:, 1:-1, 1:-1, 1:-1]
    minus_x = padded[:, :-2, 1:-1, 1:-1]
    plus_x = padded[:, 2:, 1:-1, 1:-1]
    minus_y = padded[:, 1:-1, :-2, 1:-1]
    plus_y = padded[:, 1:-1, 2:, 1:-1]
    minus_z = padded[:, 1:-1, 1:-1, :-2]
    plus_z = padded[:, 1:-1, 1:-1, 2:]
    laplace = plus_x + minus_x + (plus_y + minus_y) + (plus_z + minus_z) - 6.0 * centre
    diff_x = (plus_x - minus_x) * 0.5
    diff_y = (plus_y - minus_y) * 0.5
    diff_z = (plus_z - minus_z) * 0.5
    gradient = diff_x * diff_x + diff_y * diff_y + diff_z * diff_z
    force = smoothing * laplace + speed_rows[:, None, None, None]
    return centre + time_step * edge_maps * force * jnp.sqrt(1.0 + gradient)


def assemble_ghosts(side_faces, end_faces, beside_lists):
    face_grid = side_faces.reshape((BXN, BYN, BZN) + side_faces.shape[1:])
    widened = extended(shortened(face_grid), (("group", 0), ("dev", 1)), 1).astype(face_grid.dtype)
    from_side = jnp.stack(
        [
            widened[:-2, 1:-1, :, 1],
            widened[2:, 1:-1, :, 0],
            widened[1:-1, :-2, :, 3],
            widened[1:-1, 2:, :, 2],
        ],
        axis=3,
    ).reshape(side_faces.shape)
    end_grid = end_faces.reshape((BXN, BYN, BZN) + end_faces.shape[1:])
    zero_faces = jnp.zeros_like(end_grid[:, :, :1, 0])
    lower_ghost = jnp.concatenate([zero_faces, end_grid[:, :, :-1, 1]], axis=2)
    upper_ghost = jnp.concatenate([end_grid[:, :, 1:, 0], zero_faces], axis=2)
    from_ends = jnp.stack([lower_ghost, upper_ghost], axis=3).reshape(end_faces.shape)
    linked = beside_lists >= 0
    side_ghost = jnp.where(linked[:, :4, None, None], from_side, side_faces)
    end_ghost = jnp.where(linked[:, 4:, None, None], from_ends, end_faces)
    return (side_ghost, end_ghost)


def place_rows(values, target, usable, partners):
    items = values.shape[0]
    matches = (target[None, :] == jnp.arange(partners)[:, None]) & usable[None, :]
    chosen = jnp.sum(jnp.where(matches, jnp.arange(items)[None, :], 0), axis=1)
    present = jnp.any(matches, axis=1)
    picked = jnp.take(values, chosen, axis=0)
    return jnp.where(
        present.reshape((partners,) + (1,) * (values.ndim - 1)), picked, jnp.zeros((), values.dtype)
    )


def extended_many(items, sides):
    cells = [value for value, width in items]
    widths = [width for value, width in items]
    for axis, dim in sides:
        count = lax.axis_size(axis)
        ends = count - 1
        heads = tuple(lax.slice_in_dim(c, 0, w, axis=dim) for c, w in zip(cells, widths))
        tails = tuple(
            lax.slice_in_dim(c, c.shape[dim] - w, c.shape[dim], axis=dim) for c, w in zip(cells, widths)
        )
        from_below = lax.ppermute(tails, axis, [(i, (i + 1) % count) for i in range(ends)])
        from_above = lax.ppermute(heads, axis, [((i + 1) % count, i) for i in range(ends)])
        cells = [
            jnp.concatenate([below, c, above], axis=dim)
            for below, c, above in zip(from_below, cells, from_above)
        ]
    return cells


def region_step(lvl, edge, rate, code):
    centre = lvl[1:-1, 1:-1]
    shifted = (
        lvl[:-2, 1:-1],
        lvl[2:, 1:-1],
        lvl[1:-1, :-2],
        lvl[1:-1, 2:],
        jnp.concatenate([centre[:, :, :1], centre[:, :, :-1]], axis=2),
        jnp.concatenate([centre[:, :, 1:], centre[:, :, -1:]], axis=2),
    )
    minus_x, plus_x, minus_y, plus_y, minus_z, plus_z = (
        jnp.where((code >> side) & 1 == 1, value, centre) for side, value in enumerate(shifted)
    )
    laplace = plus_x + minus_x + (plus_y + minus_y) + (plus_z + minus_z) - 6.0 * centre
    diff_x = (plus_x - minus_x) * 0.5
    diff_y = (plus_y - minus_y) * 0.5
    diff_z = (plus_z - minus_z) * 0.5
    gradient = diff_x * diff_x + diff_y * diff_y + diff_z * diff_z
    force = smoothing * laplace + rate
    return centre + time_step * edge * force * jnp.sqrt(1.0 + gradient)


def per_device(em_image, level_set, speeds, brick_of_band, neighbours, speed_index):
    partners = lax.axis_size("dev")
    bricks_here = BXN * BYN * BZN
    choose = speed_index[:, None] == jnp.arange(speeds.shape[0])[None, :]
    rates_here = jnp.sum(jnp.where(choose, speeds[None, :], 0.0), axis=1)
    info = jnp.concatenate(
        [(neighbours >= 0).astype(jnp.float32), rates_here[:, None]], axis=1
    ).reshape(BXN, BYN, BZN, 7)
    margin, wide_level, wide_info = extended_many(
        ((em_image, 3 + STEPS), (level_set, STEPS), (info, 1)), (("group", 0), ("dev", 1))
    )
    window = jnp.pad(margin.astype(jnp.float32), ((0, 0), (0, 0), (3, 3)))
    edge = edge_map(window)
    span_x, span_y, span_z = wide_level.shape
    lead = BX - STEPS
    weights = jnp.asarray([1 << side for side in range(6)] + [0], jnp.int32)
    brick_code = jnp.sum(jnp.where(wide_info > 0.5, weights, 0), axis=-1)
    def planes(per_brick):
        spread = jnp.broadcast_to(
            per_brick.reshape(BXN + 2, BYN + 2, 1, BZN, 1), (BXN + 2, BYN + 2, BY, BZN, BZ)
        ).reshape(BXN + 2, (BYN + 2) * BY, BZN * BZ)
        return spread[:, lead : lead + span_y]
    def across_x(per_brick):
        table = planes(per_brick)
        xe = lax.broadcasted_iota(jnp.int32, wide_level.shape, 0) + lead
        value = table[BXN + 1][None]
        for bx in range(BXN, -1, -1):
            value = jnp.where(xe < (bx + 1) * BX, table[bx][None], value)
        return value
    rate = across_x(wide_info[..., 6])
    place = (
        lax.broadcasted_iota(jnp.int32, wide_level.shape, 0) + lead,
        lax.broadcasted_iota(jnp.int32, wide_level.shape, 1) + lead,
        lax.broadcasted_iota(jnp.int32, wide_level.shape, 2),
    )
    sizes = (BX, BX, BY, BY, BZ, BZ)
    code = across_x(brick_code)
    for side in range(6):
        pos = place[side // 2] % sizes[side]
        inner = pos != (0 if side % 2 == 0 else sizes[side] - 1)
        code = code | (inner.astype(jnp.int32) << side)
    lvl = wide_level
    for repeat in range(STEPS):
        lo = repeat + 1
        hi_x = span_x - repeat - 1
        hi_y = span_y - repeat - 1
        lvl = region_step(lvl, edge[lo:hi_x, lo:hi_y], rate[lo:hi_x, lo:hi_y], code[lo:hi_x, lo:hi_y])
    level_bricks = to_bricks(lvl)
    band_here = brick_of_band.shape[0]
    group_bands = lax.all_gather(brick_of_band, "dev", axis=0, tiled=True)
    device_here = lax.axis_index("group") * partners + lax.axis_index("dev")
    local_ids = device_here * bricks_here + jnp.arange(bricks_here, dtype=jnp.int32)
    found = group_bands[None, :] == local_ids[:, None]
    in_band = jnp.any(found, axis=1)
    band_place = jnp.sum(
        jnp.where(found, jnp.arange(group_bands.shape[0], dtype=jnp.int32)[None, :], 0), axis=1
    )
    owner_dev = band_place // band_here
    source_dev = brick_of_band // bricks_here % partners
    arrived = lax.all_to_all(
        place_rows(level_bricks, owner_dev, in_band, partners),
        "dev",
        split_axis=0,
        concat_axis=0,
        tiled=True,
    )
    return jnp.take(arrived, source_dev, axis=0)


def solution(mesh):
    placed = (
        P("group", "dev", None),
        P("group", "dev", None),
        P(),
        P(("group", "dev")),
        P(("group", "dev"), None),
        P(("group", "dev")),
    )
    return jax.shard_map(
        per_device,
        mesh=mesh,
        in_specs=placed,
        out_specs=P(("group", "dev"), None, None, None),
        check_vma=False,
    )
```

```python
import math

import jax
import jax.numpy as jnp
from jax import lax
from jax.sharding import PartitionSpec as P

BX = 16
BY = 16
BZ = 128
BXN = 2
BYN = 2
BZN = 4
STEPS = 4


gauss_raw = [math.exp(-0.5 * position * position) for position in range(-2, 3)]
gauss_taps = [weight / sum(gauss_raw) for weight in gauss_raw]
time_step = 0.2
smoothing = 0.15
contrast = 0.02


def shortened(value):
    return jax.tree.map(lambda a: a.astype(jnp.bfloat16) if a.dtype == jnp.float32 else a, value)


def extended(cells, sides, width):
    for axis, dim in sides:
        count = lax.axis_size(axis)
        ends = count - 1
        head = lax.slice_in_dim(cells, 0, width, axis=dim)
        tail = lax.slice_in_dim(cells, cells.shape[dim] - width, cells.shape[dim], axis=dim)
        cells = jnp.concatenate(
            [
                lax.ppermute(tail, axis, [(i, (i + 1) % count) for i in range(ends)]),
                cells,
                lax.ppermute(head, axis, [((i + 1) % count, i) for i in range(ends)]),
            ],
            axis=dim,
        )
    return cells


def smooth_axis(values, along):
    length = values.shape[along] - 4
    summed = gauss_taps[0] * lax.slice_in_dim(values, 0, length, axis=along)
    for offset in range(1, 5):
        summed = summed + gauss_taps[offset] * lax.slice_in_dim(
            values, offset, offset + length, axis=along
        )
    return summed


def edge_map(window):
    smoothed = smooth_axis(smooth_axis(smooth_axis(window, 0), 1), 2)
    grad_x = (smoothed[2:, 1:-1, 1:-1] - smoothed[:-2, 1:-1, 1:-1]) * 0.5
    grad_y = (smoothed[1:-1, 2:, 1:-1] - smoothed[1:-1, :-2, 1:-1]) * 0.5
    grad_z = (smoothed[1:-1, 1:-1, 2:] - smoothed[1:-1, 1:-1, :-2]) * 0.5
    return 1.0 / (1.0 + (grad_x * grad_x + grad_y * grad_y + grad_z * grad_z) / contrast)


def to_bricks(block):
    shaped = block.reshape(BXN, BX, BYN, BY, BZN, BZ)
    return shaped.transpose(0, 2, 4, 1, 3, 5).reshape(BXN * BYN * BZN, BX, BY, BZ)


def own_faces(levels):
    side_faces = jnp.stack([levels[:, 0], levels[:, -1], levels[:, :, 0], levels[:, :, -1]], axis=1)
    end_faces = jnp.stack([levels[:, :, :, 0], levels[:, :, :, -1]], axis=1)
    return (side_faces, end_faces)


def advance(levels, side_ghost, end_ghost, edge_maps, speed_rows):
    with_z = jnp.concatenate(
        [end_ghost[:, 0][..., None], levels, end_ghost[:, 1][..., None]], axis=3
    )
    y_faces = jnp.pad(side_ghost[:, 2:4], ((0, 0), (0, 0), (0, 0), (1, 1)))
    with_y = jnp.concatenate(
        [y_faces[:, 0][:, :, None, :], with_z, y_faces[:, 1][:, :, None, :]], axis=2
    )
    x_faces = jnp.pad(side_ghost[:, 0:2], ((0, 0), (0, 0), (1, 1), (1, 1)))
    padded = jnp.concatenate([x_faces[:, 0][:, None], with_y, x_faces[:, 1][:, None]], axis=1)
    centre = padded[:, 1:-1, 1:-1, 1:-1]
    minus_x = padded[:, :-2, 1:-1, 1:-1]
    plus_x = padded[:, 2:, 1:-1, 1:-1]
    minus_y = padded[:, 1:-1, :-2, 1:-1]
    plus_y = padded[:, 1:-1, 2:, 1:-1]
    minus_z = padded[:, 1:-1, 1:-1, :-2]
    plus_z = padded[:, 1:-1, 1:-1, 2:]
    laplace = plus_x + minus_x + (plus_y + minus_y) + (plus_z + minus_z) - 6.0 * centre
    diff_x = (plus_x - minus_x) * 0.5
    diff_y = (plus_y - minus_y) * 0.5
    diff_z = (plus_z - minus_z) * 0.5
    gradient = diff_x * diff_x + diff_y * diff_y + diff_z * diff_z
    force = smoothing * laplace + speed_rows[:, None, None, None]
    return centre + time_step * edge_maps * force * jnp.sqrt(1.0 + gradient)


def assemble_ghosts(side_faces, end_faces, beside_lists):
    face_grid = side_faces.reshape((BXN, BYN, BZN) + side_faces.shape[1:])
    widened = extended(shortened(face_grid), (("group", 0), ("dev", 1)), 1).astype(face_grid.dtype)
    from_side = jnp.stack(
        [
            widened[:-2, 1:-1, :, 1],
            widened[2:, 1:-1, :, 0],
            widened[1:-1, :-2, :, 3],
            widened[1:-1, 2:, :, 2],
        ],
        axis=3,
    ).reshape(side_faces.shape)
    end_grid = end_faces.reshape((BXN, BYN, BZN) + end_faces.shape[1:])
    zero_faces = jnp.zeros_like(end_grid[:, :, :1, 0])
    lower_ghost = jnp.concatenate([zero_faces, end_grid[:, :, :-1, 1]], axis=2)
    upper_ghost = jnp.concatenate([end_grid[:, :, 1:, 0], zero_faces], axis=2)
    from_ends = jnp.stack([lower_ghost, upper_ghost], axis=3).reshape(end_faces.shape)
    linked = beside_lists >= 0
    side_ghost = jnp.where(linked[:, :4, None, None], from_side, side_faces)
    end_ghost = jnp.where(linked[:, 4:, None, None], from_ends, end_faces)
    return (side_ghost, end_ghost)


def place_rows(values, target, usable, partners):
    items = values.shape[0]
    matches = (target[None, :] == jnp.arange(partners)[:, None]) & usable[None, :]
    chosen = jnp.sum(jnp.where(matches, jnp.arange(items)[None, :], 0), axis=1)
    present = jnp.any(matches, axis=1)
    picked = jnp.take(values, chosen, axis=0)
    return jnp.where(
        present.reshape((partners,) + (1,) * (values.ndim - 1)), picked, jnp.zeros((), values.dtype)
    )


def extended_many(items, sides):
    cells = [value for value, width in items]
    widths = [width for value, width in items]
    for axis, dim in sides:
        count = lax.axis_size(axis)
        ends = count - 1
        heads = tuple(lax.slice_in_dim(c, 0, w, axis=dim) for c, w in zip(cells, widths))
        tails = tuple(
            lax.slice_in_dim(c, c.shape[dim] - w, c.shape[dim], axis=dim) for c, w in zip(cells, widths)
        )
        from_below = lax.ppermute(tails, axis, [(i, (i + 1) % count) for i in range(ends)])
        from_above = lax.ppermute(heads, axis, [((i + 1) % count, i) for i in range(ends)])
        cells = [
            jnp.concatenate([below, c, above], axis=dim)
            for below, c, above in zip(from_below, cells, from_above)
        ]
    return cells


def region_step(lvl, edge, rate, code):
    centre = lvl[1:-1, 1:-1]
    shifted = (
        lvl[:-2, 1:-1],
        lvl[2:, 1:-1],
        lvl[1:-1, :-2],
        lvl[1:-1, 2:],
        jnp.concatenate([centre[:, :, :1], centre[:, :, :-1]], axis=2),
        jnp.concatenate([centre[:, :, 1:], centre[:, :, -1:]], axis=2),
    )
    minus_x, plus_x, minus_y, plus_y, minus_z, plus_z = (
        jnp.where((code >> side) & 1 == 1, value, centre) for side, value in enumerate(shifted)
    )
    laplace = plus_x + minus_x + (plus_y + minus_y) + (plus_z + minus_z) - 6.0 * centre
    diff_x = (plus_x - minus_x) * 0.5
    diff_y = (plus_y - minus_y) * 0.5
    diff_z = (plus_z - minus_z) * 0.5
    gradient = diff_x * diff_x + diff_y * diff_y + diff_z * diff_z
    force = smoothing * laplace + rate
    return centre + time_step * edge * force * jnp.sqrt(1.0 + gradient)


def per_device(em_image, level_set, speeds, brick_of_band, neighbours, speed_index):
    partners = lax.axis_size("dev")
    bricks_here = BXN * BYN * BZN
    choose = speed_index[:, None] == jnp.arange(speeds.shape[0])[None, :]
    rates_here = jnp.sum(jnp.where(choose, speeds[None, :], 0.0), axis=1)
    info = jnp.concatenate(
        [(neighbours >= 0).astype(jnp.float32), rates_here[:, None]], axis=1
    ).reshape(BXN, BYN, BZN, 7)
    margin, wide_level, wide_info = extended_many(
        ((em_image, 3 + STEPS), (level_set, STEPS), (info, 1)), (("group", 0), ("dev", 1))
    )
    window = jnp.pad(margin.astype(jnp.float32), ((0, 0), (0, 0), (3, 3)))
    edge = edge_map(window)
    span_x, span_y, span_z = wide_level.shape
    lead = BX - STEPS
    weights = jnp.asarray([1 << side for side in range(6)] + [0], jnp.int32)
    brick_code = jnp.sum(jnp.where(wide_info > 0.5, weights, 0), axis=-1)
    def planes(per_brick):
        spread = jnp.broadcast_to(
            per_brick.reshape(BXN + 2, BYN + 2, 1, BZN, 1), (BXN + 2, BYN + 2, BY, BZN, BZ)
        ).reshape(BXN + 2, (BYN + 2) * BY, BZN * BZ)
        return spread[:, lead : lead + span_y]
    def across_x(per_brick):
        table = planes(per_brick)
        xe = lax.broadcasted_iota(jnp.int32, wide_level.shape, 0) + lead
        value = table[BXN + 1][None]
        for bx in range(BXN, -1, -1):
            value = jnp.where(xe < (bx + 1) * BX, table[bx][None], value)
        return value
    rate = across_x(wide_info[..., 6])
    place = (
        lax.broadcasted_iota(jnp.int32, wide_level.shape, 0) + lead,
        lax.broadcasted_iota(jnp.int32, wide_level.shape, 1) + lead,
        lax.broadcasted_iota(jnp.int32, wide_level.shape, 2),
    )
    sizes = (BX, BX, BY, BY, BZ, BZ)
    code = across_x(brick_code)
    for side in range(6):
        pos = place[side // 2] % sizes[side]
        inner = pos != (0 if side % 2 == 0 else sizes[side] - 1)
        code = code | (inner.astype(jnp.int32) << side)
    lvl = wide_level
    for repeat in range(STEPS):
        lo = repeat + 1
        hi_x = span_x - repeat - 1
        hi_y = span_y - repeat - 1
        lvl = region_step(lvl, edge[lo:hi_x, lo:hi_y], rate[lo:hi_x, lo:hi_y], code[lo:hi_x, lo:hi_y])
    level_bricks = to_bricks(lvl)
    band_here = brick_of_band.shape[0]
    group_bands = lax.all_to_all(
        jnp.broadcast_to(brick_of_band[None], (partners, band_here)),
        "dev",
        split_axis=0,
        concat_axis=0,
        tiled=True,
    ).reshape(partners * band_here)
    device_here = lax.axis_index("group") * partners + lax.axis_index("dev")
    local_ids = device_here * bricks_here + jnp.arange(bricks_here, dtype=jnp.int32)
    found = group_bands[None, :] == local_ids[:, None]
    in_band = jnp.any(found, axis=1)
    band_place = jnp.sum(
        jnp.where(found, jnp.arange(group_bands.shape[0], dtype=jnp.int32)[None, :], 0), axis=1
    )
    owner_dev = band_place // band_here
    source_dev = brick_of_band // bricks_here % partners
    arrived = lax.all_to_all(
        place_rows(level_bricks, owner_dev, in_band, partners),
        "dev",
        split_axis=0,
        concat_axis=0,
        tiled=True,
    )
    return jnp.take(arrived, source_dev, axis=0)


def solution(mesh):
    placed = (
        P("group", "dev", None),
        P("group", "dev", None),
        P(),
        P(("group", "dev")),
        P(("group", "dev"), None),
        P(("group", "dev")),
    )
    return jax.shard_map(
        per_device,
        mesh=mesh,
        in_specs=placed,
        out_specs=P(("group", "dev"), None, None, None),
        check_vma=False,
    )
```

```python
import math

import jax
import jax.numpy as jnp
from jax import lax
from jax.sharding import PartitionSpec as P

BX = 16
BY = 16
BZ = 128
BXN = 2
BYN = 2
BZN = 4
STEPS = 4


gauss_raw = [math.exp(-0.5 * position * position) for position in range(-2, 3)]
gauss_taps = [weight / sum(gauss_raw) for weight in gauss_raw]
time_step = 0.2
smoothing = 0.15
contrast = 0.02


def shortened(value):
    return jax.tree.map(lambda a: a.astype(jnp.bfloat16) if a.dtype == jnp.float32 else a, value)


def extended(cells, sides, width):
    for axis, dim in sides:
        count = lax.axis_size(axis)
        ends = count - 1
        head = lax.slice_in_dim(cells, 0, width, axis=dim)
        tail = lax.slice_in_dim(cells, cells.shape[dim] - width, cells.shape[dim], axis=dim)
        cells = jnp.concatenate(
            [
                lax.ppermute(tail, axis, [(i, (i + 1) % count) for i in range(ends)]),
                cells,
                lax.ppermute(head, axis, [((i + 1) % count, i) for i in range(ends)]),
            ],
            axis=dim,
        )
    return cells


def smooth_axis(values, along):
    length = values.shape[along] - 4
    summed = gauss_taps[0] * lax.slice_in_dim(values, 0, length, axis=along)
    for offset in range(1, 5):
        summed = summed + gauss_taps[offset] * lax.slice_in_dim(
            values, offset, offset + length, axis=along
        )
    return summed


def edge_map(window):
    smoothed = smooth_axis(smooth_axis(smooth_axis(window, 0), 1), 2)
    grad_x = (smoothed[2:, 1:-1, 1:-1] - smoothed[:-2, 1:-1, 1:-1]) * 0.5
    grad_y = (smoothed[1:-1, 2:, 1:-1] - smoothed[1:-1, :-2, 1:-1]) * 0.5
    grad_z = (smoothed[1:-1, 1:-1, 2:] - smoothed[1:-1, 1:-1, :-2]) * 0.5
    return 1.0 / (1.0 + (grad_x * grad_x + grad_y * grad_y + grad_z * grad_z) / contrast)


def to_bricks(block):
    shaped = block.reshape(BXN, BX, BYN, BY, BZN, BZ)
    return shaped.transpose(0, 2, 4, 1, 3, 5).reshape(BXN * BYN * BZN, BX, BY, BZ)


def own_faces(levels):
    side_faces = jnp.stack([levels[:, 0], levels[:, -1], levels[:, :, 0], levels[:, :, -1]], axis=1)
    end_faces = jnp.stack([levels[:, :, :, 0], levels[:, :, :, -1]], axis=1)
    return (side_faces, end_faces)


def advance(levels, side_ghost, end_ghost, edge_maps, speed_rows):
    with_z = jnp.concatenate(
        [end_ghost[:, 0][..., None], levels, end_ghost[:, 1][..., None]], axis=3
    )
    y_faces = jnp.pad(side_ghost[:, 2:4], ((0, 0), (0, 0), (0, 0), (1, 1)))
    with_y = jnp.concatenate(
        [y_faces[:, 0][:, :, None, :], with_z, y_faces[:, 1][:, :, None, :]], axis=2
    )
    x_faces = jnp.pad(side_ghost[:, 0:2], ((0, 0), (0, 0), (1, 1), (1, 1)))
    padded = jnp.concatenate([x_faces[:, 0][:, None], with_y, x_faces[:, 1][:, None]], axis=1)
    centre = padded[:, 1:-1, 1:-1, 1:-1]
    minus_x = padded[:, :-2, 1:-1, 1:-1]
    plus_x = padded[:, 2:, 1:-1, 1:-1]
    minus_y = padded[:, 1:-1, :-2, 1:-1]
    plus_y = padded[:, 1:-1, 2:, 1:-1]
    minus_z = padded[:, 1:-1, 1:-1, :-2]
    plus_z = padded[:, 1:-1, 1:-1, 2:]
    laplace = plus_x + minus_x + (plus_y + minus_y) + (plus_z + minus_z) - 6.0 * centre
    diff_x = (plus_x - minus_x) * 0.5
    diff_y = (plus_y - minus_y) * 0.5
    diff_z = (plus_z - minus_z) * 0.5
    gradient = diff_x * diff_x + diff_y * diff_y + diff_z * diff_z
    force = smoothing * laplace + speed_rows[:, None, None, None]
    return centre + time_step * edge_maps * force * jnp.sqrt(1.0 + gradient)


def assemble_ghosts(side_faces, end_faces, beside_lists):
    face_grid = side_faces.reshape((BXN, BYN, BZN) + side_faces.shape[1:])
    widened = extended(shortened(face_grid), (("group", 0), ("dev", 1)), 1).astype(face_grid.dtype)
    from_side = jnp.stack(
        [
            widened[:-2, 1:-1, :, 1],
            widened[2:, 1:-1, :, 0],
            widened[1:-1, :-2, :, 3],
            widened[1:-1, 2:, :, 2],
        ],
        axis=3,
    ).reshape(side_faces.shape)
    end_grid = end_faces.reshape((BXN, BYN, BZN) + end_faces.shape[1:])
    zero_faces = jnp.zeros_like(end_grid[:, :, :1, 0])
    lower_ghost = jnp.concatenate([zero_faces, end_grid[:, :, :-1, 1]], axis=2)
    upper_ghost = jnp.concatenate([end_grid[:, :, 1:, 0], zero_faces], axis=2)
    from_ends = jnp.stack([lower_ghost, upper_ghost], axis=3).reshape(end_faces.shape)
    linked = beside_lists >= 0
    side_ghost = jnp.where(linked[:, :4, None, None], from_side, side_faces)
    end_ghost = jnp.where(linked[:, 4:, None, None], from_ends, end_faces)
    return (side_ghost, end_ghost)


def place_rows(values, target, usable, partners):
    items = values.shape[0]
    matches = (target[None, :] == jnp.arange(partners)[:, None]) & usable[None, :]
    chosen = jnp.sum(jnp.where(matches, jnp.arange(items)[None, :], 0), axis=1)
    present = jnp.any(matches, axis=1)
    picked = jnp.take(values, chosen, axis=0)
    return jnp.where(
        present.reshape((partners,) + (1,) * (values.ndim - 1)), picked, jnp.zeros((), values.dtype)
    )


def extended_many(items, sides):
    cells = [value for value, width in items]
    widths = [width for value, width in items]
    for axis, dim in sides:
        count = lax.axis_size(axis)
        ends = count - 1
        heads = tuple(lax.slice_in_dim(c, 0, w, axis=dim) for c, w in zip(cells, widths))
        tails = tuple(
            lax.slice_in_dim(c, c.shape[dim] - w, c.shape[dim], axis=dim) for c, w in zip(cells, widths)
        )
        from_below = lax.ppermute(tails, axis, [(i, (i + 1) % count) for i in range(ends)])
        from_above = lax.ppermute(heads, axis, [((i + 1) % count, i) for i in range(ends)])
        cells = [
            jnp.concatenate([below, c, above], axis=dim)
            for below, c, above in zip(from_below, cells, from_above)
        ]
    return cells


def extended_packed(em_image, level_set, info):
    cells = [em_image, level_set, info]
    widths = [3 + STEPS, STEPS, 1]
    for axis, dim in (("group", 0), ("dev", 1)):
        count = lax.axis_size(axis)
        ends = count - 1
        parts = []
        for end in (0, 1):
            pieces = []
            for c, w in zip(cells, widths):
                start = 0 if end == 0 else c.shape[dim] - w
                pieces.append(lax.slice_in_dim(c, start, start + w, axis=dim))
            parts.append(pieces)
        def sent(pieces, pairs):
            image_part = lax.ppermute(pieces[0], axis, pairs)
            flat = jnp.concatenate([pieces[1].reshape(-1), pieces[2].reshape(-1)])
            flat = lax.ppermute(flat, axis, pairs)
            size = pieces[1].size
            return [
                image_part,
                flat[:size].reshape(pieces[1].shape),
                flat[size:].reshape(pieces[2].shape),
            ]
        from_below = sent(parts[1], [(i, i + 1) for i in range(ends)])
        from_above = sent(parts[0], [(i + 1, i) for i in range(ends)])
        cells = [
            jnp.concatenate([below, c, above], axis=dim)
            for below, c, above in zip(from_below, cells, from_above)
        ]
    return cells


def region_step(lvl, edge, rate, code):
    centre = lvl[1:-1, 1:-1]
    shifted = (
        lvl[:-2, 1:-1],
        lvl[2:, 1:-1],
        lvl[1:-1, :-2],
        lvl[1:-1, 2:],
        jnp.concatenate([centre[:, :, :1], centre[:, :, :-1]], axis=2),
        jnp.concatenate([centre[:, :, 1:], centre[:, :, -1:]], axis=2),
    )
    minus_x, plus_x, minus_y, plus_y, minus_z, plus_z = (
        jnp.where((code >> side) & 1 == 1, value, centre) for side, value in enumerate(shifted)
    )
    laplace = plus_x + minus_x + (plus_y + minus_y) + (plus_z + minus_z) - 6.0 * centre
    diff_x = (plus_x - minus_x) * 0.5
    diff_y = (plus_y - minus_y) * 0.5
    diff_z = (plus_z - minus_z) * 0.5
    gradient = diff_x * diff_x + diff_y * diff_y + diff_z * diff_z
    force = smoothing * laplace + rate
    return centre + time_step * edge * force * jnp.sqrt(1.0 + gradient)


def per_device(em_image, level_set, speeds, brick_of_band, neighbours, speed_index):
    partners = lax.axis_size("dev")
    bricks_here = BXN * BYN * BZN
    choose = speed_index[:, None] == jnp.arange(speeds.shape[0])[None, :]
    rates_here = jnp.sum(jnp.where(choose, speeds[None, :], 0.0), axis=1)
    info = jnp.concatenate(
        [(neighbours >= 0).astype(jnp.float32), rates_here[:, None]], axis=1
    ).reshape(BXN, BYN, BZN, 7)
    margin, wide_level, wide_info = extended_packed(em_image, level_set, info)
    window = jnp.pad(margin.astype(jnp.float32), ((0, 0), (0, 0), (3, 3)))
    edge = edge_map(window)
    span_x, span_y, span_z = wide_level.shape
    lead = BX - STEPS
    weights = jnp.asarray([1 << side for side in range(6)] + [0], jnp.int32)
    brick_code = jnp.sum(jnp.where(wide_info > 0.5, weights, 0), axis=-1)
    def planes(per_brick):
        spread = jnp.broadcast_to(
            per_brick.reshape(BXN + 2, BYN + 2, 1, BZN, 1), (BXN + 2, BYN + 2, BY, BZN, BZ)
        ).reshape(BXN + 2, (BYN + 2) * BY, BZN * BZ)
        return spread[:, lead : lead + span_y]
    def across_x(per_brick):
        table = planes(per_brick)
        xe = lax.broadcasted_iota(jnp.int32, wide_level.shape, 0) + lead
        value = table[BXN + 1][None]
        for bx in range(BXN, -1, -1):
            value = jnp.where(xe < (bx + 1) * BX, table[bx][None], value)
        return value
    rate = across_x(wide_info[..., 6])
    place = (
        lax.broadcasted_iota(jnp.int32, wide_level.shape, 0) + lead,
        lax.broadcasted_iota(jnp.int32, wide_level.shape, 1) + lead,
        lax.broadcasted_iota(jnp.int32, wide_level.shape, 2),
    )
    sizes = (BX, BX, BY, BY, BZ, BZ)
    code = across_x(brick_code)
    for side in range(6):
        pos = place[side // 2] % sizes[side]
        inner = pos != (0 if side % 2 == 0 else sizes[side] - 1)
        code = code | (inner.astype(jnp.int32) << side)
    lvl = wide_level
    for repeat in range(STEPS):
        lo = repeat + 1
        hi_x = span_x - repeat - 1
        hi_y = span_y - repeat - 1
        lvl = region_step(lvl, edge[lo:hi_x, lo:hi_y], rate[lo:hi_x, lo:hi_y], code[lo:hi_x, lo:hi_y])
    level_bricks = to_bricks(lvl)
    band_here = brick_of_band.shape[0]
    lower = jnp.concatenate([neighbours[1:, 4], neighbours[:1, 4]])
    upper = jnp.concatenate([neighbours[-1:, 5], neighbours[:-1, 5]])
    first_in_z = jnp.arange(bricks_here, dtype=jnp.int32) % BZN == 0
    band_of = jnp.where(first_in_z, lower, upper)
    in_band = band_of >= 0
    owner_dev = band_of // band_here % partners
    source_dev = brick_of_band // bricks_here % partners
    arrived = lax.all_to_all(
        place_rows(level_bricks, owner_dev, in_band, partners),
        "dev",
        split_axis=0,
        concat_axis=0,
        tiled=True,
    )
    return jnp.take(arrived, source_dev, axis=0)


def solution(mesh):
    placed = (
        P("group", "dev", None),
        P("group", "dev", None),
        P(),
        P(("group", "dev")),
        P(("group", "dev"), None),
        P(("group", "dev")),
    )
    return jax.shard_map(
        per_device,
        mesh=mesh,
        in_specs=placed,
        out_specs=P(("group", "dev"), None, None, None),
        check_vma=False,
    )
```

```python
import math

import jax
import jax.numpy as jnp
from jax import lax
from jax.sharding import PartitionSpec as P

BX = 16
BY = 16
BZ = 128
BXN = 2
BYN = 2
BZN = 4
STEPS = 4


gauss_raw = [math.exp(-0.5 * position * position) for position in range(-2, 3)]
gauss_taps = [weight / sum(gauss_raw) for weight in gauss_raw]
time_step = 0.2
smoothing = 0.15
contrast = 0.02


def shortened(value):
    return jax.tree.map(lambda a: a.astype(jnp.bfloat16) if a.dtype == jnp.float32 else a, value)


def extended(cells, sides, width):
    for axis, dim in sides:
        count = lax.axis_size(axis)
        ends = count - 1
        head = lax.slice_in_dim(cells, 0, width, axis=dim)
        tail = lax.slice_in_dim(cells, cells.shape[dim] - width, cells.shape[dim], axis=dim)
        cells = jnp.concatenate(
            [
                lax.ppermute(tail, axis, [(i, (i + 1) % count) for i in range(ends)]),
                cells,
                lax.ppermute(head, axis, [((i + 1) % count, i) for i in range(ends)]),
            ],
            axis=dim,
        )
    return cells


def smooth_axis(values, along):
    length = values.shape[along] - 4
    summed = gauss_taps[0] * lax.slice_in_dim(values, 0, length, axis=along)
    for offset in range(1, 5):
        summed = summed + gauss_taps[offset] * lax.slice_in_dim(
            values, offset, offset + length, axis=along
        )
    return summed


def edge_map(window):
    smoothed = smooth_axis(smooth_axis(smooth_axis(window, 0), 1), 2)
    grad_x = (smoothed[2:, 1:-1, 1:-1] - smoothed[:-2, 1:-1, 1:-1]) * 0.5
    grad_y = (smoothed[1:-1, 2:, 1:-1] - smoothed[1:-1, :-2, 1:-1]) * 0.5
    grad_z = (smoothed[1:-1, 1:-1, 2:] - smoothed[1:-1, 1:-1, :-2]) * 0.5
    return 1.0 / (1.0 + (grad_x * grad_x + grad_y * grad_y + grad_z * grad_z) / contrast)


def to_bricks(block):
    shaped = block.reshape(BXN, BX, BYN, BY, BZN, BZ)
    return shaped.transpose(0, 2, 4, 1, 3, 5).reshape(BXN * BYN * BZN, BX, BY, BZ)


def own_faces(levels):
    side_faces = jnp.stack([levels[:, 0], levels[:, -1], levels[:, :, 0], levels[:, :, -1]], axis=1)
    end_faces = jnp.stack([levels[:, :, :, 0], levels[:, :, :, -1]], axis=1)
    return (side_faces, end_faces)


def advance(levels, side_ghost, end_ghost, edge_maps, speed_rows):
    with_z = jnp.concatenate(
        [end_ghost[:, 0][..., None], levels, end_ghost[:, 1][..., None]], axis=3
    )
    y_faces = jnp.pad(side_ghost[:, 2:4], ((0, 0), (0, 0), (0, 0), (1, 1)))
    with_y = jnp.concatenate(
        [y_faces[:, 0][:, :, None, :], with_z, y_faces[:, 1][:, :, None, :]], axis=2
    )
    x_faces = jnp.pad(side_ghost[:, 0:2], ((0, 0), (0, 0), (1, 1), (1, 1)))
    padded = jnp.concatenate([x_faces[:, 0][:, None], with_y, x_faces[:, 1][:, None]], axis=1)
    centre = padded[:, 1:-1, 1:-1, 1:-1]
    minus_x = padded[:, :-2, 1:-1, 1:-1]
    plus_x = padded[:, 2:, 1:-1, 1:-1]
    minus_y = padded[:, 1:-1, :-2, 1:-1]
    plus_y = padded[:, 1:-1, 2:, 1:-1]
    minus_z = padded[:, 1:-1, 1:-1, :-2]
    plus_z = padded[:, 1:-1, 1:-1, 2:]
    laplace = plus_x + minus_x + (plus_y + minus_y) + (plus_z + minus_z) - 6.0 * centre
    diff_x = (plus_x - minus_x) * 0.5
    diff_y = (plus_y - minus_y) * 0.5
    diff_z = (plus_z - minus_z) * 0.5
    gradient = diff_x * diff_x + diff_y * diff_y + diff_z * diff_z
    force = smoothing * laplace + speed_rows[:, None, None, None]
    return centre + time_step * edge_maps * force * jnp.sqrt(1.0 + gradient)


def assemble_ghosts(side_faces, end_faces, beside_lists):
    face_grid = side_faces.reshape((BXN, BYN, BZN) + side_faces.shape[1:])
    widened = extended(shortened(face_grid), (("group", 0), ("dev", 1)), 1).astype(face_grid.dtype)
    from_side = jnp.stack(
        [
            widened[:-2, 1:-1, :, 1],
            widened[2:, 1:-1, :, 0],
            widened[1:-1, :-2, :, 3],
            widened[1:-1, 2:, :, 2],
        ],
        axis=3,
    ).reshape(side_faces.shape)
    end_grid = end_faces.reshape((BXN, BYN, BZN) + end_faces.shape[1:])
    zero_faces = jnp.zeros_like(end_grid[:, :, :1, 0])
    lower_ghost = jnp.concatenate([zero_faces, end_grid[:, :, :-1, 1]], axis=2)
    upper_ghost = jnp.concatenate([end_grid[:, :, 1:, 0], zero_faces], axis=2)
    from_ends = jnp.stack([lower_ghost, upper_ghost], axis=3).reshape(end_faces.shape)
    linked = beside_lists >= 0
    side_ghost = jnp.where(linked[:, :4, None, None], from_side, side_faces)
    end_ghost = jnp.where(linked[:, 4:, None, None], from_ends, end_faces)
    return (side_ghost, end_ghost)


def place_rows(values, target, usable, partners):
    items = values.shape[0]
    matches = (target[None, :] == jnp.arange(partners)[:, None]) & usable[None, :]
    chosen = jnp.sum(jnp.where(matches, jnp.arange(items)[None, :], 0), axis=1)
    present = jnp.any(matches, axis=1)
    picked = jnp.take(values, chosen, axis=0)
    return jnp.where(
        present.reshape((partners,) + (1,) * (values.ndim - 1)), picked, jnp.zeros((), values.dtype)
    )


def extended_many(items, sides):
    cells = [value for value, width in items]
    widths = [width for value, width in items]
    for axis, dim in sides:
        count = lax.axis_size(axis)
        ends = count - 1
        heads = tuple(lax.slice_in_dim(c, 0, w, axis=dim) for c, w in zip(cells, widths))
        tails = tuple(
            lax.slice_in_dim(c, c.shape[dim] - w, c.shape[dim], axis=dim) for c, w in zip(cells, widths)
        )
        from_below = lax.ppermute(tails, axis, [(i, (i + 1) % count) for i in range(ends)])
        from_above = lax.ppermute(heads, axis, [((i + 1) % count, i) for i in range(ends)])
        cells = [
            jnp.concatenate([below, c, above], axis=dim)
            for below, c, above in zip(from_below, cells, from_above)
        ]
    return cells


def extended_packed(em_image, level_set, info):
    cells = [em_image, level_set, info]
    widths = [3 + STEPS, STEPS, 1]
    for axis, dim in (("group", 0), ("dev", 1)):
        count = lax.axis_size(axis)
        ends = count - 1
        parts = []
        for end in (0, 1):
            pieces = []
            for c, w in zip(cells, widths):
                start = 0 if end == 0 else c.shape[dim] - w
                pieces.append(lax.slice_in_dim(c, start, start + w, axis=dim))
            parts.append(pieces)
        def sent(pieces, pairs):
            image_part = lax.ppermute(pieces[0], axis, pairs)
            flat = jnp.concatenate([pieces[1].reshape(-1), pieces[2].reshape(-1)])
            flat = lax.ppermute(flat, axis, pairs)
            size = pieces[1].size
            return [
                image_part,
                flat[:size].reshape(pieces[1].shape),
                flat[size:].reshape(pieces[2].shape),
            ]
        from_below = sent(parts[1], [(i, i + 1) for i in range(ends)])
        from_above = sent(parts[0], [(i + 1, i) for i in range(ends)])
        cells = [
            jnp.concatenate([below, c, above], axis=dim)
            for below, c, above in zip(from_below, cells, from_above)
        ]
    return cells


def region_step(lvl, edge, rate, code):
    centre = lvl[1:-1, 1:-1]
    shifted = (
        lvl[:-2, 1:-1],
        lvl[2:, 1:-1],
        lvl[1:-1, :-2],
        lvl[1:-1, 2:],
        jnp.concatenate([centre[:, :, :1], centre[:, :, :-1]], axis=2),
        jnp.concatenate([centre[:, :, 1:], centre[:, :, -1:]], axis=2),
    )
    minus_x, plus_x, minus_y, plus_y, minus_z, plus_z = (
        jnp.where((code >> side) & 1 == 1, value, centre) for side, value in enumerate(shifted)
    )
    laplace = plus_x + minus_x + (plus_y + minus_y) + (plus_z + minus_z) - 6.0 * centre
    diff_x = (plus_x - minus_x) * 0.5
    diff_y = (plus_y - minus_y) * 0.5
    diff_z = (plus_z - minus_z) * 0.5
    gradient = diff_x * diff_x + diff_y * diff_y + diff_z * diff_z
    force = smoothing * laplace + rate
    return centre + time_step * edge * force * jnp.sqrt(1.0 + gradient)


def per_device(em_image, level_set, speeds, brick_of_band, neighbours, speed_index):
    partners = lax.axis_size("dev")
    bricks_here = BXN * BYN * BZN
    choose = speed_index[:, None] == jnp.arange(speeds.shape[0])[None, :]
    rates_here = jnp.sum(jnp.where(choose, speeds[None, :], 0.0), axis=1)
    info = jnp.concatenate(
        [(neighbours >= 0).astype(jnp.float32), rates_here[:, None]], axis=1
    ).reshape(BXN, BYN, BZN, 7)
    margin, wide_level, wide_info = extended_packed(em_image, level_set, info)
    window = jnp.pad(margin.astype(jnp.float32), ((0, 0), (0, 0), (3, 3)))
    edge = edge_map(window)
    span_x, span_y, span_z = wide_level.shape
    lead = BX - STEPS
    weights = jnp.asarray([1 << side for side in range(6)] + [0], jnp.int32)
    brick_code = jnp.sum(jnp.where(wide_info > 0.5, weights, 0), axis=-1)
    def planes(per_brick):
        spread = jnp.broadcast_to(
            per_brick.reshape(BXN + 2, BYN + 2, 1, BZN, 1), (BXN + 2, BYN + 2, BY, BZN, BZ)
        ).reshape(BXN + 2, (BYN + 2) * BY, BZN * BZ)
        return spread[:, lead : lead + span_y]
    def across_x(per_brick):
        table = planes(per_brick)
        xe = lax.broadcasted_iota(jnp.int32, wide_level.shape, 0) + lead
        value = table[BXN + 1][None]
        for bx in range(BXN, -1, -1):
            value = jnp.where(xe < (bx + 1) * BX, table[bx][None], value)
        return value
    rate = across_x(wide_info[..., 6])
    place = (
        lax.broadcasted_iota(jnp.int32, wide_level.shape, 0) + lead,
        lax.broadcasted_iota(jnp.int32, wide_level.shape, 1) + lead,
        lax.broadcasted_iota(jnp.int32, wide_level.shape, 2),
    )
    sizes = (BX, BX, BY, BY, BZ, BZ)
    code = across_x(brick_code)
    for side in range(6):
        pos = place[side // 2] % sizes[side]
        inner = pos != (0 if side % 2 == 0 else sizes[side] - 1)
        code = code | (inner.astype(jnp.int32) << side)
    lvl = wide_level
    for repeat in range(STEPS):
        lo = repeat + 1
        hi_x = span_x - repeat - 1
        hi_y = span_y - repeat - 1
        lvl = region_step(lvl, edge[lo:hi_x, lo:hi_y], rate[lo:hi_x, lo:hi_y], code[lo:hi_x, lo:hi_y])
    band_here = brick_of_band.shape[0]
    lower = jnp.concatenate([neighbours[1:, 4], neighbours[:1, 4]])
    upper = jnp.concatenate([neighbours[-1:, 5], neighbours[:-1, 5]])
    first_in_z = jnp.arange(bricks_here, dtype=jnp.int32) % BZN == 0
    band_of = jnp.where(first_in_z, lower, upper)
    in_band = band_of >= 0
    owner_dev = band_of // band_here % partners
    source_dev = brick_of_band // bricks_here % partners
    matches = (owner_dev[None, :] == jnp.arange(partners)[:, None]) & in_band[None, :]
    chosen = jnp.sum(jnp.where(matches, jnp.arange(bricks_here)[None, :], 0), axis=1)
    view = lvl.reshape(BXN, BX, BYN, BY, BZN, BZ)
    sending = view[chosen // (BYN * BZN), :, chosen // BZN % BYN, :, chosen % BZN, :]
    arrived = lax.all_to_all(sending, "dev", split_axis=0, concat_axis=0, tiled=True)
    return jnp.take(arrived, source_dev, axis=0)


def solution(mesh):
    placed = (
        P("group", "dev", None),
        P("group", "dev", None),
        P(),
        P(("group", "dev")),
        P(("group", "dev"), None),
        P(("group", "dev")),
    )
    return jax.shard_map(
        per_device,
        mesh=mesh,
        in_specs=placed,
        out_specs=P(("group", "dev"), None, None, None),
        check_vma=False,
    )
```

```python
import math

import jax
import jax.numpy as jnp
from jax import lax
from jax.sharding import PartitionSpec as P

BX = 16
BY = 16
BZ = 128
BXN = 2
BYN = 2
BZN = 4
STEPS = 4


gauss_raw = [math.exp(-0.5 * position * position) for position in range(-2, 3)]
gauss_taps = [weight / sum(gauss_raw) for weight in gauss_raw]
time_step = 0.2
smoothing = 0.15
contrast = 0.02


def shortened(value):
    return jax.tree.map(lambda a: a.astype(jnp.bfloat16) if a.dtype == jnp.float32 else a, value)


def extended(cells, sides, width):
    for axis, dim in sides:
        count = lax.axis_size(axis)
        ends = count - 1
        head = lax.slice_in_dim(cells, 0, width, axis=dim)
        tail = lax.slice_in_dim(cells, cells.shape[dim] - width, cells.shape[dim], axis=dim)
        cells = jnp.concatenate(
            [
                lax.ppermute(tail, axis, [(i, (i + 1) % count) for i in range(ends)]),
                cells,
                lax.ppermute(head, axis, [((i + 1) % count, i) for i in range(ends)]),
            ],
            axis=dim,
        )
    return cells


def smooth_axis(values, along):
    length = values.shape[along] - 4
    summed = gauss_taps[0] * lax.slice_in_dim(values, 0, length, axis=along)
    for offset in range(1, 5):
        summed = summed + gauss_taps[offset] * lax.slice_in_dim(
            values, offset, offset + length, axis=along
        )
    return summed


def edge_map(window):
    smoothed = smooth_axis(smooth_axis(smooth_axis(window, 0), 1), 2)
    grad_x = (smoothed[2:, 1:-1, 1:-1] - smoothed[:-2, 1:-1, 1:-1]) * 0.5
    grad_y = (smoothed[1:-1, 2:, 1:-1] - smoothed[1:-1, :-2, 1:-1]) * 0.5
    grad_z = (smoothed[1:-1, 1:-1, 2:] - smoothed[1:-1, 1:-1, :-2]) * 0.5
    return 1.0 / (1.0 + (grad_x * grad_x + grad_y * grad_y + grad_z * grad_z) / contrast)


def to_bricks(block):
    shaped = block.reshape(BXN, BX, BYN, BY, BZN, BZ)
    return shaped.transpose(0, 2, 4, 1, 3, 5).reshape(BXN * BYN * BZN, BX, BY, BZ)


def own_faces(levels):
    side_faces = jnp.stack([levels[:, 0], levels[:, -1], levels[:, :, 0], levels[:, :, -1]], axis=1)
    end_faces = jnp.stack([levels[:, :, :, 0], levels[:, :, :, -1]], axis=1)
    return (side_faces, end_faces)


def advance(levels, side_ghost, end_ghost, edge_maps, speed_rows):
    with_z = jnp.concatenate(
        [end_ghost[:, 0][..., None], levels, end_ghost[:, 1][..., None]], axis=3
    )
    y_faces = jnp.pad(side_ghost[:, 2:4], ((0, 0), (0, 0), (0, 0), (1, 1)))
    with_y = jnp.concatenate(
        [y_faces[:, 0][:, :, None, :], with_z, y_faces[:, 1][:, :, None, :]], axis=2
    )
    x_faces = jnp.pad(side_ghost[:, 0:2], ((0, 0), (0, 0), (1, 1), (1, 1)))
    padded = jnp.concatenate([x_faces[:, 0][:, None], with_y, x_faces[:, 1][:, None]], axis=1)
    centre = padded[:, 1:-1, 1:-1, 1:-1]
    minus_x = padded[:, :-2, 1:-1, 1:-1]
    plus_x = padded[:, 2:, 1:-1, 1:-1]
    minus_y = padded[:, 1:-1, :-2, 1:-1]
    plus_y = padded[:, 1:-1, 2:, 1:-1]
    minus_z = padded[:, 1:-1, 1:-1, :-2]
    plus_z = padded[:, 1:-1, 1:-1, 2:]
    laplace = plus_x + minus_x + (plus_y + minus_y) + (plus_z + minus_z) - 6.0 * centre
    diff_x = (plus_x - minus_x) * 0.5
    diff_y = (plus_y - minus_y) * 0.5
    diff_z = (plus_z - minus_z) * 0.5
    gradient = diff_x * diff_x + diff_y * diff_y + diff_z * diff_z
    force = smoothing * laplace + speed_rows[:, None, None, None]
    return centre + time_step * edge_maps * force * jnp.sqrt(1.0 + gradient)


def assemble_ghosts(side_faces, end_faces, beside_lists):
    face_grid = side_faces.reshape((BXN, BYN, BZN) + side_faces.shape[1:])
    widened = extended(shortened(face_grid), (("group", 0), ("dev", 1)), 1).astype(face_grid.dtype)
    from_side = jnp.stack(
        [
            widened[:-2, 1:-1, :, 1],
            widened[2:, 1:-1, :, 0],
            widened[1:-1, :-2, :, 3],
            widened[1:-1, 2:, :, 2],
        ],
        axis=3,
    ).reshape(side_faces.shape)
    end_grid = end_faces.reshape((BXN, BYN, BZN) + end_faces.shape[1:])
    zero_faces = jnp.zeros_like(end_grid[:, :, :1, 0])
    lower_ghost = jnp.concatenate([zero_faces, end_grid[:, :, :-1, 1]], axis=2)
    upper_ghost = jnp.concatenate([end_grid[:, :, 1:, 0], zero_faces], axis=2)
    from_ends = jnp.stack([lower_ghost, upper_ghost], axis=3).reshape(end_faces.shape)
    linked = beside_lists >= 0
    side_ghost = jnp.where(linked[:, :4, None, None], from_side, side_faces)
    end_ghost = jnp.where(linked[:, 4:, None, None], from_ends, end_faces)
    return (side_ghost, end_ghost)


def place_rows(values, target, usable, partners):
    items = values.shape[0]
    matches = (target[None, :] == jnp.arange(partners)[:, None]) & usable[None, :]
    chosen = jnp.sum(jnp.where(matches, jnp.arange(items)[None, :], 0), axis=1)
    present = jnp.any(matches, axis=1)
    picked = jnp.take(values, chosen, axis=0)
    return jnp.where(
        present.reshape((partners,) + (1,) * (values.ndim - 1)), picked, jnp.zeros((), values.dtype)
    )


def extended_many(items, sides):
    cells = [value for value, width in items]
    widths = [width for value, width in items]
    for axis, dim in sides:
        count = lax.axis_size(axis)
        ends = count - 1
        heads = tuple(lax.slice_in_dim(c, 0, w, axis=dim) for c, w in zip(cells, widths))
        tails = tuple(
            lax.slice_in_dim(c, c.shape[dim] - w, c.shape[dim], axis=dim) for c, w in zip(cells, widths)
        )
        from_below = lax.ppermute(tails, axis, [(i, (i + 1) % count) for i in range(ends)])
        from_above = lax.ppermute(heads, axis, [((i + 1) % count, i) for i in range(ends)])
        cells = [
            jnp.concatenate([below, c, above], axis=dim)
            for below, c, above in zip(from_below, cells, from_above)
        ]
    return cells


def extended_packed(em_image, level_set, info):
    cells = [em_image, level_set, info]
    widths = [3 + STEPS, STEPS, 1]
    for axis, dim in (("group", 0), ("dev", 1)):
        count = lax.axis_size(axis)
        ends = count - 1
        parts = []
        for end in (0, 1):
            pieces = []
            for c, w in zip(cells, widths):
                start = 0 if end == 0 else c.shape[dim] - w
                pieces.append(lax.slice_in_dim(c, start, start + w, axis=dim))
            parts.append(pieces)
        def sent(pieces, pairs):
            image_part = lax.ppermute(pieces[0], axis, pairs)
            flat = jnp.concatenate([pieces[1].reshape(-1), pieces[2].reshape(-1)])
            flat = lax.ppermute(flat, axis, pairs)
            size = pieces[1].size
            return [
                image_part,
                flat[:size].reshape(pieces[1].shape),
                flat[size:].reshape(pieces[2].shape),
            ]
        from_below = sent(parts[1], [(i, i + 1) for i in range(ends)])
        from_above = sent(parts[0], [(i + 1, i) for i in range(ends)])
        cells = [
            jnp.concatenate([below, c, above], axis=dim)
            for below, c, above in zip(from_below, cells, from_above)
        ]
    return cells


def region_step(lvl, edge, rate, code):
    centre = lvl[1:-1, 1:-1]
    shifted = (
        lvl[:-2, 1:-1],
        lvl[2:, 1:-1],
        lvl[1:-1, :-2],
        lvl[1:-1, 2:],
        jnp.concatenate([centre[:, :, :1], centre[:, :, :-1]], axis=2),
        jnp.concatenate([centre[:, :, 1:], centre[:, :, -1:]], axis=2),
    )
    minus_x, plus_x, minus_y, plus_y, minus_z, plus_z = (
        jnp.where((code >> side) & 1 == 1, value, centre) for side, value in enumerate(shifted)
    )
    laplace = plus_x + minus_x + (plus_y + minus_y) + (plus_z + minus_z) - 6.0 * centre
    diff_x = (plus_x - minus_x) * 0.5
    diff_y = (plus_y - minus_y) * 0.5
    diff_z = (plus_z - minus_z) * 0.5
    gradient = diff_x * diff_x + diff_y * diff_y + diff_z * diff_z
    force = smoothing * laplace + rate
    return centre + time_step * edge * force * jnp.sqrt(1.0 + gradient)


def per_device(em_image, level_set, speeds, brick_of_band, neighbours, speed_index):
    partners = lax.axis_size("dev")
    bricks_here = BXN * BYN * BZN
    choose = speed_index[:, None] == jnp.arange(speeds.shape[0])[None, :]
    rates_here = jnp.sum(jnp.where(choose, speeds[None, :], 0.0), axis=1)
    info = jnp.concatenate(
        [(neighbours >= 0).astype(jnp.float32), rates_here[:, None]], axis=1
    ).reshape(BXN, BYN, BZN, 7)
    margin, wide_level, wide_info = extended_packed(em_image, level_set, info)
    window = jnp.pad(margin.astype(jnp.float32), ((0, 0), (0, 0), (3, 3)))
    edge = edge_map(window)
    span_x, span_y, span_z = wide_level.shape
    lead = BX - STEPS
    weights = jnp.asarray([1 << side for side in range(6)] + [0], jnp.int32)
    brick_code = jnp.sum(jnp.where(wide_info > 0.5, weights, 0), axis=-1)
    def planes(per_brick):
        spread = jnp.broadcast_to(
            per_brick.reshape(BXN + 2, BYN + 2, 1, BZN, 1), (BXN + 2, BYN + 2, BY, BZN, BZ)
        ).reshape(BXN + 2, (BYN + 2) * BY, BZN * BZ)
        return spread[:, lead : lead + span_y]
    def across_x(per_brick):
        table = planes(per_brick)
        xe = lax.broadcasted_iota(jnp.int32, wide_level.shape, 0) + lead
        value = table[BXN + 1][None]
        for bx in range(BXN, -1, -1):
            value = jnp.where(xe < (bx + 1) * BX, table[bx][None], value)
        return value
    rate = across_x(wide_info[..., 6])
    place = (
        lax.broadcasted_iota(jnp.int32, wide_level.shape, 0) + lead,
        lax.broadcasted_iota(jnp.int32, wide_level.shape, 1) + lead,
        lax.broadcasted_iota(jnp.int32, wide_level.shape, 2),
    )
    sizes = (BX, BX, BY, BY, BZ, BZ)
    code = across_x(brick_code)
    for side in range(6):
        pos = place[side // 2] % sizes[side]
        inner = pos != (0 if side % 2 == 0 else sizes[side] - 1)
        code = code | (inner.astype(jnp.int32) << side)
    lvl = wide_level
    for repeat in range(STEPS):
        lo = repeat + 1
        hi_x = span_x - repeat - 1
        hi_y = span_y - repeat - 1
        lvl = region_step(lvl, edge[lo:hi_x, lo:hi_y], rate[lo:hi_x, lo:hi_y], code[lo:hi_x, lo:hi_y])
    band_here = brick_of_band.shape[0]
    lower = jnp.concatenate([neighbours[1:, 4], neighbours[:1, 4]])
    upper = jnp.concatenate([neighbours[-1:, 5], neighbours[:-1, 5]])
    first_in_z = jnp.arange(bricks_here, dtype=jnp.int32) % BZN == 0
    band_of = jnp.where(first_in_z, lower, upper)
    in_band = band_of >= 0
    owner_dev = band_of // band_here % partners
    source_dev = brick_of_band // bricks_here % partners
    matches = (owner_dev[None, :] == jnp.arange(partners)[:, None]) & in_band[None, :]
    chosen = jnp.sum(jnp.where(matches, jnp.arange(bricks_here)[None, :], 0), axis=1)
    view = lvl.reshape(BXN, BX, BYN, BY, BZN, BZ)
    sending = view[chosen // (BYN * BZN), :, chosen // BZN % BYN, :, chosen % BZN, :]
    halves = [
        lax.all_to_all(part, "dev", split_axis=0, concat_axis=0, tiled=True)
        for part in (sending[:, : BX // 2], sending[:, BX // 2 :])
    ]
    arrived = jnp.concatenate(halves, axis=1)
    return jnp.take(arrived, source_dev, axis=0)


def solution(mesh):
    placed = (
        P("group", "dev", None),
        P("group", "dev", None),
        P(),
        P(("group", "dev")),
        P(("group", "dev"), None),
        P(("group", "dev")),
    )
    return jax.shard_map(
        per_device,
        mesh=mesh,
        in_specs=placed,
        out_specs=P(("group", "dev"), None, None, None),
        check_vma=False,
    )
```

```python
import math

import jax
import jax.numpy as jnp
from jax import lax
from jax.sharding import PartitionSpec as P

BX = 16
BY = 16
BZ = 128
BXN = 2
BYN = 2
BZN = 4
STEPS = 4


gauss_raw = [math.exp(-0.5 * position * position) for position in range(-2, 3)]
gauss_taps = [weight / sum(gauss_raw) for weight in gauss_raw]
time_step = 0.2
smoothing = 0.15
contrast = 0.02


def shortened(value):
    return jax.tree.map(lambda a: a.astype(jnp.bfloat16) if a.dtype == jnp.float32 else a, value)


def extended(cells, sides, width):
    for axis, dim in sides:
        count = lax.axis_size(axis)
        ends = count - 1
        head = lax.slice_in_dim(cells, 0, width, axis=dim)
        tail = lax.slice_in_dim(cells, cells.shape[dim] - width, cells.shape[dim], axis=dim)
        cells = jnp.concatenate(
            [
                lax.ppermute(tail, axis, [(i, (i + 1) % count) for i in range(ends)]),
                cells,
                lax.ppermute(head, axis, [((i + 1) % count, i) for i in range(ends)]),
            ],
            axis=dim,
        )
    return cells


def smooth_axis(values, along):
    length = values.shape[along] - 4
    summed = gauss_taps[0] * lax.slice_in_dim(values, 0, length, axis=along)
    for offset in range(1, 5):
        summed = summed + gauss_taps[offset] * lax.slice_in_dim(
            values, offset, offset + length, axis=along
        )
    return summed


def edge_map(window):
    smoothed = smooth_axis(smooth_axis(smooth_axis(window, 0), 1), 2)
    grad_x = (smoothed[2:, 1:-1, 1:-1] - smoothed[:-2, 1:-1, 1:-1]) * 0.5
    grad_y = (smoothed[1:-1, 2:, 1:-1] - smoothed[1:-1, :-2, 1:-1]) * 0.5
    grad_z = (smoothed[1:-1, 1:-1, 2:] - smoothed[1:-1, 1:-1, :-2]) * 0.5
    return 1.0 / (1.0 + (grad_x * grad_x + grad_y * grad_y + grad_z * grad_z) / contrast)


def to_bricks(block):
    shaped = block.reshape(BXN, BX, BYN, BY, BZN, BZ)
    return shaped.transpose(0, 2, 4, 1, 3, 5).reshape(BXN * BYN * BZN, BX, BY, BZ)


def own_faces(levels):
    side_faces = jnp.stack([levels[:, 0], levels[:, -1], levels[:, :, 0], levels[:, :, -1]], axis=1)
    end_faces = jnp.stack([levels[:, :, :, 0], levels[:, :, :, -1]], axis=1)
    return (side_faces, end_faces)


def advance(levels, side_ghost, end_ghost, edge_maps, speed_rows):
    with_z = jnp.concatenate(
        [end_ghost[:, 0][..., None], levels, end_ghost[:, 1][..., None]], axis=3
    )
    y_faces = jnp.pad(side_ghost[:, 2:4], ((0, 0), (0, 0), (0, 0), (1, 1)))
    with_y = jnp.concatenate(
        [y_faces[:, 0][:, :, None, :], with_z, y_faces[:, 1][:, :, None, :]], axis=2
    )
    x_faces = jnp.pad(side_ghost[:, 0:2], ((0, 0), (0, 0), (1, 1), (1, 1)))
    padded = jnp.concatenate([x_faces[:, 0][:, None], with_y, x_faces[:, 1][:, None]], axis=1)
    centre = padded[:, 1:-1, 1:-1, 1:-1]
    minus_x = padded[:, :-2, 1:-1, 1:-1]
    plus_x = padded[:, 2:, 1:-1, 1:-1]
    minus_y = padded[:, 1:-1, :-2, 1:-1]
    plus_y = padded[:, 1:-1, 2:, 1:-1]
    minus_z = padded[:, 1:-1, 1:-1, :-2]
    plus_z = padded[:, 1:-1, 1:-1, 2:]
    laplace = plus_x + minus_x + (plus_y + minus_y) + (plus_z + minus_z) - 6.0 * centre
    diff_x = (plus_x - minus_x) * 0.5
    diff_y = (plus_y - minus_y) * 0.5
    diff_z = (plus_z - minus_z) * 0.5
    gradient = diff_x * diff_x + diff_y * diff_y + diff_z * diff_z
    force = smoothing * laplace + speed_rows[:, None, None, None]
    return centre + time_step * edge_maps * force * jnp.sqrt(1.0 + gradient)


def assemble_ghosts(side_faces, end_faces, beside_lists):
    face_grid = side_faces.reshape((BXN, BYN, BZN) + side_faces.shape[1:])
    widened = extended(shortened(face_grid), (("group", 0), ("dev", 1)), 1).astype(face_grid.dtype)
    from_side = jnp.stack(
        [
            widened[:-2, 1:-1, :, 1],
            widened[2:, 1:-1, :, 0],
            widened[1:-1, :-2, :, 3],
            widened[1:-1, 2:, :, 2],
        ],
        axis=3,
    ).reshape(side_faces.shape)
    end_grid = end_faces.reshape((BXN, BYN, BZN) + end_faces.shape[1:])
    zero_faces = jnp.zeros_like(end_grid[:, :, :1, 0])
    lower_ghost = jnp.concatenate([zero_faces, end_grid[:, :, :-1, 1]], axis=2)
    upper_ghost = jnp.concatenate([end_grid[:, :, 1:, 0], zero_faces], axis=2)
    from_ends = jnp.stack([lower_ghost, upper_ghost], axis=3).reshape(end_faces.shape)
    linked = beside_lists >= 0
    side_ghost = jnp.where(linked[:, :4, None, None], from_side, side_faces)
    end_ghost = jnp.where(linked[:, 4:, None, None], from_ends, end_faces)
    return (side_ghost, end_ghost)


def place_rows(values, target, usable, partners):
    items = values.shape[0]
    matches = (target[None, :] == jnp.arange(partners)[:, None]) & usable[None, :]
    chosen = jnp.sum(jnp.where(matches, jnp.arange(items)[None, :], 0), axis=1)
    present = jnp.any(matches, axis=1)
    picked = jnp.take(values, chosen, axis=0)
    return jnp.where(
        present.reshape((partners,) + (1,) * (values.ndim - 1)), picked, jnp.zeros((), values.dtype)
    )


def extended_many(items, sides):
    cells = [value for value, width in items]
    widths = [width for value, width in items]
    for axis, dim in sides:
        count = lax.axis_size(axis)
        ends = count - 1
        heads = tuple(lax.slice_in_dim(c, 0, w, axis=dim) for c, w in zip(cells, widths))
        tails = tuple(
            lax.slice_in_dim(c, c.shape[dim] - w, c.shape[dim], axis=dim) for c, w in zip(cells, widths)
        )
        from_below = lax.ppermute(tails, axis, [(i, (i + 1) % count) for i in range(ends)])
        from_above = lax.ppermute(heads, axis, [((i + 1) % count, i) for i in range(ends)])
        cells = [
            jnp.concatenate([below, c, above], axis=dim)
            for below, c, above in zip(from_below, cells, from_above)
        ]
    return cells


def extended_packed(em_image, level_set, info):
    cells = [em_image, level_set, info]
    widths = [2 + STEPS, STEPS, 1]
    for axis, dim in (("group", 0), ("dev", 1)):
        count = lax.axis_size(axis)
        ends = count - 1
        parts = []
        for end in (0, 1):
            pieces = []
            for c, w in zip(cells, widths):
                start = 0 if end == 0 else c.shape[dim] - w
                pieces.append(lax.slice_in_dim(c, start, start + w, axis=dim))
            parts.append(pieces)
        def sent(pieces, pairs):
            image_part = lax.ppermute(pieces[0], axis, pairs)
            flat = jnp.concatenate([pieces[1].reshape(-1), pieces[2].reshape(-1)])
            flat = lax.ppermute(flat, axis, pairs)
            size = pieces[1].size
            return [
                image_part,
                flat[:size].reshape(pieces[1].shape),
                flat[size:].reshape(pieces[2].shape),
            ]
        from_below = sent(parts[1], [(i, i + 1) for i in range(ends)])
        from_above = sent(parts[0], [(i + 1, i) for i in range(ends)])
        cells = [
            jnp.concatenate([below, c, above], axis=dim)
            for below, c, above in zip(from_below, cells, from_above)
        ]
    return cells


def region_step(lvl, edge, rate, code):
    centre = lvl[1:-1, 1:-1]
    shifted = (
        lvl[:-2, 1:-1],
        lvl[2:, 1:-1],
        lvl[1:-1, :-2],
        lvl[1:-1, 2:],
        jnp.concatenate([centre[:, :, :1], centre[:, :, :-1]], axis=2),
        jnp.concatenate([centre[:, :, 1:], centre[:, :, -1:]], axis=2),
    )
    minus_x, plus_x, minus_y, plus_y, minus_z, plus_z = (
        jnp.where((code >> side) & 1 == 1, value, centre) for side, value in enumerate(shifted)
    )
    laplace = plus_x + minus_x + (plus_y + minus_y) + (plus_z + minus_z) - 6.0 * centre
    diff_x = (plus_x - minus_x) * 0.5
    diff_y = (plus_y - minus_y) * 0.5
    diff_z = (plus_z - minus_z) * 0.5
    gradient = diff_x * diff_x + diff_y * diff_y + diff_z * diff_z
    force = smoothing * laplace + rate
    return centre + time_step * edge * force * jnp.sqrt(1.0 + gradient)


def per_device(em_image, level_set, speeds, brick_of_band, neighbours, speed_index):
    partners = lax.axis_size("dev")
    bricks_here = BXN * BYN * BZN
    choose = speed_index[:, None] == jnp.arange(speeds.shape[0])[None, :]
    rates_here = jnp.sum(jnp.where(choose, speeds[None, :], 0.0), axis=1)
    info = jnp.concatenate(
        [(neighbours >= 0).astype(jnp.float32), rates_here[:, None]], axis=1
    ).reshape(BXN, BYN, BZN, 7)
    margin, wide_level, wide_info = extended_packed(em_image, level_set, info)
    window = jnp.pad(margin.astype(jnp.float32), ((0, 0), (0, 0), (3, 3)))
    edge = edge_map(window)
    span_x, span_y, span_z = wide_level.shape
    lead = BX - STEPS + 1
    inner_shape = (span_x - 2, span_y - 2, span_z)
    weights = jnp.asarray([1 << side for side in range(6)] + [0], jnp.int32)
    brick_code = jnp.sum(jnp.where(wide_info > 0.5, weights, 0), axis=-1)
    def planes(per_brick):
        spread = jnp.broadcast_to(
            per_brick.reshape(BXN + 2, BYN + 2, 1, BZN, 1), (BXN + 2, BYN + 2, BY, BZN, BZ)
        ).reshape(BXN + 2, (BYN + 2) * BY, BZN * BZ)
        return spread[:, lead : lead + span_y - 2]
    def across_x(per_brick):
        table = planes(per_brick)
        xe = lax.broadcasted_iota(jnp.int32, inner_shape, 0) + lead
        value = table[BXN + 1][None]
        for bx in range(BXN, -1, -1):
            value = jnp.where(xe < (bx + 1) * BX, table[bx][None], value)
        return value
    rate = across_x(wide_info[..., 6])
    place = (
        lax.broadcasted_iota(jnp.int32, inner_shape, 0) + lead,
        lax.broadcasted_iota(jnp.int32, inner_shape, 1) + lead,
        lax.broadcasted_iota(jnp.int32, inner_shape, 2),
    )
    sizes = (BX, BX, BY, BY, BZ, BZ)
    code = across_x(brick_code)
    for side in range(6):
        pos = place[side // 2] % sizes[side]
        inner = pos != (0 if side % 2 == 0 else sizes[side] - 1)
        code = code | (inner.astype(jnp.int32) << side)
    lvl = wide_level
    for repeat in range(STEPS):
        lo = repeat + 1
        hi_x = span_x - repeat - 1
        hi_y = span_y - repeat - 1
        cut = (slice(lo - 1, hi_x - 1), slice(lo - 1, hi_y - 1))
        lvl = region_step(lvl, edge[cut], rate[cut], code[cut])
    band_here = brick_of_band.shape[0]
    lower = jnp.concatenate([neighbours[1:, 4], neighbours[:1, 4]])
    upper = jnp.concatenate([neighbours[-1:, 5], neighbours[:-1, 5]])
    first_in_z = jnp.arange(bricks_here, dtype=jnp.int32) % BZN == 0
    band_of = jnp.where(first_in_z, lower, upper)
    in_band = band_of >= 0
    owner_dev = band_of // band_here % partners
    source_dev = brick_of_band // bricks_here % partners
    matches = (owner_dev[None, :] == jnp.arange(partners)[:, None]) & in_band[None, :]
    chosen = jnp.sum(jnp.where(matches, jnp.arange(bricks_here)[None, :], 0), axis=1)
    view = lvl.reshape(BXN, BX, BYN, BY, BZN, BZ)
    sending = view[chosen // (BYN * BZN), :, chosen // BZN % BYN, :, chosen % BZN, :]
    arrived = lax.all_to_all(sending, "dev", split_axis=0, concat_axis=0, tiled=True)
    return jnp.take(arrived, source_dev, axis=0)


def solution(mesh):
    placed = (
        P("group", "dev", None),
        P("group", "dev", None),
        P(),
        P(("group", "dev")),
        P(("group", "dev"), None),
        P(("group", "dev")),
    )
    return jax.shard_map(
        per_device,
        mesh=mesh,
        in_specs=placed,
        out_specs=P(("group", "dev"), None, None, None),
        check_vma=False,
    )
```

```python
import math

import jax
import jax.numpy as jnp
from jax import lax
from jax.sharding import PartitionSpec as P

BX = 16
BY = 16
BZ = 128
BXN = 2
BYN = 2
BZN = 4
STEPS = 4


gauss_raw = [math.exp(-0.5 * position * position) for position in range(-2, 3)]
gauss_taps = [weight / sum(gauss_raw) for weight in gauss_raw]
time_step = 0.2
smoothing = 0.15
contrast = 0.02


def shortened(value):
    return jax.tree.map(lambda a: a.astype(jnp.bfloat16) if a.dtype == jnp.float32 else a, value)


def extended(cells, sides, width):
    for axis, dim in sides:
        count = lax.axis_size(axis)
        ends = count - 1
        head = lax.slice_in_dim(cells, 0, width, axis=dim)
        tail = lax.slice_in_dim(cells, cells.shape[dim] - width, cells.shape[dim], axis=dim)
        cells = jnp.concatenate(
            [
                lax.ppermute(tail, axis, [(i, (i + 1) % count) for i in range(ends)]),
                cells,
                lax.ppermute(head, axis, [((i + 1) % count, i) for i in range(ends)]),
            ],
            axis=dim,
        )
    return cells


def smooth_axis(values, along):
    length = values.shape[along] - 4
    summed = gauss_taps[0] * lax.slice_in_dim(values, 0, length, axis=along)
    for offset in range(1, 5):
        summed = summed + gauss_taps[offset] * lax.slice_in_dim(
            values, offset, offset + length, axis=along
        )
    return summed


def edge_map(window):
    smoothed = smooth_axis(smooth_axis(smooth_axis(window, 0), 1), 2)
    grad_x = (smoothed[2:, 1:-1, 1:-1] - smoothed[:-2, 1:-1, 1:-1]) * 0.5
    grad_y = (smoothed[1:-1, 2:, 1:-1] - smoothed[1:-1, :-2, 1:-1]) * 0.5
    grad_z = (smoothed[1:-1, 1:-1, 2:] - smoothed[1:-1, 1:-1, :-2]) * 0.5
    return 1.0 / (1.0 + (grad_x * grad_x + grad_y * grad_y + grad_z * grad_z) / contrast)


def to_bricks(block):
    shaped = block.reshape(BXN, BX, BYN, BY, BZN, BZ)
    return shaped.transpose(0, 2, 4, 1, 3, 5).reshape(BXN * BYN * BZN, BX, BY, BZ)


def own_faces(levels):
    side_faces = jnp.stack([levels[:, 0], levels[:, -1], levels[:, :, 0], levels[:, :, -1]], axis=1)
    end_faces = jnp.stack([levels[:, :, :, 0], levels[:, :, :, -1]], axis=1)
    return (side_faces, end_faces)


def advance(levels, side_ghost, end_ghost, edge_maps, speed_rows):
    with_z = jnp.concatenate(
        [end_ghost[:, 0][..., None], levels, end_ghost[:, 1][..., None]], axis=3
    )
    y_faces = jnp.pad(side_ghost[:, 2:4], ((0, 0), (0, 0), (0, 0), (1, 1)))
    with_y = jnp.concatenate(
        [y_faces[:, 0][:, :, None, :], with_z, y_faces[:, 1][:, :, None, :]], axis=2
    )
    x_faces = jnp.pad(side_ghost[:, 0:2], ((0, 0), (0, 0), (1, 1), (1, 1)))
    padded = jnp.concatenate([x_faces[:, 0][:, None], with_y, x_faces[:, 1][:, None]], axis=1)
    centre = padded[:, 1:-1, 1:-1, 1:-1]
    minus_x = padded[:, :-2, 1:-1, 1:-1]
    plus_x = padded[:, 2:, 1:-1, 1:-1]
    minus_y = padded[:, 1:-1, :-2, 1:-1]
    plus_y = padded[:, 1:-1, 2:, 1:-1]
    minus_z = padded[:, 1:-1, 1:-1, :-2]
    plus_z = padded[:, 1:-1, 1:-1, 2:]
    laplace = plus_x + minus_x + (plus_y + minus_y) + (plus_z + minus_z) - 6.0 * centre
    diff_x = (plus_x - minus_x) * 0.5
    diff_y = (plus_y - minus_y) * 0.5
    diff_z = (plus_z - minus_z) * 0.5
    gradient = diff_x * diff_x + diff_y * diff_y + diff_z * diff_z
    force = smoothing * laplace + speed_rows[:, None, None, None]
    return centre + time_step * edge_maps * force * jnp.sqrt(1.0 + gradient)


def assemble_ghosts(side_faces, end_faces, beside_lists):
    face_grid = side_faces.reshape((BXN, BYN, BZN) + side_faces.shape[1:])
    widened = extended(shortened(face_grid), (("group", 0), ("dev", 1)), 1).astype(face_grid.dtype)
    from_side = jnp.stack(
        [
            widened[:-2, 1:-1, :, 1],
            widened[2:, 1:-1, :, 0],
            widened[1:-1, :-2, :, 3],
            widened[1:-1, 2:, :, 2],
        ],
        axis=3,
    ).reshape(side_faces.shape)
    end_grid = end_faces.reshape((BXN, BYN, BZN) + end_faces.shape[1:])
    zero_faces = jnp.zeros_like(end_grid[:, :, :1, 0])
    lower_ghost = jnp.concatenate([zero_faces, end_grid[:, :, :-1, 1]], axis=2)
    upper_ghost = jnp.concatenate([end_grid[:, :, 1:, 0], zero_faces], axis=2)
    from_ends = jnp.stack([lower_ghost, upper_ghost], axis=3).reshape(end_faces.shape)
    linked = beside_lists >= 0
    side_ghost = jnp.where(linked[:, :4, None, None], from_side, side_faces)
    end_ghost = jnp.where(linked[:, 4:, None, None], from_ends, end_faces)
    return (side_ghost, end_ghost)


def place_rows(values, target, usable, partners):
    items = values.shape[0]
    matches = (target[None, :] == jnp.arange(partners)[:, None]) & usable[None, :]
    chosen = jnp.sum(jnp.where(matches, jnp.arange(items)[None, :], 0), axis=1)
    present = jnp.any(matches, axis=1)
    picked = jnp.take(values, chosen, axis=0)
    return jnp.where(
        present.reshape((partners,) + (1,) * (values.ndim - 1)), picked, jnp.zeros((), values.dtype)
    )


def extended_many(items, sides):
    cells = [value for value, width in items]
    widths = [width for value, width in items]
    for axis, dim in sides:
        count = lax.axis_size(axis)
        ends = count - 1
        heads = tuple(lax.slice_in_dim(c, 0, w, axis=dim) for c, w in zip(cells, widths))
        tails = tuple(
            lax.slice_in_dim(c, c.shape[dim] - w, c.shape[dim], axis=dim) for c, w in zip(cells, widths)
        )
        from_below = lax.ppermute(tails, axis, [(i, (i + 1) % count) for i in range(ends)])
        from_above = lax.ppermute(heads, axis, [((i + 1) % count, i) for i in range(ends)])
        cells = [
            jnp.concatenate([below, c, above], axis=dim)
            for below, c, above in zip(from_below, cells, from_above)
        ]
    return cells


def extended_packed(em_image, level_set, info):
    cells = [em_image, level_set, info]
    widths = [3 + STEPS, STEPS, 1]
    for axis, dim in (("group", 0), ("dev", 1)):
        count = lax.axis_size(axis)
        ends = count - 1
        parts = []
        for end in (0, 1):
            pieces = []
            for c, w in zip(cells, widths):
                start = 0 if end == 0 else c.shape[dim] - w
                pieces.append(lax.slice_in_dim(c, start, start + w, axis=dim))
            parts.append(pieces)
        def sent(pieces, pairs):
            flat = jnp.concatenate([p.astype(jnp.float32).reshape(-1) for p in pieces])
            flat = lax.ppermute(flat, axis, pairs)
            out = []
            start = 0
            for p in pieces:
                out.append(flat[start : start + p.size].reshape(p.shape).astype(p.dtype))
                start += p.size
            return out
        from_below = sent(parts[1], [(i, i + 1) for i in range(ends)])
        from_above = sent(parts[0], [(i + 1, i) for i in range(ends)])
        cells = [
            jnp.concatenate([below, c, above], axis=dim)
            for below, c, above in zip(from_below, cells, from_above)
        ]
    return cells


def region_step(lvl, edge, rate, code):
    centre = lvl[1:-1, 1:-1]
    shifted = (
        lvl[:-2, 1:-1],
        lvl[2:, 1:-1],
        lvl[1:-1, :-2],
        lvl[1:-1, 2:],
        jnp.concatenate([centre[:, :, :1], centre[:, :, :-1]], axis=2),
        jnp.concatenate([centre[:, :, 1:], centre[:, :, -1:]], axis=2),
    )
    minus_x, plus_x, minus_y, plus_y, minus_z, plus_z = (
        jnp.where((code >> side) & 1 == 1, value, centre) for side, value in enumerate(shifted)
    )
    laplace = plus_x + minus_x + (plus_y + minus_y) + (plus_z + minus_z) - 6.0 * centre
    diff_x = (plus_x - minus_x) * 0.5
    diff_y = (plus_y - minus_y) * 0.5
    diff_z = (plus_z - minus_z) * 0.5
    gradient = diff_x * diff_x + diff_y * diff_y + diff_z * diff_z
    force = smoothing * laplace + rate
    return centre + time_step * edge * force * jnp.sqrt(1.0 + gradient)


def per_device(em_image, level_set, speeds, brick_of_band, neighbours, speed_index):
    partners = lax.axis_size("dev")
    bricks_here = BXN * BYN * BZN
    choose = speed_index[:, None] == jnp.arange(speeds.shape[0])[None, :]
    rates_here = jnp.sum(jnp.where(choose, speeds[None, :], 0.0), axis=1)
    info = jnp.concatenate(
        [(neighbours >= 0).astype(jnp.float32), rates_here[:, None]], axis=1
    ).reshape(BXN, BYN, BZN, 7)
    margin, wide_level, wide_info = extended_packed(em_image, level_set, info)
    window = jnp.pad(margin.astype(jnp.float32), ((0, 0), (0, 0), (3, 3)))
    edge = edge_map(window)
    span_x, span_y, span_z = wide_level.shape
    lead = BX - STEPS
    weights = jnp.asarray([1 << side for side in range(6)] + [0], jnp.int32)
    brick_code = jnp.sum(jnp.where(wide_info > 0.5, weights, 0), axis=-1)
    def planes(per_brick):
        spread = jnp.broadcast_to(
            per_brick.reshape(BXN + 2, BYN + 2, 1, BZN, 1), (BXN + 2, BYN + 2, BY, BZN, BZ)
        ).reshape(BXN + 2, (BYN + 2) * BY, BZN * BZ)
        return spread[:, lead : lead + span_y]
    def across_x(per_brick):
        table = planes(per_brick)
        xe = lax.broadcasted_iota(jnp.int32, wide_level.shape, 0) + lead
        value = table[BXN + 1][None]
        for bx in range(BXN, -1, -1):
            value = jnp.where(xe < (bx + 1) * BX, table[bx][None], value)
        return value
    rate = across_x(wide_info[..., 6])
    place = (
        lax.broadcasted_iota(jnp.int32, wide_level.shape, 0) + lead,
        lax.broadcasted_iota(jnp.int32, wide_level.shape, 1) + lead,
        lax.broadcasted_iota(jnp.int32, wide_level.shape, 2),
    )
    sizes = (BX, BX, BY, BY, BZ, BZ)
    code = across_x(brick_code)
    for side in range(6):
        pos = place[side // 2] % sizes[side]
        inner = pos != (0 if side % 2 == 0 else sizes[side] - 1)
        code = code | (inner.astype(jnp.int32) << side)
    lvl = wide_level
    for repeat in range(STEPS):
        lo = repeat + 1
        hi_x = span_x - repeat - 1
        hi_y = span_y - repeat - 1
        lvl = region_step(lvl, edge[lo:hi_x, lo:hi_y], rate[lo:hi_x, lo:hi_y], code[lo:hi_x, lo:hi_y])
    band_here = brick_of_band.shape[0]
    lower = jnp.concatenate([neighbours[1:, 4], neighbours[:1, 4]])
    upper = jnp.concatenate([neighbours[-1:, 5], neighbours[:-1, 5]])
    first_in_z = jnp.arange(bricks_here, dtype=jnp.int32) % BZN == 0
    band_of = jnp.where(first_in_z, lower, upper)
    in_band = band_of >= 0
    owner_dev = band_of // band_here % partners
    source_dev = brick_of_band // bricks_here % partners
    matches = (owner_dev[None, :] == jnp.arange(partners)[:, None]) & in_band[None, :]
    chosen = jnp.sum(jnp.where(matches, jnp.arange(bricks_here)[None, :], 0), axis=1)
    view = lvl.reshape(BXN, BX, BYN, BY, BZN, BZ)
    sending = view[chosen // (BYN * BZN), :, chosen // BZN % BYN, :, chosen % BZN, :]
    arrived = lax.all_to_all(sending, "dev", split_axis=0, concat_axis=0, tiled=True)
    return jnp.take(arrived, source_dev, axis=0)


def solution(mesh):
    placed = (
        P("group", "dev", None),
        P("group", "dev", None),
        P(),
        P(("group", "dev")),
        P(("group", "dev"), None),
        P(("group", "dev")),
    )
    return jax.shard_map(
        per_device,
        mesh=mesh,
        in_specs=placed,
        out_specs=P(("group", "dev"), None, None, None),
        check_vma=False,
    )
```

```python
import math

import jax
import jax.numpy as jnp
from jax import lax
from jax.sharding import PartitionSpec as P

BX = 16
BY = 16
BZ = 128
BXN = 2
BYN = 2
BZN = 4
STEPS = 4


gauss_raw = [math.exp(-0.5 * position * position) for position in range(-2, 3)]
gauss_taps = [weight / sum(gauss_raw) for weight in gauss_raw]
time_step = 0.2
smoothing = 0.15
contrast = 0.02


def shortened(value):
    return jax.tree.map(lambda a: a.astype(jnp.bfloat16) if a.dtype == jnp.float32 else a, value)


def extended(cells, sides, width):
    for axis, dim in sides:
        count = lax.axis_size(axis)
        ends = count - 1
        head = lax.slice_in_dim(cells, 0, width, axis=dim)
        tail = lax.slice_in_dim(cells, cells.shape[dim] - width, cells.shape[dim], axis=dim)
        cells = jnp.concatenate(
            [
                lax.ppermute(tail, axis, [(i, (i + 1) % count) for i in range(ends)]),
                cells,
                lax.ppermute(head, axis, [((i + 1) % count, i) for i in range(ends)]),
            ],
            axis=dim,
        )
    return cells


def smooth_axis(values, along):
    length = values.shape[along] - 4
    summed = gauss_taps[0] * lax.slice_in_dim(values, 0, length, axis=along)
    for offset in range(1, 5):
        summed = summed + gauss_taps[offset] * lax.slice_in_dim(
            values, offset, offset + length, axis=along
        )
    return summed


def edge_map(window):
    smoothed = smooth_axis(smooth_axis(smooth_axis(window, 0), 1), 2)
    grad_x = (smoothed[2:, 1:-1, 1:-1] - smoothed[:-2, 1:-1, 1:-1]) * 0.5
    grad_y = (smoothed[1:-1, 2:, 1:-1] - smoothed[1:-1, :-2, 1:-1]) * 0.5
    grad_z = (smoothed[1:-1, 1:-1, 2:] - smoothed[1:-1, 1:-1, :-2]) * 0.5
    return 1.0 / (1.0 + (grad_x * grad_x + grad_y * grad_y + grad_z * grad_z) / contrast)


def to_bricks(block):
    shaped = block.reshape(BXN, BX, BYN, BY, BZN, BZ)
    return shaped.transpose(0, 2, 4, 1, 3, 5).reshape(BXN * BYN * BZN, BX, BY, BZ)


def own_faces(levels):
    side_faces = jnp.stack([levels[:, 0], levels[:, -1], levels[:, :, 0], levels[:, :, -1]], axis=1)
    end_faces = jnp.stack([levels[:, :, :, 0], levels[:, :, :, -1]], axis=1)
    return (side_faces, end_faces)


def advance(levels, side_ghost, end_ghost, edge_maps, speed_rows):
    with_z = jnp.concatenate(
        [end_ghost[:, 0][..., None], levels, end_ghost[:, 1][..., None]], axis=3
    )
    y_faces = jnp.pad(side_ghost[:, 2:4], ((0, 0), (0, 0), (0, 0), (1, 1)))
    with_y = jnp.concatenate(
        [y_faces[:, 0][:, :, None, :], with_z, y_faces[:, 1][:, :, None, :]], axis=2
    )
    x_faces = jnp.pad(side_ghost[:, 0:2], ((0, 0), (0, 0), (1, 1), (1, 1)))
    padded = jnp.concatenate([x_faces[:, 0][:, None], with_y, x_faces[:, 1][:, None]], axis=1)
    centre = padded[:, 1:-1, 1:-1, 1:-1]
    minus_x = padded[:, :-2, 1:-1, 1:-1]
    plus_x = padded[:, 2:, 1:-1, 1:-1]
    minus_y = padded[:, 1:-1, :-2, 1:-1]
    plus_y = padded[:, 1:-1, 2:, 1:-1]
    minus_z = padded[:, 1:-1, 1:-1, :-2]
    plus_z = padded[:, 1:-1, 1:-1, 2:]
    laplace = plus_x + minus_x + (plus_y + minus_y) + (plus_z + minus_z) - 6.0 * centre
    diff_x = (plus_x - minus_x) * 0.5
    diff_y = (plus_y - minus_y) * 0.5
    diff_z = (plus_z - minus_z) * 0.5
    gradient = diff_x * diff_x + diff_y * diff_y + diff_z * diff_z
    force = smoothing * laplace + speed_rows[:, None, None, None]
    return centre + time_step * edge_maps * force * jnp.sqrt(1.0 + gradient)


def assemble_ghosts(side_faces, end_faces, beside_lists):
    face_grid = side_faces.reshape((BXN, BYN, BZN) + side_faces.shape[1:])
    widened = extended(shortened(face_grid), (("group", 0), ("dev", 1)), 1).astype(face_grid.dtype)
    from_side = jnp.stack(
        [
            widened[:-2, 1:-1, :, 1],
            widened[2:, 1:-1, :, 0],
            widened[1:-1, :-2, :, 3],
            widened[1:-1, 2:, :, 2],
        ],
        axis=3,
    ).reshape(side_faces.shape)
    end_grid = end_faces.reshape((BXN, BYN, BZN) + end_faces.shape[1:])
    zero_faces = jnp.zeros_like(end_grid[:, :, :1, 0])
    lower_ghost = jnp.concatenate([zero_faces, end_grid[:, :, :-1, 1]], axis=2)
    upper_ghost = jnp.concatenate([end_grid[:, :, 1:, 0], zero_faces], axis=2)
    from_ends = jnp.stack([lower_ghost, upper_ghost], axis=3).reshape(end_faces.shape)
    linked = beside_lists >= 0
    side_ghost = jnp.where(linked[:, :4, None, None], from_side, side_faces)
    end_ghost = jnp.where(linked[:, 4:, None, None], from_ends, end_faces)
    return (side_ghost, end_ghost)


def place_rows(values, target, usable, partners):
    items = values.shape[0]
    matches = (target[None, :] == jnp.arange(partners)[:, None]) & usable[None, :]
    chosen = jnp.sum(jnp.where(matches, jnp.arange(items)[None, :], 0), axis=1)
    present = jnp.any(matches, axis=1)
    picked = jnp.take(values, chosen, axis=0)
    return jnp.where(
        present.reshape((partners,) + (1,) * (values.ndim - 1)), picked, jnp.zeros((), values.dtype)
    )


def extended_many(items, sides):
    cells = [value for value, width in items]
    widths = [width for value, width in items]
    for axis, dim in sides:
        count = lax.axis_size(axis)
        ends = count - 1
        heads = tuple(lax.slice_in_dim(c, 0, w, axis=dim) for c, w in zip(cells, widths))
        tails = tuple(
            lax.slice_in_dim(c, c.shape[dim] - w, c.shape[dim], axis=dim) for c, w in zip(cells, widths)
        )
        from_below = lax.ppermute(tails, axis, [(i, (i + 1) % count) for i in range(ends)])
        from_above = lax.ppermute(heads, axis, [((i + 1) % count, i) for i in range(ends)])
        cells = [
            jnp.concatenate([below, c, above], axis=dim)
            for below, c, above in zip(from_below, cells, from_above)
        ]
    return cells


def extended_packed(em_image, level_set, info):
    cells = [em_image, level_set, info]
    widths = [3 + STEPS, STEPS, 1]
    for axis, dim in (("group", 0), ("dev", 1)):
        count = lax.axis_size(axis)
        ends = count - 1
        parts = []
        for end in (0, 1):
            pieces = []
            for c, w in zip(cells, widths):
                start = 0 if end == 0 else c.shape[dim] - w
                pieces.append(lax.slice_in_dim(c, start, start + w, axis=dim))
            parts.append(pieces)
        def sent(pieces, pairs):
            image_part = lax.ppermute(pieces[0], axis, pairs)
            flat = jnp.concatenate([pieces[1].reshape(-1), pieces[2].reshape(-1)])
            flat = lax.ppermute(flat, axis, pairs)
            size = pieces[1].size
            return [
                image_part,
                flat[:size].reshape(pieces[1].shape),
                flat[size:].reshape(pieces[2].shape),
            ]
        from_below = sent(parts[1], [(i, i + 1) for i in range(ends)])
        from_above = sent(parts[0], [(i + 1, i) for i in range(ends)])
        cells = [
            jnp.concatenate([below, c, above], axis=dim)
            for below, c, above in zip(from_below, cells, from_above)
        ]
    return cells


def region_step(lvl, edge, rate, code):
    centre = lvl[1:-1, 1:-1]
    shifted = (
        lvl[:-2, 1:-1],
        lvl[2:, 1:-1],
        lvl[1:-1, :-2],
        lvl[1:-1, 2:],
        jnp.concatenate([centre[:, :, :1], centre[:, :, :-1]], axis=2),
        jnp.concatenate([centre[:, :, 1:], centre[:, :, -1:]], axis=2),
    )
    minus_x, plus_x, minus_y, plus_y, minus_z, plus_z = (
        jnp.where((code >> side) & 1 == 1, value, centre) for side, value in enumerate(shifted)
    )
    laplace = plus_x + minus_x + (plus_y + minus_y) + (plus_z + minus_z) - 6.0 * centre
    diff_x = (plus_x - minus_x) * 0.5
    diff_y = (plus_y - minus_y) * 0.5
    diff_z = (plus_z - minus_z) * 0.5
    gradient = diff_x * diff_x + diff_y * diff_y + diff_z * diff_z
    force = smoothing * laplace + rate
    return centre + time_step * edge * force * jnp.sqrt(1.0 + gradient)


def per_device(em_image, level_set, speeds, brick_of_band, neighbours, speed_index):
    partners = lax.axis_size("dev")
    bricks_here = BXN * BYN * BZN
    choose = speed_index[:, None] == jnp.arange(speeds.shape[0])[None, :]
    rates_here = jnp.sum(jnp.where(choose, speeds[None, :], 0.0), axis=1)
    info = jnp.concatenate(
        [(neighbours >= 0).astype(jnp.float32), rates_here[:, None]], axis=1
    ).reshape(BXN, BYN, BZN, 7)
    margin, wide_level, wide_info = extended_packed(em_image, level_set, info)
    window = jnp.pad(margin.astype(jnp.float32), ((0, 0), (0, 0), (3, 3)))
    edge = edge_map(window)
    span_x, span_y, span_z = wide_level.shape
    lead = BX - STEPS
    weights = jnp.asarray([1 << side for side in range(6)] + [0], jnp.int32)
    brick_code = jnp.sum(jnp.where(wide_info > 0.5, weights, 0), axis=-1)
    def planes(per_brick):
        spread = jnp.broadcast_to(
            per_brick.reshape(BXN + 2, BYN + 2, 1, BZN, 1), (BXN + 2, BYN + 2, BY, BZN, BZ)
        ).reshape(BXN + 2, (BYN + 2) * BY, BZN * BZ)
        return spread[:, lead : lead + span_y]
    def across_x(per_brick):
        table = planes(per_brick)
        xe = lax.broadcasted_iota(jnp.int32, wide_level.shape, 0) + lead
        value = table[BXN + 1][None]
        for bx in range(BXN, -1, -1):
            value = jnp.where(xe < (bx + 1) * BX, table[bx][None], value)
        return value
    rate = across_x(wide_info[..., 6])
    place = (
        lax.broadcasted_iota(jnp.int32, wide_level.shape, 0) + lead,
        lax.broadcasted_iota(jnp.int32, wide_level.shape, 1) + lead,
        lax.broadcasted_iota(jnp.int32, wide_level.shape, 2),
    )
    sizes = (BX, BX, BY, BY, BZ, BZ)
    code = across_x(brick_code)
    for side in range(6):
        pos = place[side // 2] % sizes[side]
        inner = pos != (0 if side % 2 == 0 else sizes[side] - 1)
        code = code | (inner.astype(jnp.int32) << side)
    lvl = wide_level
    for repeat in range(STEPS):
        lo = repeat + 1
        hi_x = span_x - repeat - 1
        hi_y = span_y - repeat - 1
        lvl = region_step(lvl, edge[lo:hi_x, lo:hi_y], rate[lo:hi_x, lo:hi_y], code[lo:hi_x, lo:hi_y])
    band_here = brick_of_band.shape[0]
    lower = jnp.concatenate([neighbours[1:, 4], neighbours[:1, 4]])
    upper = jnp.concatenate([neighbours[-1:, 5], neighbours[:-1, 5]])
    first_in_z = jnp.arange(bricks_here, dtype=jnp.int32) % BZN == 0
    band_of = jnp.where(first_in_z, lower, upper)
    in_band = band_of >= 0
    owner_dev = band_of // band_here % partners
    source_dev = brick_of_band // bricks_here % partners
    matches = (owner_dev[None, :] == jnp.arange(partners)[:, None]) & in_band[None, :]
    chosen = jnp.sum(jnp.where(matches, jnp.arange(bricks_here)[None, :], 0), axis=1)
    view = lvl.reshape(BXN, BX, BYN, BY, BZN, BZ)
    sending = view.at[chosen // (BYN * BZN), :, chosen // BZN % BYN, :, chosen % BZN, :].get(
        mode="promise_in_bounds"
    )
    arrived = lax.all_to_all(sending, "dev", split_axis=0, concat_axis=0, tiled=True)
    return arrived.at[source_dev].get(mode="promise_in_bounds")


def solution(mesh):
    placed = (
        P("group", "dev", None),
        P("group", "dev", None),
        P(),
        P(("group", "dev")),
        P(("group", "dev"), None),
        P(("group", "dev")),
    )
    return jax.shard_map(
        per_device,
        mesh=mesh,
        in_specs=placed,
        out_specs=P(("group", "dev"), None, None, None),
        check_vma=False,
    )
```

```python
import math

import jax
import jax.numpy as jnp
from jax import lax
from jax.sharding import PartitionSpec as P

BX = 16
BY = 16
BZ = 128
BXN = 2
BYN = 2
BZN = 4
STEPS = 4


gauss_raw = [math.exp(-0.5 * position * position) for position in range(-2, 3)]
gauss_taps = [weight / sum(gauss_raw) for weight in gauss_raw]
time_step = 0.2
smoothing = 0.15
contrast = 0.02


def shortened(value):
    return jax.tree.map(lambda a: a.astype(jnp.bfloat16) if a.dtype == jnp.float32 else a, value)


def extended(cells, sides, width):
    for axis, dim in sides:
        count = lax.axis_size(axis)
        ends = count - 1
        head = lax.slice_in_dim(cells, 0, width, axis=dim)
        tail = lax.slice_in_dim(cells, cells.shape[dim] - width, cells.shape[dim], axis=dim)
        cells = jnp.concatenate(
            [
                lax.ppermute(tail, axis, [(i, (i + 1) % count) for i in range(ends)]),
                cells,
                lax.ppermute(head, axis, [((i + 1) % count, i) for i in range(ends)]),
            ],
            axis=dim,
        )
    return cells


def smooth_axis(values, along):
    length = values.shape[along] - 4
    summed = gauss_taps[0] * lax.slice_in_dim(values, 0, length, axis=along)
    for offset in range(1, 5):
        summed = summed + gauss_taps[offset] * lax.slice_in_dim(
            values, offset, offset + length, axis=along
        )
    return summed


def edge_map(window):
    smoothed = smooth_axis(smooth_axis(smooth_axis(window, 0), 1), 2)
    grad_x = (smoothed[2:, 1:-1, 1:-1] - smoothed[:-2, 1:-1, 1:-1]) * 0.5
    grad_y = (smoothed[1:-1, 2:, 1:-1] - smoothed[1:-1, :-2, 1:-1]) * 0.5
    grad_z = (smoothed[1:-1, 1:-1, 2:] - smoothed[1:-1, 1:-1, :-2]) * 0.5
    return 1.0 / (1.0 + (grad_x * grad_x + grad_y * grad_y + grad_z * grad_z) / contrast)


def to_bricks(block):
    shaped = block.reshape(BXN, BX, BYN, BY, BZN, BZ)
    return shaped.transpose(0, 2, 4, 1, 3, 5).reshape(BXN * BYN * BZN, BX, BY, BZ)


def own_faces(levels):
    side_faces = jnp.stack([levels[:, 0], levels[:, -1], levels[:, :, 0], levels[:, :, -1]], axis=1)
    end_faces = jnp.stack([levels[:, :, :, 0], levels[:, :, :, -1]], axis=1)
    return (side_faces, end_faces)


def advance(levels, side_ghost, end_ghost, edge_maps, speed_rows):
    with_z = jnp.concatenate(
        [end_ghost[:, 0][..., None], levels, end_ghost[:, 1][..., None]], axis=3
    )
    y_faces = jnp.pad(side_ghost[:, 2:4], ((0, 0), (0, 0), (0, 0), (1, 1)))
    with_y = jnp.concatenate(
        [y_faces[:, 0][:, :, None, :], with_z, y_faces[:, 1][:, :, None, :]], axis=2
    )
    x_faces = jnp.pad(side_ghost[:, 0:2], ((0, 0), (0, 0), (1, 1), (1, 1)))
    padded = jnp.concatenate([x_faces[:, 0][:, None], with_y, x_faces[:, 1][:, None]], axis=1)
    centre = padded[:, 1:-1, 1:-1, 1:-1]
    minus_x = padded[:, :-2, 1:-1, 1:-1]
    plus_x = padded[:, 2:, 1:-1, 1:-1]
    minus_y = padded[:, 1:-1, :-2, 1:-1]
    plus_y = padded[:, 1:-1, 2:, 1:-1]
    minus_z = padded[:, 1:-1, 1:-1, :-2]
    plus_z = padded[:, 1:-1, 1:-1, 2:]
    laplace = plus_x + minus_x + (plus_y + minus_y) + (plus_z + minus_z) - 6.0 * centre
    diff_x = (plus_x - minus_x) * 0.5
    diff_y = (plus_y - minus_y) * 0.5
    diff_z = (plus_z - minus_z) * 0.5
    gradient = diff_x * diff_x + diff_y * diff_y + diff_z * diff_z
    force = smoothing * laplace + speed_rows[:, None, None, None]
    return centre + time_step * edge_maps * force * jnp.sqrt(1.0 + gradient)


def assemble_ghosts(side_faces, end_faces, beside_lists):
    face_grid = side_faces.reshape((BXN, BYN, BZN) + side_faces.shape[1:])
    widened = extended(shortened(face_grid), (("group", 0), ("dev", 1)), 1).astype(face_grid.dtype)
    from_side = jnp.stack(
        [
            widened[:-2, 1:-1, :, 1],
            widened[2:, 1:-1, :, 0],
            widened[1:-1, :-2, :, 3],
            widened[1:-1, 2:, :, 2],
        ],
        axis=3,
    ).reshape(side_faces.shape)
    end_grid = end_faces.reshape((BXN, BYN, BZN) + end_faces.shape[1:])
    zero_faces = jnp.zeros_like(end_grid[:, :, :1, 0])
    lower_ghost = jnp.concatenate([zero_faces, end_grid[:, :, :-1, 1]], axis=2)
    upper_ghost = jnp.concatenate([end_grid[:, :, 1:, 0], zero_faces], axis=2)
    from_ends = jnp.stack([lower_ghost, upper_ghost], axis=3).reshape(end_faces.shape)
    linked = beside_lists >= 0
    side_ghost = jnp.where(linked[:, :4, None, None], from_side, side_faces)
    end_ghost = jnp.where(linked[:, 4:, None, None], from_ends, end_faces)
    return (side_ghost, end_ghost)


def place_rows(values, target, usable, partners):
    items = values.shape[0]
    matches = (target[None, :] == jnp.arange(partners)[:, None]) & usable[None, :]
    chosen = jnp.sum(jnp.where(matches, jnp.arange(items)[None, :], 0), axis=1)
    present = jnp.any(matches, axis=1)
    picked = jnp.take(values, chosen, axis=0)
    return jnp.where(
        present.reshape((partners,) + (1,) * (values.ndim - 1)), picked, jnp.zeros((), values.dtype)
    )


def extended_many(items, sides):
    cells = [value for value, width in items]
    widths = [width for value, width in items]
    for axis, dim in sides:
        count = lax.axis_size(axis)
        ends = count - 1
        heads = tuple(lax.slice_in_dim(c, 0, w, axis=dim) for c, w in zip(cells, widths))
        tails = tuple(
            lax.slice_in_dim(c, c.shape[dim] - w, c.shape[dim], axis=dim) for c, w in zip(cells, widths)
        )
        from_below = lax.ppermute(tails, axis, [(i, (i + 1) % count) for i in range(ends)])
        from_above = lax.ppermute(heads, axis, [((i + 1) % count, i) for i in range(ends)])
        cells = [
            jnp.concatenate([below, c, above], axis=dim)
            for below, c, above in zip(from_below, cells, from_above)
        ]
    return cells


def extended_packed(em_image, level_set, info):
    cells = [em_image, level_set, info]
    widths = [3 + STEPS, STEPS, 1]
    for axis, dim in (("group", 0), ("dev", 1)):
        count = lax.axis_size(axis)
        ends = count - 1
        parts = []
        for end in (0, 1):
            pieces = []
            for c, w in zip(cells, widths):
                start = 0 if end == 0 else c.shape[dim] - w
                pieces.append(lax.slice_in_dim(c, start, start + w, axis=dim))
            parts.append(pieces)
        def sent(pieces, pairs):
            image_part = lax.ppermute(pieces[0], axis, pairs)
            flat = jnp.concatenate([pieces[1].reshape(-1), pieces[2].reshape(-1)])
            flat = lax.ppermute(flat, axis, pairs)
            size = pieces[1].size
            return [
                image_part,
                flat[:size].reshape(pieces[1].shape),
                flat[size:].reshape(pieces[2].shape),
            ]
        from_below = sent(parts[1], [(i, i + 1) for i in range(ends)])
        from_above = sent(parts[0], [(i + 1, i) for i in range(ends)])
        cells = [
            jnp.concatenate([below, c, above], axis=dim)
            for below, c, above in zip(from_below, cells, from_above)
        ]
    return cells


def region_step(lvl, edge, rate, code):
    centre = lvl[1:-1, 1:-1]
    shifted = (
        lvl[:-2, 1:-1],
        lvl[2:, 1:-1],
        lvl[1:-1, :-2],
        lvl[1:-1, 2:],
        jnp.concatenate([centre[:, :, :1], centre[:, :, :-1]], axis=2),
        jnp.concatenate([centre[:, :, 1:], centre[:, :, -1:]], axis=2),
    )
    minus_x, plus_x, minus_y, plus_y, minus_z, plus_z = (
        jnp.where((code >> side) & 1 == 1, value, centre) for side, value in enumerate(shifted)
    )
    laplace = plus_x + minus_x + (plus_y + minus_y) + (plus_z + minus_z) - 6.0 * centre
    diff_x = (plus_x - minus_x) * 0.5
    diff_y = (plus_y - minus_y) * 0.5
    diff_z = (plus_z - minus_z) * 0.5
    gradient = diff_x * diff_x + diff_y * diff_y + diff_z * diff_z
    force = smoothing * laplace + rate
    return centre + time_step * edge * force * jnp.sqrt(1.0 + gradient)


def per_device(em_image, level_set, speeds, brick_of_band, neighbours, speed_index):
    partners = lax.axis_size("dev")
    bricks_here = BXN * BYN * BZN
    choose = speed_index[:, None] == jnp.arange(speeds.shape[0])[None, :]
    rates_here = jnp.sum(jnp.where(choose, speeds[None, :], 0.0), axis=1)
    info = jnp.concatenate(
        [(neighbours >= 0).astype(jnp.float32), rates_here[:, None]], axis=1
    ).reshape(BXN, BYN, BZN, 7)
    margin, wide_level, wide_info = extended_packed(em_image, level_set, info)
    window = jnp.pad(margin.astype(jnp.float32), ((0, 0), (0, 0), (3, 3)))
    edge = edge_map(window)
    span_x, span_y, span_z = wide_level.shape
    lead = BX - STEPS
    weights = jnp.asarray([1 << side for side in range(6)] + [0], jnp.int32)
    brick_code = jnp.sum(jnp.where(wide_info > 0.5, weights, 0), axis=-1)
    def planes(per_brick):
        spread = jnp.broadcast_to(
            per_brick.reshape(BXN + 2, BYN + 2, 1, BZN, 1), (BXN + 2, BYN + 2, BY, BZN, BZ)
        ).reshape(BXN + 2, (BYN + 2) * BY, BZN * BZ)
        return spread[:, lead : lead + span_y]
    def across_x(per_brick):
        table = planes(per_brick)
        xe = lax.broadcasted_iota(jnp.int32, wide_level.shape, 0) + lead
        value = table[BXN + 1][None]
        for bx in range(BXN, -1, -1):
            value = jnp.where(xe < (bx + 1) * BX, table[bx][None], value)
        return value
    rate = across_x(wide_info[..., 6])
    place = (
        lax.broadcasted_iota(jnp.int32, wide_level.shape, 0) + lead,
        lax.broadcasted_iota(jnp.int32, wide_level.shape, 1) + lead,
        lax.broadcasted_iota(jnp.int32, wide_level.shape, 2),
    )
    sizes = (BX, BX, BY, BY, BZ, BZ)
    code = across_x(brick_code)
    for side in range(6):
        pos = place[side // 2] % sizes[side]
        inner = pos != (0 if side % 2 == 0 else sizes[side] - 1)
        code = code | (inner.astype(jnp.int32) << side)
    code = code.astype(jnp.int8)
    lvl = wide_level
    for repeat in range(STEPS):
        lo = repeat + 1
        hi_x = span_x - repeat - 1
        hi_y = span_y - repeat - 1
        lvl = region_step(lvl, edge[lo:hi_x, lo:hi_y], rate[lo:hi_x, lo:hi_y], code[lo:hi_x, lo:hi_y])
    band_here = brick_of_band.shape[0]
    lower = jnp.concatenate([neighbours[1:, 4], neighbours[:1, 4]])
    upper = jnp.concatenate([neighbours[-1:, 5], neighbours[:-1, 5]])
    first_in_z = jnp.arange(bricks_here, dtype=jnp.int32) % BZN == 0
    band_of = jnp.where(first_in_z, lower, upper)
    in_band = band_of >= 0
    owner_dev = band_of // band_here % partners
    source_dev = brick_of_band // bricks_here % partners
    matches = (owner_dev[None, :] == jnp.arange(partners)[:, None]) & in_band[None, :]
    chosen = jnp.sum(jnp.where(matches, jnp.arange(bricks_here)[None, :], 0), axis=1)
    view = lvl.reshape(BXN, BX, BYN, BY, BZN, BZ)
    sending = view.at[chosen // (BYN * BZN), :, chosen // BZN % BYN, :, chosen % BZN, :].get(
        mode="promise_in_bounds"
    )
    arrived = lax.all_to_all(sending, "dev", split_axis=0, concat_axis=0, tiled=True)
    return arrived.at[source_dev].get(mode="promise_in_bounds")


def solution(mesh):
    placed = (
        P("group", "dev", None),
        P("group", "dev", None),
        P(),
        P(("group", "dev")),
        P(("group", "dev"), None),
        P(("group", "dev")),
    )
    return jax.shard_map(
        per_device,
        mesh=mesh,
        in_specs=placed,
        out_specs=P(("group", "dev"), None, None, None),
        check_vma=False,
    )
```

```python
import math

import jax
import jax.numpy as jnp
from jax import lax
from jax.sharding import PartitionSpec as P

BX = 16
BY = 16
BZ = 128
BXN = 2
BYN = 2
BZN = 4
STEPS = 4


gauss_raw = [math.exp(-0.5 * position * position) for position in range(-2, 3)]
gauss_taps = [weight / sum(gauss_raw) for weight in gauss_raw]
time_step = 0.2
smoothing = 0.15
contrast = 0.02


def shortened(value):
    return jax.tree.map(lambda a: a.astype(jnp.bfloat16) if a.dtype == jnp.float32 else a, value)


def extended(cells, sides, width):
    for axis, dim in sides:
        count = lax.axis_size(axis)
        ends = count - 1
        head = lax.slice_in_dim(cells, 0, width, axis=dim)
        tail = lax.slice_in_dim(cells, cells.shape[dim] - width, cells.shape[dim], axis=dim)
        cells = jnp.concatenate(
            [
                lax.ppermute(tail, axis, [(i, (i + 1) % count) for i in range(ends)]),
                cells,
                lax.ppermute(head, axis, [((i + 1) % count, i) for i in range(ends)]),
            ],
            axis=dim,
        )
    return cells


def smooth_axis(values, along):
    length = values.shape[along] - 4
    summed = gauss_taps[0] * lax.slice_in_dim(values, 0, length, axis=along)
    for offset in range(1, 5):
        summed = summed + gauss_taps[offset] * lax.slice_in_dim(
            values, offset, offset + length, axis=along
        )
    return summed


def edge_map(window):
    smoothed = smooth_axis(smooth_axis(smooth_axis(window, 0), 1), 2)
    grad_x = (smoothed[2:, 1:-1, 1:-1] - smoothed[:-2, 1:-1, 1:-1]) * 0.5
    grad_y = (smoothed[1:-1, 2:, 1:-1] - smoothed[1:-1, :-2, 1:-1]) * 0.5
    grad_z = (smoothed[1:-1, 1:-1, 2:] - smoothed[1:-1, 1:-1, :-2]) * 0.5
    return 1.0 / (1.0 + (grad_x * grad_x + grad_y * grad_y + grad_z * grad_z) / contrast)


def to_bricks(block):
    shaped = block.reshape(BXN, BX, BYN, BY, BZN, BZ)
    return shaped.transpose(0, 2, 4, 1, 3, 5).reshape(BXN * BYN * BZN, BX, BY, BZ)


def own_faces(levels):
    side_faces = jnp.stack([levels[:, 0], levels[:, -1], levels[:, :, 0], levels[:, :, -1]], axis=1)
    end_faces = jnp.stack([levels[:, :, :, 0], levels[:, :, :, -1]], axis=1)
    return (side_faces, end_faces)


def advance(levels, side_ghost, end_ghost, edge_maps, speed_rows):
    with_z = jnp.concatenate(
        [end_ghost[:, 0][..., None], levels, end_ghost[:, 1][..., None]], axis=3
    )
    y_faces = jnp.pad(side_ghost[:, 2:4], ((0, 0), (0, 0), (0, 0), (1, 1)))
    with_y = jnp.concatenate(
        [y_faces[:, 0][:, :, None, :], with_z, y_faces[:, 1][:, :, None, :]], axis=2
    )
    x_faces = jnp.pad(side_ghost[:, 0:2], ((0, 0), (0, 0), (1, 1), (1, 1)))
    padded = jnp.concatenate([x_faces[:, 0][:, None], with_y, x_faces[:, 1][:, None]], axis=1)
    centre = padded[:, 1:-1, 1:-1, 1:-1]
    minus_x = padded[:, :-2, 1:-1, 1:-1]
    plus_x = padded[:, 2:, 1:-1, 1:-1]
    minus_y = padded[:, 1:-1, :-2, 1:-1]
    plus_y = padded[:, 1:-1, 2:, 1:-1]
    minus_z = padded[:, 1:-1, 1:-1, :-2]
    plus_z = padded[:, 1:-1, 1:-1, 2:]
    laplace = plus_x + minus_x + (plus_y + minus_y) + (plus_z + minus_z) - 6.0 * centre
    diff_x = (plus_x - minus_x) * 0.5
    diff_y = (plus_y - minus_y) * 0.5
    diff_z = (plus_z - minus_z) * 0.5
    gradient = diff_x * diff_x + diff_y * diff_y + diff_z * diff_z
    force = smoothing * laplace + speed_rows[:, None, None, None]
    return centre + time_step * edge_maps * force * jnp.sqrt(1.0 + gradient)


def assemble_ghosts(side_faces, end_faces, beside_lists):
    face_grid = side_faces.reshape((BXN, BYN, BZN) + side_faces.shape[1:])
    widened = extended(shortened(face_grid), (("group", 0), ("dev", 1)), 1).astype(face_grid.dtype)
    from_side = jnp.stack(
        [
            widened[:-2, 1:-1, :, 1],
            widened[2:, 1:-1, :, 0],
            widened[1:-1, :-2, :, 3],
            widened[1:-1, 2:, :, 2],
        ],
        axis=3,
    ).reshape(side_faces.shape)
    end_grid = end_faces.reshape((BXN, BYN, BZN) + end_faces.shape[1:])
    zero_faces = jnp.zeros_like(end_grid[:, :, :1, 0])
    lower_ghost = jnp.concatenate([zero_faces, end_grid[:, :, :-1, 1]], axis=2)
    upper_ghost = jnp.concatenate([end_grid[:, :, 1:, 0], zero_faces], axis=2)
    from_ends = jnp.stack([lower_ghost, upper_ghost], axis=3).reshape(end_faces.shape)
    linked = beside_lists >= 0
    side_ghost = jnp.where(linked[:, :4, None, None], from_side, side_faces)
    end_ghost = jnp.where(linked[:, 4:, None, None], from_ends, end_faces)
    return (side_ghost, end_ghost)


def place_rows(values, target, usable, partners):
    items = values.shape[0]
    matches = (target[None, :] == jnp.arange(partners)[:, None]) & usable[None, :]
    chosen = jnp.sum(jnp.where(matches, jnp.arange(items)[None, :], 0), axis=1)
    present = jnp.any(matches, axis=1)
    picked = jnp.take(values, chosen, axis=0)
    return jnp.where(
        present.reshape((partners,) + (1,) * (values.ndim - 1)), picked, jnp.zeros((), values.dtype)
    )


def extended_many(items, sides):
    cells = [value for value, width in items]
    widths = [width for value, width in items]
    for axis, dim in sides:
        count = lax.axis_size(axis)
        ends = count - 1
        heads = tuple(lax.slice_in_dim(c, 0, w, axis=dim) for c, w in zip(cells, widths))
        tails = tuple(
            lax.slice_in_dim(c, c.shape[dim] - w, c.shape[dim], axis=dim) for c, w in zip(cells, widths)
        )
        from_below = lax.ppermute(tails, axis, [(i, (i + 1) % count) for i in range(ends)])
        from_above = lax.ppermute(heads, axis, [((i + 1) % count, i) for i in range(ends)])
        cells = [
            jnp.concatenate([below, c, above], axis=dim)
            for below, c, above in zip(from_below, cells, from_above)
        ]
    return cells


def extended_packed(em_image, level_set, info):
    cells = [em_image, level_set, info]
    widths = [3 + STEPS, STEPS, 1]
    for axis, dim in (("group", 0), ("dev", 1)):
        count = lax.axis_size(axis)
        ends = count - 1
        parts = []
        for end in (0, 1):
            pieces = []
            for c, w in zip(cells, widths):
                start = 0 if end == 0 else c.shape[dim] - w
                pieces.append(lax.slice_in_dim(c, start, start + w, axis=dim))
            parts.append(pieces)
        def sent(pieces, pairs):
            image_part = lax.ppermute(pieces[0], axis, pairs)
            flat = jnp.concatenate([pieces[1].reshape(-1), pieces[2].reshape(-1)])
            flat = lax.ppermute(flat, axis, pairs)
            size = pieces[1].size
            return [
                image_part,
                flat[:size].reshape(pieces[1].shape),
                flat[size:].reshape(pieces[2].shape),
            ]
        from_below = sent(parts[1], [(i, i + 1) for i in range(ends)])
        from_above = sent(parts[0], [(i + 1, i) for i in range(ends)])
        cells = [
            jnp.concatenate([below, c, above], axis=dim)
            for below, c, above in zip(from_below, cells, from_above)
        ]
    return cells


def region_step(lvl, edge, rate, code):
    centre = lvl[1:-1, 1:-1]
    shifted = (
        lvl[:-2, 1:-1],
        lvl[2:, 1:-1],
        lvl[1:-1, :-2],
        lvl[1:-1, 2:],
        jnp.concatenate([centre[:, :, :1], centre[:, :, :-1]], axis=2),
        jnp.concatenate([centre[:, :, 1:], centre[:, :, -1:]], axis=2),
    )
    minus_x, plus_x, minus_y, plus_y, minus_z, plus_z = (
        jnp.where((code >> side) & 1 == 1, value, centre) for side, value in enumerate(shifted)
    )
    laplace = plus_x + minus_x + (plus_y + minus_y) + (plus_z + minus_z) - 6.0 * centre
    diff_x = (plus_x - minus_x) * 0.5
    diff_y = (plus_y - minus_y) * 0.5
    diff_z = (plus_z - minus_z) * 0.5
    gradient = diff_x * diff_x + diff_y * diff_y + diff_z * diff_z
    force = smoothing * laplace + rate
    return centre + time_step * edge * force * jnp.sqrt(1.0 + gradient)


def per_device(em_image, level_set, speeds, brick_of_band, neighbours, speed_index):
    partners = lax.axis_size("dev")
    bricks_here = BXN * BYN * BZN
    choose = speed_index[:, None] == jnp.arange(speeds.shape[0])[None, :]
    rates_here = jnp.sum(jnp.where(choose, speeds[None, :], 0.0), axis=1)
    info = jnp.concatenate(
        [(neighbours >= 0).astype(jnp.float32), rates_here[:, None]], axis=1
    ).reshape(BXN, BYN, BZN, 7)
    margin, wide_level, wide_info = extended_packed(em_image, level_set, info)
    window = jnp.pad(margin.astype(jnp.float32), ((0, 0), (0, 0), (3, 3)))
    edge = edge_map(window)
    span_x, span_y, span_z = wide_level.shape
    lead = BX - STEPS
    weights = jnp.asarray([1 << side for side in range(6)] + [0], jnp.int32)
    brick_code = jnp.sum(jnp.where(wide_info > 0.5, weights, 0), axis=-1)
    def spread(per_brick):
        table = jnp.broadcast_to(
            per_brick.reshape(BXN + 2, 1, BYN + 2, 1, BZN), (BXN + 2, BX, BYN + 2, BY, BZN)
        ).reshape((BXN + 2) * BX, (BYN + 2) * BY, BZN)
        table = table[lead : lead + span_x, lead : lead + span_y]
        return jnp.broadcast_to(table[..., None], (span_x, span_y, BZN, BZ)).reshape(
            span_x, span_y, BZN * BZ
        )
    rate = spread(wide_info[..., 6])
    place = (
        lax.broadcasted_iota(jnp.int32, wide_level.shape, 0) + lead,
        lax.broadcasted_iota(jnp.int32, wide_level.shape, 1) + lead,
        lax.broadcasted_iota(jnp.int32, wide_level.shape, 2),
    )
    sizes = (BX, BX, BY, BY, BZ, BZ)
    code = spread(brick_code)
    for side in range(6):
        pos = place[side // 2] % sizes[side]
        inner = pos != (0 if side % 2 == 0 else sizes[side] - 1)
        code = code | (inner.astype(jnp.int32) << side)
    lvl = wide_level
    for repeat in range(STEPS):
        lo = repeat + 1
        hi_x = span_x - repeat - 1
        hi_y = span_y - repeat - 1
        lvl = region_step(lvl, edge[lo:hi_x, lo:hi_y], rate[lo:hi_x, lo:hi_y], code[lo:hi_x, lo:hi_y])
    band_here = brick_of_band.shape[0]
    lower = jnp.concatenate([neighbours[1:, 4], neighbours[:1, 4]])
    upper = jnp.concatenate([neighbours[-1:, 5], neighbours[:-1, 5]])
    first_in_z = jnp.arange(bricks_here, dtype=jnp.int32) % BZN == 0
    band_of = jnp.where(first_in_z, lower, upper)
    in_band = band_of >= 0
    owner_dev = band_of // band_here % partners
    source_dev = brick_of_band // bricks_here % partners
    matches = (owner_dev[None, :] == jnp.arange(partners)[:, None]) & in_band[None, :]
    chosen = jnp.sum(jnp.where(matches, jnp.arange(bricks_here)[None, :], 0), axis=1)
    view = lvl.reshape(BXN, BX, BYN, BY, BZN, BZ)
    sending = view.at[chosen // (BYN * BZN), :, chosen // BZN % BYN, :, chosen % BZN, :].get(
        mode="promise_in_bounds"
    )
    arrived = lax.all_to_all(sending, "dev", split_axis=0, concat_axis=0, tiled=True)
    return arrived.at[source_dev].get(mode="promise_in_bounds")


def solution(mesh):
    placed = (
        P("group", "dev", None),
        P("group", "dev", None),
        P(),
        P(("group", "dev")),
        P(("group", "dev"), None),
        P(("group", "dev")),
    )
    return jax.shard_map(
        per_device,
        mesh=mesh,
        in_specs=placed,
        out_specs=P(("group", "dev"), None, None, None),
        check_vma=False,
    )
```

```python
import math

import jax
import jax.numpy as jnp
from jax import lax
from jax.sharding import PartitionSpec as P

BX = 16
BY = 16
BZ = 128
BXN = 2
BYN = 2
BZN = 4
STEPS = 4


gauss_raw = [math.exp(-0.5 * position * position) for position in range(-2, 3)]
gauss_taps = [weight / sum(gauss_raw) for weight in gauss_raw]
time_step = 0.2
smoothing = 0.15
contrast = 0.02


def shortened(value):
    return jax.tree.map(lambda a: a.astype(jnp.bfloat16) if a.dtype == jnp.float32 else a, value)


def extended(cells, sides, width):
    for axis, dim in sides:
        count = lax.axis_size(axis)
        ends = count - 1
        head = lax.slice_in_dim(cells, 0, width, axis=dim)
        tail = lax.slice_in_dim(cells, cells.shape[dim] - width, cells.shape[dim], axis=dim)
        cells = jnp.concatenate(
            [
                lax.ppermute(tail, axis, [(i, (i + 1) % count) for i in range(ends)]),
                cells,
                lax.ppermute(head, axis, [((i + 1) % count, i) for i in range(ends)]),
            ],
            axis=dim,
        )
    return cells


def smooth_axis(values, along):
    length = values.shape[along] - 4
    summed = gauss_taps[0] * lax.slice_in_dim(values, 0, length, axis=along)
    for offset in range(1, 5):
        summed = summed + gauss_taps[offset] * lax.slice_in_dim(
            values, offset, offset + length, axis=along
        )
    return summed


def edge_map(window):
    smoothed = smooth_axis(smooth_axis(smooth_axis(window, 0), 1), 2)
    grad_x = (smoothed[2:, 1:-1, 1:-1] - smoothed[:-2, 1:-1, 1:-1]) * 0.5
    grad_y = (smoothed[1:-1, 2:, 1:-1] - smoothed[1:-1, :-2, 1:-1]) * 0.5
    grad_z = (smoothed[1:-1, 1:-1, 2:] - smoothed[1:-1, 1:-1, :-2]) * 0.5
    return 1.0 / (1.0 + (grad_x * grad_x + grad_y * grad_y + grad_z * grad_z) / contrast)


def to_bricks(block):
    shaped = block.reshape(BXN, BX, BYN, BY, BZN, BZ)
    return shaped.transpose(0, 2, 4, 1, 3, 5).reshape(BXN * BYN * BZN, BX, BY, BZ)


def own_faces(levels):
    side_faces = jnp.stack([levels[:, 0], levels[:, -1], levels[:, :, 0], levels[:, :, -1]], axis=1)
    end_faces = jnp.stack([levels[:, :, :, 0], levels[:, :, :, -1]], axis=1)
    return (side_faces, end_faces)


def advance(levels, side_ghost, end_ghost, edge_maps, speed_rows):
    with_z = jnp.concatenate(
        [end_ghost[:, 0][..., None], levels, end_ghost[:, 1][..., None]], axis=3
    )
    y_faces = jnp.pad(side_ghost[:, 2:4], ((0, 0), (0, 0), (0, 0), (1, 1)))
    with_y = jnp.concatenate(
        [y_faces[:, 0][:, :, None, :], with_z, y_faces[:, 1][:, :, None, :]], axis=2
    )
    x_faces = jnp.pad(side_ghost[:, 0:2], ((0, 0), (0, 0), (1, 1), (1, 1)))
    padded = jnp.concatenate([x_faces[:, 0][:, None], with_y, x_faces[:, 1][:, None]], axis=1)
    centre = padded[:, 1:-1, 1:-1, 1:-1]
    minus_x = padded[:, :-2, 1:-1, 1:-1]
    plus_x = padded[:, 2:, 1:-1, 1:-1]
    minus_y = padded[:, 1:-1, :-2, 1:-1]
    plus_y = padded[:, 1:-1, 2:, 1:-1]
    minus_z = padded[:, 1:-1, 1:-1, :-2]
    plus_z = padded[:, 1:-1, 1:-1, 2:]
    laplace = plus_x + minus_x + (plus_y + minus_y) + (plus_z + minus_z) - 6.0 * centre
    diff_x = (plus_x - minus_x) * 0.5
    diff_y = (plus_y - minus_y) * 0.5
    diff_z = (plus_z - minus_z) * 0.5
    gradient = diff_x * diff_x + diff_y * diff_y + diff_z * diff_z
    force = smoothing * laplace + speed_rows[:, None, None, None]
    return centre + time_step * edge_maps * force * jnp.sqrt(1.0 + gradient)


def assemble_ghosts(side_faces, end_faces, beside_lists):
    face_grid = side_faces.reshape((BXN, BYN, BZN) + side_faces.shape[1:])
    widened = extended(shortened(face_grid), (("group", 0), ("dev", 1)), 1).astype(face_grid.dtype)
    from_side = jnp.stack(
        [
            widened[:-2, 1:-1, :, 1],
            widened[2:, 1:-1, :, 0],
            widened[1:-1, :-2, :, 3],
            widened[1:-1, 2:, :, 2],
        ],
        axis=3,
    ).reshape(side_faces.shape)
    end_grid = end_faces.reshape((BXN, BYN, BZN) + end_faces.shape[1:])
    zero_faces = jnp.zeros_like(end_grid[:, :, :1, 0])
    lower_ghost = jnp.concatenate([zero_faces, end_grid[:, :, :-1, 1]], axis=2)
    upper_ghost = jnp.concatenate([end_grid[:, :, 1:, 0], zero_faces], axis=2)
    from_ends = jnp.stack([lower_ghost, upper_ghost], axis=3).reshape(end_faces.shape)
    linked = beside_lists >= 0
    side_ghost = jnp.where(linked[:, :4, None, None], from_side, side_faces)
    end_ghost = jnp.where(linked[:, 4:, None, None], from_ends, end_faces)
    return (side_ghost, end_ghost)


def place_rows(values, target, usable, partners):
    items = values.shape[0]
    matches = (target[None, :] == jnp.arange(partners)[:, None]) & usable[None, :]
    chosen = jnp.sum(jnp.where(matches, jnp.arange(items)[None, :], 0), axis=1)
    present = jnp.any(matches, axis=1)
    picked = jnp.take(values, chosen, axis=0)
    return jnp.where(
        present.reshape((partners,) + (1,) * (values.ndim - 1)), picked, jnp.zeros((), values.dtype)
    )


def extended_many(items, sides):
    cells = [value for value, width in items]
    widths = [width for value, width in items]
    for axis, dim in sides:
        count = lax.axis_size(axis)
        ends = count - 1
        heads = tuple(lax.slice_in_dim(c, 0, w, axis=dim) for c, w in zip(cells, widths))
        tails = tuple(
            lax.slice_in_dim(c, c.shape[dim] - w, c.shape[dim], axis=dim) for c, w in zip(cells, widths)
        )
        from_below = lax.ppermute(tails, axis, [(i, (i + 1) % count) for i in range(ends)])
        from_above = lax.ppermute(heads, axis, [((i + 1) % count, i) for i in range(ends)])
        cells = [
            jnp.concatenate([below, c, above], axis=dim)
            for below, c, above in zip(from_below, cells, from_above)
        ]
    return cells


def extended_packed(em_image, level_set, info):
    cells = [em_image, level_set, info]
    widths = [3 + STEPS, STEPS, 1]
    for axis, dim in (("group", 0), ("dev", 1)):
        count = lax.axis_size(axis)
        ends = count - 1
        parts = []
        for end in (0, 1):
            pieces = []
            for c, w in zip(cells, widths):
                start = 0 if end == 0 else c.shape[dim] - w
                pieces.append(lax.slice_in_dim(c, start, start + w, axis=dim))
            parts.append(pieces)
        def sent(pieces, pairs):
            image_part = lax.ppermute(pieces[0], axis, pairs)
            flat = jnp.concatenate([pieces[1].reshape(-1), pieces[2].reshape(-1)])
            flat = lax.ppermute(flat, axis, pairs)
            size = pieces[1].size
            return [
                image_part,
                flat[:size].reshape(pieces[1].shape),
                flat[size:].reshape(pieces[2].shape),
            ]
        from_below = sent(parts[1], [(i, i + 1) for i in range(ends)])
        from_above = sent(parts[0], [(i + 1, i) for i in range(ends)])
        cells = [
            jnp.concatenate([below, c, above], axis=dim)
            for below, c, above in zip(from_below, cells, from_above)
        ]
    return cells


def region_step(lvl, edge, rate, code):
    centre = lvl[1:-1, 1:-1]
    shifted = (
        lvl[:-2, 1:-1],
        lvl[2:, 1:-1],
        lvl[1:-1, :-2],
        lvl[1:-1, 2:],
        jnp.concatenate([centre[:, :, :1], centre[:, :, :-1]], axis=2),
        jnp.concatenate([centre[:, :, 1:], centre[:, :, -1:]], axis=2),
    )
    minus_x, plus_x, minus_y, plus_y, minus_z, plus_z = (
        jnp.where((code >> side) & 1 == 1, value, centre) for side, value in enumerate(shifted)
    )
    laplace = plus_x + minus_x + (plus_y + minus_y) + (plus_z + minus_z) - 6.0 * centre
    diff_x = (plus_x - minus_x) * 0.5
    diff_y = (plus_y - minus_y) * 0.5
    diff_z = (plus_z - minus_z) * 0.5
    gradient = diff_x * diff_x + diff_y * diff_y + diff_z * diff_z
    force = smoothing * laplace + rate
    return centre + time_step * edge * force * jnp.sqrt(1.0 + gradient)


def per_device(em_image, level_set, speeds, brick_of_band, neighbours, speed_index):
    partners = lax.axis_size("dev")
    bricks_here = BXN * BYN * BZN
    choose = speed_index[:, None] == jnp.arange(speeds.shape[0])[None, :]
    rates_here = jnp.sum(jnp.where(choose, speeds[None, :], 0.0), axis=1)
    info = jnp.concatenate(
        [(neighbours >= 0).astype(jnp.float32), rates_here[:, None]], axis=1
    ).reshape(BXN, BYN, BZN, 7)
    margin, wide_level, wide_info = extended_packed(em_image, level_set, info)
    window = jnp.pad(margin.astype(jnp.float32), ((0, 0), (0, 0), (3, 3)))
    edge = edge_map(window)
    span_x, span_y, span_z = wide_level.shape
    lead = BX - STEPS
    weights = jnp.asarray([1 << side for side in range(6)] + [0], jnp.int32)
    brick_code = jnp.sum(jnp.where(wide_info > 0.5, weights, 0), axis=-1)
    def spread(per_brick):
        table = jnp.broadcast_to(
            per_brick.reshape(BXN + 2, 1, BYN + 2, 1, BZN), (BXN + 2, BX, BYN + 2, BY, BZN)
        ).reshape((BXN + 2) * BX, (BYN + 2) * BY, BZN)
        table = table[lead : lead + span_x, lead : lead + span_y]
        zi = lax.broadcasted_iota(jnp.int32, wide_level.shape, 2)
        value = table[:, :, BZN - 1][..., None]
        for bz in range(BZN - 2, -1, -1):
            value = jnp.where(zi < (bz + 1) * BZ, table[:, :, bz][..., None], value)
        return value
    rate = spread(wide_info[..., 6])
    place = (
        lax.broadcasted_iota(jnp.int32, wide_level.shape, 0) + lead,
        lax.broadcasted_iota(jnp.int32, wide_level.shape, 1) + lead,
        lax.broadcasted_iota(jnp.int32, wide_level.shape, 2),
    )
    sizes = (BX, BX, BY, BY, BZ, BZ)
    code = spread(brick_code)
    for side in range(6):
        pos = place[side // 2] % sizes[side]
        inner = pos != (0 if side % 2 == 0 else sizes[side] - 1)
        code = code | (inner.astype(jnp.int32) << side)
    lvl = wide_level
    for repeat in range(STEPS):
        lo = repeat + 1
        hi_x = span_x - repeat - 1
        hi_y = span_y - repeat - 1
        lvl = region_step(lvl, edge[lo:hi_x, lo:hi_y], rate[lo:hi_x, lo:hi_y], code[lo:hi_x, lo:hi_y])
    band_here = brick_of_band.shape[0]
    lower = jnp.concatenate([neighbours[1:, 4], neighbours[:1, 4]])
    upper = jnp.concatenate([neighbours[-1:, 5], neighbours[:-1, 5]])
    first_in_z = jnp.arange(bricks_here, dtype=jnp.int32) % BZN == 0
    band_of = jnp.where(first_in_z, lower, upper)
    in_band = band_of >= 0
    owner_dev = band_of // band_here % partners
    source_dev = brick_of_band // bricks_here % partners
    matches = (owner_dev[None, :] == jnp.arange(partners)[:, None]) & in_band[None, :]
    chosen = jnp.sum(jnp.where(matches, jnp.arange(bricks_here)[None, :], 0), axis=1)
    view = lvl.reshape(BXN, BX, BYN, BY, BZN, BZ)
    sending = view.at[chosen // (BYN * BZN), :, chosen // BZN % BYN, :, chosen % BZN, :].get(
        mode="promise_in_bounds"
    )
    arrived = lax.all_to_all(sending, "dev", split_axis=0, concat_axis=0, tiled=True)
    return arrived.at[source_dev].get(mode="promise_in_bounds")


def solution(mesh):
    placed = (
        P("group", "dev", None),
        P("group", "dev", None),
        P(),
        P(("group", "dev")),
        P(("group", "dev"), None),
        P(("group", "dev")),
    )
    return jax.shard_map(
        per_device,
        mesh=mesh,
        in_specs=placed,
        out_specs=P(("group", "dev"), None, None, None),
        check_vma=False,
    )
```

```python
import math

import jax
import jax.numpy as jnp
from jax import lax
from jax.sharding import PartitionSpec as P

BX = 16
BY = 16
BZ = 128
BXN = 2
BYN = 2
BZN = 4
STEPS = 4


gauss_raw = [math.exp(-0.5 * position * position) for position in range(-2, 3)]
gauss_taps = [weight / sum(gauss_raw) for weight in gauss_raw]
time_step = 0.2
smoothing = 0.15
contrast = 0.02


def shortened(value):
    return jax.tree.map(lambda a: a.astype(jnp.bfloat16) if a.dtype == jnp.float32 else a, value)


def extended(cells, sides, width):
    for axis, dim in sides:
        count = lax.axis_size(axis)
        ends = count - 1
        head = lax.slice_in_dim(cells, 0, width, axis=dim)
        tail = lax.slice_in_dim(cells, cells.shape[dim] - width, cells.shape[dim], axis=dim)
        cells = jnp.concatenate(
            [
                lax.ppermute(tail, axis, [(i, (i + 1) % count) for i in range(ends)]),
                cells,
                lax.ppermute(head, axis, [((i + 1) % count, i) for i in range(ends)]),
            ],
            axis=dim,
        )
    return cells


def smooth_axis(values, along):
    length = values.shape[along] - 4
    summed = gauss_taps[0] * lax.slice_in_dim(values, 0, length, axis=along)
    for offset in range(1, 5):
        summed = summed + gauss_taps[offset] * lax.slice_in_dim(
            values, offset, offset + length, axis=along
        )
    return summed


def edge_map(window):
    smoothed = smooth_axis(smooth_axis(smooth_axis(window, 0), 1), 2)
    grad_x = (smoothed[2:, 1:-1, 1:-1] - smoothed[:-2, 1:-1, 1:-1]) * 0.5
    grad_y = (smoothed[1:-1, 2:, 1:-1] - smoothed[1:-1, :-2, 1:-1]) * 0.5
    grad_z = (smoothed[1:-1, 1:-1, 2:] - smoothed[1:-1, 1:-1, :-2]) * 0.5
    return 1.0 / (1.0 + (grad_x * grad_x + grad_y * grad_y + grad_z * grad_z) / contrast)


def to_bricks(block):
    shaped = block.reshape(BXN, BX, BYN, BY, BZN, BZ)
    return shaped.transpose(0, 2, 4, 1, 3, 5).reshape(BXN * BYN * BZN, BX, BY, BZ)


def own_faces(levels):
    side_faces = jnp.stack([levels[:, 0], levels[:, -1], levels[:, :, 0], levels[:, :, -1]], axis=1)
    end_faces = jnp.stack([levels[:, :, :, 0], levels[:, :, :, -1]], axis=1)
    return (side_faces, end_faces)


def advance(levels, side_ghost, end_ghost, edge_maps, speed_rows):
    with_z = jnp.concatenate(
        [end_ghost[:, 0][..., None], levels, end_ghost[:, 1][..., None]], axis=3
    )
    y_faces = jnp.pad(side_ghost[:, 2:4], ((0, 0), (0, 0), (0, 0), (1, 1)))
    with_y = jnp.concatenate(
        [y_faces[:, 0][:, :, None, :], with_z, y_faces[:, 1][:, :, None, :]], axis=2
    )
    x_faces = jnp.pad(side_ghost[:, 0:2], ((0, 0), (0, 0), (1, 1), (1, 1)))
    padded = jnp.concatenate([x_faces[:, 0][:, None], with_y, x_faces[:, 1][:, None]], axis=1)
    centre = padded[:, 1:-1, 1:-1, 1:-1]
    minus_x = padded[:, :-2, 1:-1, 1:-1]
    plus_x = padded[:, 2:, 1:-1, 1:-1]
    minus_y = padded[:, 1:-1, :-2, 1:-1]
    plus_y = padded[:, 1:-1, 2:, 1:-1]
    minus_z = padded[:, 1:-1, 1:-1, :-2]
    plus_z = padded[:, 1:-1, 1:-1, 2:]
    laplace = plus_x + minus_x + (plus_y + minus_y) + (plus_z + minus_z) - 6.0 * centre
    diff_x = (plus_x - minus_x) * 0.5
    diff_y = (plus_y - minus_y) * 0.5
    diff_z = (plus_z - minus_z) * 0.5
    gradient = diff_x * diff_x + diff_y * diff_y + diff_z * diff_z
    force = smoothing * laplace + speed_rows[:, None, None, None]
    return centre + time_step * edge_maps * force * jnp.sqrt(1.0 + gradient)


def assemble_ghosts(side_faces, end_faces, beside_lists):
    face_grid = side_faces.reshape((BXN, BYN, BZN) + side_faces.shape[1:])
    widened = extended(shortened(face_grid), (("group", 0), ("dev", 1)), 1).astype(face_grid.dtype)
    from_side = jnp.stack(
        [
            widened[:-2, 1:-1, :, 1],
            widened[2:, 1:-1, :, 0],
            widened[1:-1, :-2, :, 3],
            widened[1:-1, 2:, :, 2],
        ],
        axis=3,
    ).reshape(side_faces.shape)
    end_grid = end_faces.reshape((BXN, BYN, BZN) + end_faces.shape[1:])
    zero_faces = jnp.zeros_like(end_grid[:, :, :1, 0])
    lower_ghost = jnp.concatenate([zero_faces, end_grid[:, :, :-1, 1]], axis=2)
    upper_ghost = jnp.concatenate([end_grid[:, :, 1:, 0], zero_faces], axis=2)
    from_ends = jnp.stack([lower_ghost, upper_ghost], axis=3).reshape(end_faces.shape)
    linked = beside_lists >= 0
    side_ghost = jnp.where(linked[:, :4, None, None], from_side, side_faces)
    end_ghost = jnp.where(linked[:, 4:, None, None], from_ends, end_faces)
    return (side_ghost, end_ghost)


def place_rows(values, target, usable, partners):
    items = values.shape[0]
    matches = (target[None, :] == jnp.arange(partners)[:, None]) & usable[None, :]
    chosen = jnp.sum(jnp.where(matches, jnp.arange(items)[None, :], 0), axis=1)
    present = jnp.any(matches, axis=1)
    picked = jnp.take(values, chosen, axis=0)
    return jnp.where(
        present.reshape((partners,) + (1,) * (values.ndim - 1)), picked, jnp.zeros((), values.dtype)
    )


def extended_many(items, sides):
    cells = [value for value, width in items]
    widths = [width for value, width in items]
    for axis, dim in sides:
        count = lax.axis_size(axis)
        ends = count - 1
        heads = tuple(lax.slice_in_dim(c, 0, w, axis=dim) for c, w in zip(cells, widths))
        tails = tuple(
            lax.slice_in_dim(c, c.shape[dim] - w, c.shape[dim], axis=dim) for c, w in zip(cells, widths)
        )
        from_below = lax.ppermute(tails, axis, [(i, (i + 1) % count) for i in range(ends)])
        from_above = lax.ppermute(heads, axis, [((i + 1) % count, i) for i in range(ends)])
        cells = [
            jnp.concatenate([below, c, above], axis=dim)
            for below, c, above in zip(from_below, cells, from_above)
        ]
    return cells


def extended_packed(em_image, level_set, info):
    cells = [em_image, level_set, info]
    widths = [3 + STEPS, STEPS, 1]
    for axis, dim in (("group", 0), ("dev", 1)):
        count = lax.axis_size(axis)
        ends = count - 1
        parts = []
        for end in (0, 1):
            pieces = []
            for c, w in zip(cells, widths):
                start = 0 if end == 0 else c.shape[dim] - w
                pieces.append(lax.slice_in_dim(c, start, start + w, axis=dim))
            parts.append(pieces)
        def sent(pieces, pairs):
            image_part = lax.ppermute(pieces[0], axis, pairs)
            flat = jnp.concatenate([pieces[1].reshape(-1), pieces[2].reshape(-1)])
            flat = lax.ppermute(flat, axis, pairs)
            size = pieces[1].size
            return [
                image_part,
                flat[:size].reshape(pieces[1].shape),
                flat[size:].reshape(pieces[2].shape),
            ]
        from_below = sent(parts[1], [(i, i + 1) for i in range(ends)])
        from_above = sent(parts[0], [(i + 1, i) for i in range(ends)])
        cells = [
            jnp.concatenate([below, c, above], axis=dim)
            for below, c, above in zip(from_below, cells, from_above)
        ]
    return cells


def region_step(lvl, edge, rate, code):
    centre = lvl[1:-1, 1:-1]
    shifted = (
        lvl[:-2, 1:-1],
        lvl[2:, 1:-1],
        lvl[1:-1, :-2],
        lvl[1:-1, 2:],
        jnp.concatenate([centre[:, :, :1], centre[:, :, :-1]], axis=2),
        jnp.concatenate([centre[:, :, 1:], centre[:, :, -1:]], axis=2),
    )
    minus_x, plus_x, minus_y, plus_y, minus_z, plus_z = (
        jnp.where((code >> side) & 1 == 1, value, centre) for side, value in enumerate(shifted)
    )
    laplace = plus_x + minus_x + (plus_y + minus_y) + (plus_z + minus_z) - 6.0 * centre
    diff_x = (plus_x - minus_x) * 0.5
    diff_y = (plus_y - minus_y) * 0.5
    diff_z = (plus_z - minus_z) * 0.5
    gradient = diff_x * diff_x + diff_y * diff_y + diff_z * diff_z
    force = smoothing * laplace + rate
    return centre + time_step * edge * force * jnp.sqrt(1.0 + gradient)


def per_device(em_image, level_set, speeds, brick_of_band, neighbours, speed_index):
    partners = lax.axis_size("dev")
    bricks_here = BXN * BYN * BZN
    choose = speed_index[:, None] == jnp.arange(speeds.shape[0])[None, :]
    rates_here = jnp.sum(jnp.where(choose, speeds[None, :], 0.0), axis=1)
    info = jnp.concatenate(
        [(neighbours >= 0).astype(jnp.float32), rates_here[:, None]], axis=1
    ).reshape(BXN, BYN, BZN, 7)
    margin, wide_level, wide_info = extended_packed(em_image, level_set, info)
    window = jnp.pad(margin.astype(jnp.float32), ((0, 0), (0, 0), (3, 3)))
    edge = edge_map(window)
    span_x, span_y, span_z = wide_level.shape
    lead = BX - STEPS
    weights = jnp.asarray([1 << side for side in range(6)] + [0], jnp.int32)
    brick_code = jnp.sum(jnp.where(wide_info > 0.5, weights, 0), axis=-1)
    def spread(per_brick):
        table = jnp.broadcast_to(
            per_brick.reshape(BXN + 2, 1, BYN + 2, 1, BZN), (BXN + 2, BX, BYN + 2, BY, BZN)
        ).reshape((BXN + 2) * BX, (BYN + 2) * BY, BZN)
        table = table[lead : lead + span_x, lead : lead + span_y]
        zi = lax.broadcasted_iota(jnp.int32, wide_level.shape, 2)
        value = table[:, :, BZN - 1][..., None]
        for bz in range(BZN - 2, -1, -1):
            value = jnp.where(zi < (bz + 1) * BZ, table[:, :, bz][..., None], value)
        return value
    rate = spread(wide_info[..., 6])
    place = (
        lax.broadcasted_iota(jnp.int32, wide_level.shape, 0) + lead,
        lax.broadcasted_iota(jnp.int32, wide_level.shape, 1) + lead,
        lax.broadcasted_iota(jnp.int32, wide_level.shape, 2),
    )
    sizes = (BX, BX, BY, BY, BZ, BZ)
    code = spread(brick_code)
    for side in range(6):
        pos = place[side // 2] % sizes[side]
        inner = pos != (0 if side % 2 == 0 else sizes[side] - 1)
        code = code | (inner.astype(jnp.int32) << side)
    lvl = wide_level
    for repeat in range(STEPS):
        lo = repeat + 1
        hi_x = span_x - repeat - 1
        hi_y = span_y - repeat - 1
        lvl = region_step(lvl, edge[lo:hi_x, lo:hi_y], rate[lo:hi_x, lo:hi_y], code[lo:hi_x, lo:hi_y])
    band_here = brick_of_band.shape[0]
    lower = jnp.concatenate([neighbours[1:, 4], neighbours[:1, 4]])
    upper = jnp.concatenate([neighbours[-1:, 5], neighbours[:-1, 5]])
    first_in_z = jnp.arange(bricks_here, dtype=jnp.int32) % BZN == 0
    band_of = jnp.where(first_in_z, lower, upper)
    in_band = band_of >= 0
    owner_dev = band_of // band_here % partners
    source_dev = brick_of_band // bricks_here % partners
    matches = (owner_dev[None, :] == jnp.arange(partners)[:, None]) & in_band[None, :]
    chosen = jnp.sum(jnp.where(matches, jnp.arange(bricks_here)[None, :], 0), axis=1)
    corner_x = chosen // (BYN * BZN) * BX
    corner_y = chosen // BZN % BYN * BY
    corner_z = chosen % BZN * BZ
    sending = jax.vmap(
        lambda cx, cy, cz: lax.dynamic_slice(lvl, (cx, cy, cz), (BX, BY, BZ))
    )(corner_x, corner_y, corner_z)
    arrived = lax.all_to_all(sending, "dev", split_axis=0, concat_axis=0, tiled=True)
    return arrived.at[source_dev].get(mode="promise_in_bounds")


def solution(mesh):
    placed = (
        P("group", "dev", None),
        P("group", "dev", None),
        P(),
        P(("group", "dev")),
        P(("group", "dev"), None),
        P(("group", "dev")),
    )
    return jax.shard_map(
        per_device,
        mesh=mesh,
        in_specs=placed,
        out_specs=P(("group", "dev"), None, None, None),
        check_vma=False,
    )
```

```python
import math

import jax
import jax.numpy as jnp
from jax import lax
from jax.sharding import PartitionSpec as P

BX = 16
BY = 16
BZ = 128
BXN = 2
BYN = 2
BZN = 4
STEPS = 4


gauss_raw = [math.exp(-0.5 * position * position) for position in range(-2, 3)]
gauss_taps = [weight / sum(gauss_raw) for weight in gauss_raw]
time_step = 0.2
smoothing = 0.15
contrast = 0.02


def shortened(value):
    return jax.tree.map(lambda a: a.astype(jnp.bfloat16) if a.dtype == jnp.float32 else a, value)


def extended(cells, sides, width):
    for axis, dim in sides:
        count = lax.axis_size(axis)
        ends = count - 1
        head = lax.slice_in_dim(cells, 0, width, axis=dim)
        tail = lax.slice_in_dim(cells, cells.shape[dim] - width, cells.shape[dim], axis=dim)
        cells = jnp.concatenate(
            [
                lax.ppermute(tail, axis, [(i, (i + 1) % count) for i in range(ends)]),
                cells,
                lax.ppermute(head, axis, [((i + 1) % count, i) for i in range(ends)]),
            ],
            axis=dim,
        )
    return cells


def smooth_axis(values, along):
    length = values.shape[along] - 4
    summed = gauss_taps[0] * lax.slice_in_dim(values, 0, length, axis=along)
    for offset in range(1, 5):
        summed = summed + gauss_taps[offset] * lax.slice_in_dim(
            values, offset, offset + length, axis=along
        )
    return summed


def edge_map(window):
    smoothed = smooth_axis(smooth_axis(smooth_axis(window, 0), 1), 2)
    grad_x = (smoothed[2:, 1:-1, 1:-1] - smoothed[:-2, 1:-1, 1:-1]) * 0.5
    grad_y = (smoothed[1:-1, 2:, 1:-1] - smoothed[1:-1, :-2, 1:-1]) * 0.5
    grad_z = (smoothed[1:-1, 1:-1, 2:] - smoothed[1:-1, 1:-1, :-2]) * 0.5
    return 1.0 / (1.0 + (grad_x * grad_x + grad_y * grad_y + grad_z * grad_z) / contrast)


def to_bricks(block):
    shaped = block.reshape(BXN, BX, BYN, BY, BZN, BZ)
    return shaped.transpose(0, 2, 4, 1, 3, 5).reshape(BXN * BYN * BZN, BX, BY, BZ)


def own_faces(levels):
    side_faces = jnp.stack([levels[:, 0], levels[:, -1], levels[:, :, 0], levels[:, :, -1]], axis=1)
    end_faces = jnp.stack([levels[:, :, :, 0], levels[:, :, :, -1]], axis=1)
    return (side_faces, end_faces)


def advance(levels, side_ghost, end_ghost, edge_maps, speed_rows):
    with_z = jnp.concatenate(
        [end_ghost[:, 0][..., None], levels, end_ghost[:, 1][..., None]], axis=3
    )
    y_faces = jnp.pad(side_ghost[:, 2:4], ((0, 0), (0, 0), (0, 0), (1, 1)))
    with_y = jnp.concatenate(
        [y_faces[:, 0][:, :, None, :], with_z, y_faces[:, 1][:, :, None, :]], axis=2
    )
    x_faces = jnp.pad(side_ghost[:, 0:2], ((0, 0), (0, 0), (1, 1), (1, 1)))
    padded = jnp.concatenate([x_faces[:, 0][:, None], with_y, x_faces[:, 1][:, None]], axis=1)
    centre = padded[:, 1:-1, 1:-1, 1:-1]
    minus_x = padded[:, :-2, 1:-1, 1:-1]
    plus_x = padded[:, 2:, 1:-1, 1:-1]
    minus_y = padded[:, 1:-1, :-2, 1:-1]
    plus_y = padded[:, 1:-1, 2:, 1:-1]
    minus_z = padded[:, 1:-1, 1:-1, :-2]
    plus_z = padded[:, 1:-1, 1:-1, 2:]
    laplace = plus_x + minus_x + (plus_y + minus_y) + (plus_z + minus_z) - 6.0 * centre
    diff_x = (plus_x - minus_x) * 0.5
    diff_y = (plus_y - minus_y) * 0.5
    diff_z = (plus_z - minus_z) * 0.5
    gradient = diff_x * diff_x + diff_y * diff_y + diff_z * diff_z
    force = smoothing * laplace + speed_rows[:, None, None, None]
    return centre + time_step * edge_maps * force * jnp.sqrt(1.0 + gradient)


def assemble_ghosts(side_faces, end_faces, beside_lists):
    face_grid = side_faces.reshape((BXN, BYN, BZN) + side_faces.shape[1:])
    widened = extended(shortened(face_grid), (("group", 0), ("dev", 1)), 1).astype(face_grid.dtype)
    from_side = jnp.stack(
        [
            widened[:-2, 1:-1, :, 1],
            widened[2:, 1:-1, :, 0],
            widened[1:-1, :-2, :, 3],
            widened[1:-1, 2:, :, 2],
        ],
        axis=3,
    ).reshape(side_faces.shape)
    end_grid = end_faces.reshape((BXN, BYN, BZN) + end_faces.shape[1:])
    zero_faces = jnp.zeros_like(end_grid[:, :, :1, 0])
    lower_ghost = jnp.concatenate([zero_faces, end_grid[:, :, :-1, 1]], axis=2)
    upper_ghost = jnp.concatenate([end_grid[:, :, 1:, 0], zero_faces], axis=2)
    from_ends = jnp.stack([lower_ghost, upper_ghost], axis=3).reshape(end_faces.shape)
    linked = beside_lists >= 0
    side_ghost = jnp.where(linked[:, :4, None, None], from_side, side_faces)
    end_ghost = jnp.where(linked[:, 4:, None, None], from_ends, end_faces)
    return (side_ghost, end_ghost)


def place_rows(values, target, usable, partners):
    items = values.shape[0]
    matches = (target[None, :] == jnp.arange(partners)[:, None]) & usable[None, :]
    chosen = jnp.sum(jnp.where(matches, jnp.arange(items)[None, :], 0), axis=1)
    present = jnp.any(matches, axis=1)
    picked = jnp.take(values, chosen, axis=0)
    return jnp.where(
        present.reshape((partners,) + (1,) * (values.ndim - 1)), picked, jnp.zeros((), values.dtype)
    )


def extended_many(items, sides):
    cells = [value for value, width in items]
    widths = [width for value, width in items]
    for axis, dim in sides:
        count = lax.axis_size(axis)
        ends = count - 1
        heads = tuple(lax.slice_in_dim(c, 0, w, axis=dim) for c, w in zip(cells, widths))
        tails = tuple(
            lax.slice_in_dim(c, c.shape[dim] - w, c.shape[dim], axis=dim) for c, w in zip(cells, widths)
        )
        from_below = lax.ppermute(tails, axis, [(i, (i + 1) % count) for i in range(ends)])
        from_above = lax.ppermute(heads, axis, [((i + 1) % count, i) for i in range(ends)])
        cells = [
            jnp.concatenate([below, c, above], axis=dim)
            for below, c, above in zip(from_below, cells, from_above)
        ]
    return cells


def extended_packed(em_image, level_set, info):
    cells = [em_image, level_set, info]
    widths = [3 + STEPS, STEPS, 1]
    for axis, dim in (("group", 0), ("dev", 1)):
        count = lax.axis_size(axis)
        ends = count - 1
        parts = []
        for end in (0, 1):
            pieces = []
            for c, w in zip(cells, widths):
                start = 0 if end == 0 else c.shape[dim] - w
                pieces.append(lax.slice_in_dim(c, start, start + w, axis=dim))
            parts.append(pieces)
        def sent(pieces, pairs):
            image_part = lax.ppermute(pieces[0], axis, pairs)
            flat = jnp.concatenate([pieces[1].reshape(-1), pieces[2].reshape(-1)])
            flat = lax.ppermute(flat, axis, pairs)
            size = pieces[1].size
            return [
                image_part,
                flat[:size].reshape(pieces[1].shape),
                flat[size:].reshape(pieces[2].shape),
            ]
        from_below = sent(parts[1], [(i, i + 1) for i in range(ends)])
        from_above = sent(parts[0], [(i + 1, i) for i in range(ends)])
        cells = [
            jnp.concatenate([below, c, above], axis=dim)
            for below, c, above in zip(from_below, cells, from_above)
        ]
    return cells


def region_step(lvl, edge, rate, code):
    centre = lvl[1:-1, 1:-1, 1:-1]
    shifted = (
        lvl[:-2, 1:-1, 1:-1],
        lvl[2:, 1:-1, 1:-1],
        lvl[1:-1, :-2, 1:-1],
        lvl[1:-1, 2:, 1:-1],
        lvl[1:-1, 1:-1, :-2],
        lvl[1:-1, 1:-1, 2:],
    )
    minus_x, plus_x, minus_y, plus_y, minus_z, plus_z = (
        jnp.where((code >> side) & 1 == 1, value, centre) for side, value in enumerate(shifted)
    )
    laplace = plus_x + minus_x + (plus_y + minus_y) + (plus_z + minus_z) - 6.0 * centre
    diff_x = (plus_x - minus_x) * 0.5
    diff_y = (plus_y - minus_y) * 0.5
    diff_z = (plus_z - minus_z) * 0.5
    gradient = diff_x * diff_x + diff_y * diff_y + diff_z * diff_z
    force = smoothing * laplace + rate
    updated = centre + time_step * edge * force * jnp.sqrt(1.0 + gradient)
    return jnp.pad(updated, ((0, 0), (0, 0), (1, 1)))


def per_device(em_image, level_set, speeds, brick_of_band, neighbours, speed_index):
    partners = lax.axis_size("dev")
    bricks_here = BXN * BYN * BZN
    choose = speed_index[:, None] == jnp.arange(speeds.shape[0])[None, :]
    rates_here = jnp.sum(jnp.where(choose, speeds[None, :], 0.0), axis=1)
    info = jnp.concatenate(
        [(neighbours >= 0).astype(jnp.float32), rates_here[:, None]], axis=1
    ).reshape(BXN, BYN, BZN, 7)
    margin, wide_level, wide_info = extended_packed(em_image, level_set, info)
    window = jnp.pad(margin.astype(jnp.float32), ((0, 0), (0, 0), (3, 3)))
    edge = edge_map(window)
    span_x, span_y, span_z = wide_level.shape
    lead = BX - STEPS
    weights = jnp.asarray([1 << side for side in range(6)] + [0], jnp.int32)
    brick_code = jnp.sum(jnp.where(wide_info > 0.5, weights, 0), axis=-1)
    def spread(per_brick):
        table = jnp.broadcast_to(
            per_brick.reshape(BXN + 2, 1, BYN + 2, 1, BZN), (BXN + 2, BX, BYN + 2, BY, BZN)
        ).reshape((BXN + 2) * BX, (BYN + 2) * BY, BZN)
        table = table[lead : lead + span_x, lead : lead + span_y]
        zi = lax.broadcasted_iota(jnp.int32, wide_level.shape, 2)
        value = table[:, :, BZN - 1][..., None]
        for bz in range(BZN - 2, -1, -1):
            value = jnp.where(zi < (bz + 1) * BZ, table[:, :, bz][..., None], value)
        return value
    rate = spread(wide_info[..., 6])
    place = (
        lax.broadcasted_iota(jnp.int32, wide_level.shape, 0) + lead,
        lax.broadcasted_iota(jnp.int32, wide_level.shape, 1) + lead,
        lax.broadcasted_iota(jnp.int32, wide_level.shape, 2),
    )
    sizes = (BX, BX, BY, BY, BZ, BZ)
    code = spread(brick_code)
    for side in range(6):
        pos = place[side // 2] % sizes[side]
        inner = pos != (0 if side % 2 == 0 else sizes[side] - 1)
        code = code | (inner.astype(jnp.int32) << side)
    lvl = jnp.pad(wide_level, ((0, 0), (0, 0), (1, 1)))
    for repeat in range(STEPS):
        lo = repeat + 1
        hi_x = span_x - repeat - 1
        hi_y = span_y - repeat - 1
        lvl = region_step(lvl, edge[lo:hi_x, lo:hi_y], rate[lo:hi_x, lo:hi_y], code[lo:hi_x, lo:hi_y])
    band_here = brick_of_band.shape[0]
    lower = jnp.concatenate([neighbours[1:, 4], neighbours[:1, 4]])
    upper = jnp.concatenate([neighbours[-1:, 5], neighbours[:-1, 5]])
    first_in_z = jnp.arange(bricks_here, dtype=jnp.int32) % BZN == 0
    band_of = jnp.where(first_in_z, lower, upper)
    in_band = band_of >= 0
    owner_dev = band_of // band_here % partners
    source_dev = brick_of_band // bricks_here % partners
    matches = (owner_dev[None, :] == jnp.arange(partners)[:, None]) & in_band[None, :]
    chosen = jnp.sum(jnp.where(matches, jnp.arange(bricks_here)[None, :], 0), axis=1)
    lvl = lvl[:, :, 1:-1]
    view = lvl.reshape(BXN, BX, BYN, BY, BZN, BZ)
    sending = view.at[chosen // (BYN * BZN), :, chosen // BZN % BYN, :, chosen % BZN, :].get(
        mode="promise_in_bounds"
    )
    arrived = lax.all_to_all(sending, "dev", split_axis=0, concat_axis=0, tiled=True)
    return arrived.at[source_dev].get(mode="promise_in_bounds")


def solution(mesh):
    placed = (
        P("group", "dev", None),
        P("group", "dev", None),
        P(),
        P(("group", "dev")),
        P(("group", "dev"), None),
        P(("group", "dev")),
    )
    return jax.shard_map(
        per_device,
        mesh=mesh,
        in_specs=placed,
        out_specs=P(("group", "dev"), None, None, None),
        check_vma=False,
    )
```

```python
import math

import jax
import jax.numpy as jnp
from jax import lax
from jax.sharding import PartitionSpec as P

BX = 16
BY = 16
BZ = 128
BXN = 2
BYN = 2
BZN = 4
STEPS = 4


gauss_raw = [math.exp(-0.5 * position * position) for position in range(-2, 3)]
gauss_taps = [weight / sum(gauss_raw) for weight in gauss_raw]
time_step = 0.2
smoothing = 0.15
contrast = 0.02


def shortened(value):
    return jax.tree.map(lambda a: a.astype(jnp.bfloat16) if a.dtype == jnp.float32 else a, value)


def extended(cells, sides, width):
    for axis, dim in sides:
        count = lax.axis_size(axis)
        ends = count - 1
        head = lax.slice_in_dim(cells, 0, width, axis=dim)
        tail = lax.slice_in_dim(cells, cells.shape[dim] - width, cells.shape[dim], axis=dim)
        cells = jnp.concatenate(
            [
                lax.ppermute(tail, axis, [(i, (i + 1) % count) for i in range(ends)]),
                cells,
                lax.ppermute(head, axis, [((i + 1) % count, i) for i in range(ends)]),
            ],
            axis=dim,
        )
    return cells


def smooth_axis(values, along):
    length = values.shape[along] - 4
    summed = gauss_taps[0] * lax.slice_in_dim(values, 0, length, axis=along)
    for offset in range(1, 5):
        summed = summed + gauss_taps[offset] * lax.slice_in_dim(
            values, offset, offset + length, axis=along
        )
    return summed


def edge_map(window):
    smoothed = smooth_axis(smooth_axis(smooth_axis(window, 0), 1), 2)
    grad_x = (smoothed[2:, 1:-1, 1:-1] - smoothed[:-2, 1:-1, 1:-1]) * 0.5
    grad_y = (smoothed[1:-1, 2:, 1:-1] - smoothed[1:-1, :-2, 1:-1]) * 0.5
    grad_z = (smoothed[1:-1, 1:-1, 2:] - smoothed[1:-1, 1:-1, :-2]) * 0.5
    return 1.0 / (1.0 + (grad_x * grad_x + grad_y * grad_y + grad_z * grad_z) / contrast)


def to_bricks(block):
    shaped = block.reshape(BXN, BX, BYN, BY, BZN, BZ)
    return shaped.transpose(0, 2, 4, 1, 3, 5).reshape(BXN * BYN * BZN, BX, BY, BZ)


def own_faces(levels):
    side_faces = jnp.stack([levels[:, 0], levels[:, -1], levels[:, :, 0], levels[:, :, -1]], axis=1)
    end_faces = jnp.stack([levels[:, :, :, 0], levels[:, :, :, -1]], axis=1)
    return (side_faces, end_faces)


def advance(levels, side_ghost, end_ghost, edge_maps, speed_rows):
    with_z = jnp.concatenate(
        [end_ghost[:, 0][..., None], levels, end_ghost[:, 1][..., None]], axis=3
    )
    y_faces = jnp.pad(side_ghost[:, 2:4], ((0, 0), (0, 0), (0, 0), (1, 1)))
    with_y = jnp.concatenate(
        [y_faces[:, 0][:, :, None, :], with_z, y_faces[:, 1][:, :, None, :]], axis=2
    )
    x_faces = jnp.pad(side_ghost[:, 0:2], ((0, 0), (0, 0), (1, 1), (1, 1)))
    padded = jnp.concatenate([x_faces[:, 0][:, None], with_y, x_faces[:, 1][:, None]], axis=1)
    centre = padded[:, 1:-1, 1:-1, 1:-1]
    minus_x = padded[:, :-2, 1:-1, 1:-1]
    plus_x = padded[:, 2:, 1:-1, 1:-1]
    minus_y = padded[:, 1:-1, :-2, 1:-1]
    plus_y = padded[:, 1:-1, 2:, 1:-1]
    minus_z = padded[:, 1:-1, 1:-1, :-2]
    plus_z = padded[:, 1:-1, 1:-1, 2:]
    laplace = plus_x + minus_x + (plus_y + minus_y) + (plus_z + minus_z) - 6.0 * centre
    diff_x = (plus_x - minus_x) * 0.5
    diff_y = (plus_y - minus_y) * 0.5
    diff_z = (plus_z - minus_z) * 0.5
    gradient = diff_x * diff_x + diff_y * diff_y + diff_z * diff_z
    force = smoothing * laplace + speed_rows[:, None, None, None]
    return centre + time_step * edge_maps * force * jnp.sqrt(1.0 + gradient)


def assemble_ghosts(side_faces, end_faces, beside_lists):
    face_grid = side_faces.reshape((BXN, BYN, BZN) + side_faces.shape[1:])
    widened = extended(shortened(face_grid), (("group", 0), ("dev", 1)), 1).astype(face_grid.dtype)
    from_side = jnp.stack(
        [
            widened[:-2, 1:-1, :, 1],
            widened[2:, 1:-1, :, 0],
            widened[1:-1, :-2, :, 3],
            widened[1:-1, 2:, :, 2],
        ],
        axis=3,
    ).reshape(side_faces.shape)
    end_grid = end_faces.reshape((BXN, BYN, BZN) + end_faces.shape[1:])
    zero_faces = jnp.zeros_like(end_grid[:, :, :1, 0])
    lower_ghost = jnp.concatenate([zero_faces, end_grid[:, :, :-1, 1]], axis=2)
    upper_ghost = jnp.concatenate([end_grid[:, :, 1:, 0], zero_faces], axis=2)
    from_ends = jnp.stack([lower_ghost, upper_ghost], axis=3).reshape(end_faces.shape)
    linked = beside_lists >= 0
    side_ghost = jnp.where(linked[:, :4, None, None], from_side, side_faces)
    end_ghost = jnp.where(linked[:, 4:, None, None], from_ends, end_faces)
    return (side_ghost, end_ghost)


def place_rows(values, target, usable, partners):
    items = values.shape[0]
    matches = (target[None, :] == jnp.arange(partners)[:, None]) & usable[None, :]
    chosen = jnp.sum(jnp.where(matches, jnp.arange(items)[None, :], 0), axis=1)
    present = jnp.any(matches, axis=1)
    picked = jnp.take(values, chosen, axis=0)
    return jnp.where(
        present.reshape((partners,) + (1,) * (values.ndim - 1)), picked, jnp.zeros((), values.dtype)
    )


def extended_many(items, sides):
    cells = [value for value, width in items]
    widths = [width for value, width in items]
    for axis, dim in sides:
        count = lax.axis_size(axis)
        ends = count - 1
        heads = tuple(lax.slice_in_dim(c, 0, w, axis=dim) for c, w in zip(cells, widths))
        tails = tuple(
            lax.slice_in_dim(c, c.shape[dim] - w, c.shape[dim], axis=dim) for c, w in zip(cells, widths)
        )
        from_below = lax.ppermute(tails, axis, [(i, (i + 1) % count) for i in range(ends)])
        from_above = lax.ppermute(heads, axis, [((i + 1) % count, i) for i in range(ends)])
        cells = [
            jnp.concatenate([below, c, above], axis=dim)
            for below, c, above in zip(from_below, cells, from_above)
        ]
    return cells


def extended_packed(em_image, level_set, info):
    cells = [em_image, level_set, info]
    widths = [3 + STEPS, STEPS, 1]
    for axis, dim in (("group", 0), ("dev", 1)):
        count = lax.axis_size(axis)
        ends = count - 1
        parts = []
        for end in (0, 1):
            pieces = []
            for c, w in zip(cells, widths):
                start = 0 if end == 0 else c.shape[dim] - w
                pieces.append(lax.slice_in_dim(c, start, start + w, axis=dim))
            parts.append(pieces)
        def sent(pieces, pairs):
            image_part = lax.ppermute(pieces[0], axis, pairs)
            flat = jnp.concatenate([pieces[1].reshape(-1), pieces[2].reshape(-1)])
            flat = lax.ppermute(flat, axis, pairs)
            size = pieces[1].size
            return [
                image_part,
                flat[:size].reshape(pieces[1].shape),
                flat[size:].reshape(pieces[2].shape),
            ]
        from_below = sent(parts[1], [(i, i + 1) for i in range(ends)])
        from_above = sent(parts[0], [(i + 1, i) for i in range(ends)])
        cells = [
            jnp.concatenate([below, c, above], axis=dim)
            for below, c, above in zip(from_below, cells, from_above)
        ]
    return cells


def region_step(lvl, edge, rate, code):
    centre = lvl[1:-1, 1:-1, 1:-1]
    shifted = (
        lvl[:-2, 1:-1, 1:-1],
        lvl[2:, 1:-1, 1:-1],
        lvl[1:-1, :-2, 1:-1],
        lvl[1:-1, 2:, 1:-1],
        lvl[1:-1, 1:-1, :-2],
        lvl[1:-1, 1:-1, 2:],
    )
    minus_x, plus_x, minus_y, plus_y, minus_z, plus_z = (
        jnp.where((code >> side) & 1 == 1, value, centre) for side, value in enumerate(shifted)
    )
    laplace = plus_x + minus_x + (plus_y + minus_y) + (plus_z + minus_z) - 6.0 * centre
    diff_x = (plus_x - minus_x) * 0.5
    diff_y = (plus_y - minus_y) * 0.5
    diff_z = (plus_z - minus_z) * 0.5
    gradient = diff_x * diff_x + diff_y * diff_y + diff_z * diff_z
    force = smoothing * laplace + rate
    updated = centre + time_step * edge * force * jnp.sqrt(1.0 + gradient)
    return jnp.pad(updated, ((0, 0), (0, 0), (1, 1)))


def per_device(em_image, level_set, speeds, brick_of_band, neighbours, speed_index):
    partners = lax.axis_size("dev")
    bricks_here = BXN * BYN * BZN
    choose = speed_index[:, None] == jnp.arange(speeds.shape[0])[None, :]
    rates_here = jnp.sum(jnp.where(choose, speeds[None, :], 0.0), axis=1)
    info = jnp.concatenate(
        [(neighbours >= 0).astype(jnp.float32), rates_here[:, None]], axis=1
    ).reshape(BXN, BYN, BZN, 7)
    margin, wide_level, wide_info = extended_packed(em_image, level_set, info)
    window = jnp.pad(margin.astype(jnp.float32), ((0, 0), (0, 0), (3, 3)))
    edge = edge_map(window)
    span_x, span_y, span_z = wide_level.shape
    lead = BX - STEPS
    weights = jnp.asarray([1 << side for side in range(6)] + [0], jnp.int32)
    brick_code = jnp.sum(jnp.where(wide_info > 0.5, weights, 0), axis=-1)
    def spread(per_brick):
        xe = lax.broadcasted_iota(jnp.int32, (span_x, BYN + 2, BZN), 0) + lead
        along_x = per_brick[BXN + 1][None]
        for bx in range(BXN, -1, -1):
            along_x = jnp.where(xe < (bx + 1) * BX, per_brick[bx][None], along_x)
        ye = lax.broadcasted_iota(jnp.int32, (span_x, span_y, BZN), 1) + lead
        table = along_x[:, BYN + 1][:, None]
        for by in range(BYN, -1, -1):
            table = jnp.where(ye < (by + 1) * BY, along_x[:, by][:, None], table)
        zi = lax.broadcasted_iota(jnp.int32, wide_level.shape, 2)
        value = table[:, :, BZN - 1][..., None]
        for bz in range(BZN - 2, -1, -1):
            value = jnp.where(zi < (bz + 1) * BZ, table[:, :, bz][..., None], value)
        return value
    rate = spread(wide_info[..., 6])
    place = (
        lax.broadcasted_iota(jnp.int32, wide_level.shape, 0) + lead,
        lax.broadcasted_iota(jnp.int32, wide_level.shape, 1) + lead,
        lax.broadcasted_iota(jnp.int32, wide_level.shape, 2),
    )
    sizes = (BX, BX, BY, BY, BZ, BZ)
    code = spread(brick_code)
    for side in range(6):
        pos = place[side // 2] % sizes[side]
        inner = pos != (0 if side % 2 == 0 else sizes[side] - 1)
        code = code | (inner.astype(jnp.int32) << side)
    lvl = jnp.pad(wide_level, ((0, 0), (0, 0), (1, 1)))
    for repeat in range(STEPS):
        lo = repeat + 1
        hi_x = span_x - repeat - 1
        hi_y = span_y - repeat - 1
        lvl = region_step(lvl, edge[lo:hi_x, lo:hi_y], rate[lo:hi_x, lo:hi_y], code[lo:hi_x, lo:hi_y])
    band_here = brick_of_band.shape[0]
    lower = jnp.concatenate([neighbours[1:, 4], neighbours[:1, 4]])
    upper = jnp.concatenate([neighbours[-1:, 5], neighbours[:-1, 5]])
    first_in_z = jnp.arange(bricks_here, dtype=jnp.int32) % BZN == 0
    band_of = jnp.where(first_in_z, lower, upper)
    in_band = band_of >= 0
    owner_dev = band_of // band_here % partners
    source_dev = brick_of_band // bricks_here % partners
    matches = (owner_dev[None, :] == jnp.arange(partners)[:, None]) & in_band[None, :]
    chosen = jnp.sum(jnp.where(matches, jnp.arange(bricks_here)[None, :], 0), axis=1)
    lvl = lvl[:, :, 1:-1]
    view = lvl.reshape(BXN, BX, BYN, BY, BZN, BZ)
    sending = view.at[chosen // (BYN * BZN), :, chosen // BZN % BYN, :, chosen % BZN, :].get(
        mode="promise_in_bounds"
    )
    arrived = lax.all_to_all(sending, "dev", split_axis=0, concat_axis=0, tiled=True)
    return arrived.at[source_dev].get(mode="promise_in_bounds")


def solution(mesh):
    placed = (
        P("group", "dev", None),
        P("group", "dev", None),
        P(),
        P(("group", "dev")),
        P(("group", "dev"), None),
        P(("group", "dev")),
    )
    return jax.shard_map(
        per_device,
        mesh=mesh,
        in_specs=placed,
        out_specs=P(("group", "dev"), None, None, None),
        check_vma=False,
    )
```

```python
import math

import jax
import jax.numpy as jnp
from jax import lax
from jax.sharding import PartitionSpec as P

BX = 16
BY = 16
BZ = 128
BXN = 2
BYN = 2
BZN = 4
STEPS = 4


gauss_raw = [math.exp(-0.5 * position * position) for position in range(-2, 3)]
gauss_taps = [weight / sum(gauss_raw) for weight in gauss_raw]
time_step = 0.2
smoothing = 0.15
contrast = 0.02


def shortened(value):
    return jax.tree.map(lambda a: a.astype(jnp.bfloat16) if a.dtype == jnp.float32 else a, value)


def extended(cells, sides, width):
    for axis, dim in sides:
        count = lax.axis_size(axis)
        ends = count - 1
        head = lax.slice_in_dim(cells, 0, width, axis=dim)
        tail = lax.slice_in_dim(cells, cells.shape[dim] - width, cells.shape[dim], axis=dim)
        cells = jnp.concatenate(
            [
                lax.ppermute(tail, axis, [(i, (i + 1) % count) for i in range(ends)]),
                cells,
                lax.ppermute(head, axis, [((i + 1) % count, i) for i in range(ends)]),
            ],
            axis=dim,
        )
    return cells


def smooth_axis(values, along):
    length = values.shape[along] - 4
    summed = gauss_taps[0] * lax.slice_in_dim(values, 0, length, axis=along)
    for offset in range(1, 5):
        summed = summed + gauss_taps[offset] * lax.slice_in_dim(
            values, offset, offset + length, axis=along
        )
    return summed


def edge_map(window):
    smoothed = smooth_axis(smooth_axis(smooth_axis(window, 0), 1), 2)
    grad_x = (smoothed[2:, 1:-1, 1:-1] - smoothed[:-2, 1:-1, 1:-1]) * 0.5
    grad_y = (smoothed[1:-1, 2:, 1:-1] - smoothed[1:-1, :-2, 1:-1]) * 0.5
    grad_z = (smoothed[1:-1, 1:-1, 2:] - smoothed[1:-1, 1:-1, :-2]) * 0.5
    return 1.0 / (1.0 + (grad_x * grad_x + grad_y * grad_y + grad_z * grad_z) / contrast)


def to_bricks(block):
    shaped = block.reshape(BXN, BX, BYN, BY, BZN, BZ)
    return shaped.transpose(0, 2, 4, 1, 3, 5).reshape(BXN * BYN * BZN, BX, BY, BZ)


def own_faces(levels):
    side_faces = jnp.stack([levels[:, 0], levels[:, -1], levels[:, :, 0], levels[:, :, -1]], axis=1)
    end_faces = jnp.stack([levels[:, :, :, 0], levels[:, :, :, -1]], axis=1)
    return (side_faces, end_faces)


def advance(levels, side_ghost, end_ghost, edge_maps, speed_rows):
    with_z = jnp.concatenate(
        [end_ghost[:, 0][..., None], levels, end_ghost[:, 1][..., None]], axis=3
    )
    y_faces = jnp.pad(side_ghost[:, 2:4], ((0, 0), (0, 0), (0, 0), (1, 1)))
    with_y = jnp.concatenate(
        [y_faces[:, 0][:, :, None, :], with_z, y_faces[:, 1][:, :, None, :]], axis=2
    )
    x_faces = jnp.pad(side_ghost[:, 0:2], ((0, 0), (0, 0), (1, 1), (1, 1)))
    padded = jnp.concatenate([x_faces[:, 0][:, None], with_y, x_faces[:, 1][:, None]], axis=1)
    centre = padded[:, 1:-1, 1:-1, 1:-1]
    minus_x = padded[:, :-2, 1:-1, 1:-1]
    plus_x = padded[:, 2:, 1:-1, 1:-1]
    minus_y = padded[:, 1:-1, :-2, 1:-1]
    plus_y = padded[:, 1:-1, 2:, 1:-1]
    minus_z = padded[:, 1:-1, 1:-1, :-2]
    plus_z = padded[:, 1:-1, 1:-1, 2:]
    laplace = plus_x + minus_x + (plus_y + minus_y) + (plus_z + minus_z) - 6.0 * centre
    diff_x = (plus_x - minus_x) * 0.5
    diff_y = (plus_y - minus_y) * 0.5
    diff_z = (plus_z - minus_z) * 0.5
    gradient = diff_x * diff_x + diff_y * diff_y + diff_z * diff_z
    force = smoothing * laplace + speed_rows[:, None, None, None]
    return centre + time_step * edge_maps * force * jnp.sqrt(1.0 + gradient)


def assemble_ghosts(side_faces, end_faces, beside_lists):
    face_grid = side_faces.reshape((BXN, BYN, BZN) + side_faces.shape[1:])
    widened = extended(shortened(face_grid), (("group", 0), ("dev", 1)), 1).astype(face_grid.dtype)
    from_side = jnp.stack(
        [
            widened[:-2, 1:-1, :, 1],
            widened[2:, 1:-1, :, 0],
            widened[1:-1, :-2, :, 3],
            widened[1:-1, 2:, :, 2],
        ],
        axis=3,
    ).reshape(side_faces.shape)
    end_grid = end_faces.reshape((BXN, BYN, BZN) + end_faces.shape[1:])
    zero_faces = jnp.zeros_like(end_grid[:, :, :1, 0])
    lower_ghost = jnp.concatenate([zero_faces, end_grid[:, :, :-1, 1]], axis=2)
    upper_ghost = jnp.concatenate([end_grid[:, :, 1:, 0], zero_faces], axis=2)
    from_ends = jnp.stack([lower_ghost, upper_ghost], axis=3).reshape(end_faces.shape)
    linked = beside_lists >= 0
    side_ghost = jnp.where(linked[:, :4, None, None], from_side, side_faces)
    end_ghost = jnp.where(linked[:, 4:, None, None], from_ends, end_faces)
    return (side_ghost, end_ghost)


def place_rows(values, target, usable, partners):
    items = values.shape[0]
    matches = (target[None, :] == jnp.arange(partners)[:, None]) & usable[None, :]
    chosen = jnp.sum(jnp.where(matches, jnp.arange(items)[None, :], 0), axis=1)
    present = jnp.any(matches, axis=1)
    picked = jnp.take(values, chosen, axis=0)
    return jnp.where(
        present.reshape((partners,) + (1,) * (values.ndim - 1)), picked, jnp.zeros((), values.dtype)
    )


def extended_many(items, sides):
    cells = [value for value, width in items]
    widths = [width for value, width in items]
    for axis, dim in sides:
        count = lax.axis_size(axis)
        ends = count - 1
        heads = tuple(lax.slice_in_dim(c, 0, w, axis=dim) for c, w in zip(cells, widths))
        tails = tuple(
            lax.slice_in_dim(c, c.shape[dim] - w, c.shape[dim], axis=dim) for c, w in zip(cells, widths)
        )
        from_below = lax.ppermute(tails, axis, [(i, (i + 1) % count) for i in range(ends)])
        from_above = lax.ppermute(heads, axis, [((i + 1) % count, i) for i in range(ends)])
        cells = [
            jnp.concatenate([below, c, above], axis=dim)
            for below, c, above in zip(from_below, cells, from_above)
        ]
    return cells


def extended_packed(em_image, level_set, info):
    cells = [em_image, level_set, info]
    widths = [3 + STEPS, STEPS, 1]
    for axis, dim in (("group", 0), ("dev", 1)):
        count = lax.axis_size(axis)
        ends = count - 1
        parts = []
        for end in (0, 1):
            pieces = []
            for c, w in zip(cells, widths):
                start = 0 if end == 0 else c.shape[dim] - w
                pieces.append(lax.slice_in_dim(c, start, start + w, axis=dim))
            parts.append(pieces)
        def sent(pieces, pairs):
            image_part = lax.ppermute(pieces[0], axis, pairs)
            flat = jnp.concatenate([pieces[1].reshape(-1), pieces[2].reshape(-1)])
            flat = lax.ppermute(flat, axis, pairs)
            size = pieces[1].size
            return [
                image_part,
                flat[:size].reshape(pieces[1].shape),
                flat[size:].reshape(pieces[2].shape),
            ]
        from_below = sent(parts[1], [(i, i + 1) for i in range(ends)])
        from_above = sent(parts[0], [(i + 1, i) for i in range(ends)])
        cells = [
            jnp.concatenate([below, c, above], axis=dim)
            for below, c, above in zip(from_below, cells, from_above)
        ]
    return cells


def region_step(lvl, edge, rate, code):
    centre = lvl[1:-1, 1:-1, 1:-1]
    shifted = (
        lvl[:-2, 1:-1, 1:-1],
        lvl[2:, 1:-1, 1:-1],
        lvl[1:-1, :-2, 1:-1],
        lvl[1:-1, 2:, 1:-1],
        lvl[1:-1, 1:-1, :-2],
        lvl[1:-1, 1:-1, 2:],
    )
    minus_x, plus_x, minus_y, plus_y, minus_z, plus_z = (
        jnp.where((code >> side) & 1 == 1, value, centre) for side, value in enumerate(shifted)
    )
    laplace = plus_x + minus_x + (plus_y + minus_y) + (plus_z + minus_z) - 6.0 * centre
    diff_x = (plus_x - minus_x) * 0.5
    diff_y = (plus_y - minus_y) * 0.5
    diff_z = (plus_z - minus_z) * 0.5
    gradient = diff_x * diff_x + diff_y * diff_y + diff_z * diff_z
    force = smoothing * laplace + rate
    updated = centre + edge * force * jnp.sqrt(1.0 + gradient)
    return jnp.pad(updated, ((0, 0), (0, 0), (1, 1)))


def per_device(em_image, level_set, speeds, brick_of_band, neighbours, speed_index):
    partners = lax.axis_size("dev")
    bricks_here = BXN * BYN * BZN
    choose = speed_index[:, None] == jnp.arange(speeds.shape[0])[None, :]
    rates_here = jnp.sum(jnp.where(choose, speeds[None, :], 0.0), axis=1)
    info = jnp.concatenate(
        [(neighbours >= 0).astype(jnp.float32), rates_here[:, None]], axis=1
    ).reshape(BXN, BYN, BZN, 7)
    margin, wide_level, wide_info = extended_packed(em_image, level_set, info)
    window = jnp.pad(margin.astype(jnp.float32), ((0, 0), (0, 0), (3, 3)))
    edge = time_step * edge_map(window)
    span_x, span_y, span_z = wide_level.shape
    lead = BX - STEPS
    weights = jnp.asarray([1 << side for side in range(6)] + [0], jnp.int32)
    brick_code = jnp.sum(jnp.where(wide_info > 0.5, weights, 0), axis=-1)
    def spread(per_brick):
        xe = lax.broadcasted_iota(jnp.int32, (span_x, BYN + 2, BZN), 0) + lead
        along_x = per_brick[BXN + 1][None]
        for bx in range(BXN, -1, -1):
            along_x = jnp.where(xe < (bx + 1) * BX, per_brick[bx][None], along_x)
        ye = lax.broadcasted_iota(jnp.int32, (span_x, span_y, BZN), 1) + lead
        table = along_x[:, BYN + 1][:, None]
        for by in range(BYN, -1, -1):
            table = jnp.where(ye < (by + 1) * BY, along_x[:, by][:, None], table)
        zi = lax.broadcasted_iota(jnp.int32, wide_level.shape, 2)
        value = table[:, :, BZN - 1][..., None]
        for bz in range(BZN - 2, -1, -1):
            value = jnp.where(zi < (bz + 1) * BZ, table[:, :, bz][..., None], value)
        return value
    rate = spread(wide_info[..., 6])
    place = (
        lax.broadcasted_iota(jnp.int32, wide_level.shape, 0) + lead,
        lax.broadcasted_iota(jnp.int32, wide_level.shape, 1) + lead,
        lax.broadcasted_iota(jnp.int32, wide_level.shape, 2),
    )
    sizes = (BX, BX, BY, BY, BZ, BZ)
    code = spread(brick_code)
    for side in range(6):
        pos = place[side // 2] % sizes[side]
        inner = pos != (0 if side % 2 == 0 else sizes[side] - 1)
        code = code | (inner.astype(jnp.int32) << side)
    lvl = jnp.pad(wide_level, ((0, 0), (0, 0), (1, 1)))
    for repeat in range(STEPS):
        lo = repeat + 1
        hi_x = span_x - repeat - 1
        hi_y = span_y - repeat - 1
        lvl = region_step(lvl, edge[lo:hi_x, lo:hi_y], rate[lo:hi_x, lo:hi_y], code[lo:hi_x, lo:hi_y])
    band_here = brick_of_band.shape[0]
    lower = jnp.concatenate([neighbours[1:, 4], neighbours[:1, 4]])
    upper = jnp.concatenate([neighbours[-1:, 5], neighbours[:-1, 5]])
    first_in_z = jnp.arange(bricks_here, dtype=jnp.int32) % BZN == 0
    band_of = jnp.where(first_in_z, lower, upper)
    in_band = band_of >= 0
    owner_dev = band_of // band_here % partners
    source_dev = brick_of_band // bricks_here % partners
    matches = (owner_dev[None, :] == jnp.arange(partners)[:, None]) & in_band[None, :]
    chosen = jnp.sum(jnp.where(matches, jnp.arange(bricks_here)[None, :], 0), axis=1)
    lvl = lvl[:, :, 1:-1]
    view = lvl.reshape(BXN, BX, BYN, BY, BZN, BZ)
    sending = view.at[chosen // (BYN * BZN), :, chosen // BZN % BYN, :, chosen % BZN, :].get(
        mode="promise_in_bounds"
    )
    arrived = lax.all_to_all(sending, "dev", split_axis=0, concat_axis=0, tiled=True)
    return arrived.at[source_dev].get(mode="promise_in_bounds")


def solution(mesh):
    placed = (
        P("group", "dev", None),
        P("group", "dev", None),
        P(),
        P(("group", "dev")),
        P(("group", "dev"), None),
        P(("group", "dev")),
    )
    return jax.shard_map(
        per_device,
        mesh=mesh,
        in_specs=placed,
        out_specs=P(("group", "dev"), None, None, None),
        check_vma=False,
    )
```

```python
import math

import jax
import jax.numpy as jnp
from jax import lax
from jax.sharding import PartitionSpec as P

BX = 16
BY = 16
BZ = 128
BXN = 2
BYN = 2
BZN = 4
STEPS = 4


gauss_raw = [math.exp(-0.5 * position * position) for position in range(-2, 3)]
gauss_taps = [weight / sum(gauss_raw) for weight in gauss_raw]
time_step = 0.2
smoothing = 0.15
contrast = 0.02


def shortened(value):
    return jax.tree.map(lambda a: a.astype(jnp.bfloat16) if a.dtype == jnp.float32 else a, value)


def extended(cells, sides, width):
    for axis, dim in sides:
        count = lax.axis_size(axis)
        ends = count - 1
        head = lax.slice_in_dim(cells, 0, width, axis=dim)
        tail = lax.slice_in_dim(cells, cells.shape[dim] - width, cells.shape[dim], axis=dim)
        cells = jnp.concatenate(
            [
                lax.ppermute(tail, axis, [(i, (i + 1) % count) for i in range(ends)]),
                cells,
                lax.ppermute(head, axis, [((i + 1) % count, i) for i in range(ends)]),
            ],
            axis=dim,
        )
    return cells


def smooth_axis(values, along):
    length = values.shape[along] - 4
    summed = gauss_taps[0] * lax.slice_in_dim(values, 0, length, axis=along)
    for offset in range(1, 5):
        summed = summed + gauss_taps[offset] * lax.slice_in_dim(
            values, offset, offset + length, axis=along
        )
    return summed


def edge_map(window):
    smoothed = smooth_axis(smooth_axis(smooth_axis(window, 0), 1), 2)
    grad_x = (smoothed[2:, 1:-1, 1:-1] - smoothed[:-2, 1:-1, 1:-1]) * 0.5
    grad_y = (smoothed[1:-1, 2:, 1:-1] - smoothed[1:-1, :-2, 1:-1]) * 0.5
    grad_z = (smoothed[1:-1, 1:-1, 2:] - smoothed[1:-1, 1:-1, :-2]) * 0.5
    return 1.0 / (1.0 + (grad_x * grad_x + grad_y * grad_y + grad_z * grad_z) / contrast)


def to_bricks(block):
    shaped = block.reshape(BXN, BX, BYN, BY, BZN, BZ)
    return shaped.transpose(0, 2, 4, 1, 3, 5).reshape(BXN * BYN * BZN, BX, BY, BZ)


def own_faces(levels):
    side_faces = jnp.stack([levels[:, 0], levels[:, -1], levels[:, :, 0], levels[:, :, -1]], axis=1)
    end_faces = jnp.stack([levels[:, :, :, 0], levels[:, :, :, -1]], axis=1)
    return (side_faces, end_faces)


def advance(levels, side_ghost, end_ghost, edge_maps, speed_rows):
    with_z = jnp.concatenate(
        [end_ghost[:, 0][..., None], levels, end_ghost[:, 1][..., None]], axis=3
    )
    y_faces = jnp.pad(side_ghost[:, 2:4], ((0, 0), (0, 0), (0, 0), (1, 1)))
    with_y = jnp.concatenate(
        [y_faces[:, 0][:, :, None, :], with_z, y_faces[:, 1][:, :, None, :]], axis=2
    )
    x_faces = jnp.pad(side_ghost[:, 0:2], ((0, 0), (0, 0), (1, 1), (1, 1)))
    padded = jnp.concatenate([x_faces[:, 0][:, None], with_y, x_faces[:, 1][:, None]], axis=1)
    centre = padded[:, 1:-1, 1:-1, 1:-1]
    minus_x = padded[:, :-2, 1:-1, 1:-1]
    plus_x = padded[:, 2:, 1:-1, 1:-1]
    minus_y = padded[:, 1:-1, :-2, 1:-1]
    plus_y = padded[:, 1:-1, 2:, 1:-1]
    minus_z = padded[:, 1:-1, 1:-1, :-2]
    plus_z = padded[:, 1:-1, 1:-1, 2:]
    laplace = plus_x + minus_x + (plus_y + minus_y) + (plus_z + minus_z) - 6.0 * centre
    diff_x = (plus_x - minus_x) * 0.5
    diff_y = (plus_y - minus_y) * 0.5
    diff_z = (plus_z - minus_z) * 0.5
    gradient = diff_x * diff_x + diff_y * diff_y + diff_z * diff_z
    force = smoothing * laplace + speed_rows[:, None, None, None]
    return centre + time_step * edge_maps * force * jnp.sqrt(1.0 + gradient)


def assemble_ghosts(side_faces, end_faces, beside_lists):
    face_grid = side_faces.reshape((BXN, BYN, BZN) + side_faces.shape[1:])
    widened = extended(shortened(face_grid), (("group", 0), ("dev", 1)), 1).astype(face_grid.dtype)
    from_side = jnp.stack(
        [
            widened[:-2, 1:-1, :, 1],
            widened[2:, 1:-1, :, 0],
            widened[1:-1, :-2, :, 3],
            widened[1:-1, 2:, :, 2],
        ],
        axis=3,
    ).reshape(side_faces.shape)
    end_grid = end_faces.reshape((BXN, BYN, BZN) + end_faces.shape[1:])
    zero_faces = jnp.zeros_like(end_grid[:, :, :1, 0])
    lower_ghost = jnp.concatenate([zero_faces, end_grid[:, :, :-1, 1]], axis=2)
    upper_ghost = jnp.concatenate([end_grid[:, :, 1:, 0], zero_faces], axis=2)
    from_ends = jnp.stack([lower_ghost, upper_ghost], axis=3).reshape(end_faces.shape)
    linked = beside_lists >= 0
    side_ghost = jnp.where(linked[:, :4, None, None], from_side, side_faces)
    end_ghost = jnp.where(linked[:, 4:, None, None], from_ends, end_faces)
    return (side_ghost, end_ghost)


def place_rows(values, target, usable, partners):
    items = values.shape[0]
    matches = (target[None, :] == jnp.arange(partners)[:, None]) & usable[None, :]
    chosen = jnp.sum(jnp.where(matches, jnp.arange(items)[None, :], 0), axis=1)
    present = jnp.any(matches, axis=1)
    picked = jnp.take(values, chosen, axis=0)
    return jnp.where(
        present.reshape((partners,) + (1,) * (values.ndim - 1)), picked, jnp.zeros((), values.dtype)
    )


def extended_many(items, sides):
    cells = [value for value, width in items]
    widths = [width for value, width in items]
    for axis, dim in sides:
        count = lax.axis_size(axis)
        ends = count - 1
        heads = tuple(lax.slice_in_dim(c, 0, w, axis=dim) for c, w in zip(cells, widths))
        tails = tuple(
            lax.slice_in_dim(c, c.shape[dim] - w, c.shape[dim], axis=dim) for c, w in zip(cells, widths)
        )
        from_below = lax.ppermute(tails, axis, [(i, (i + 1) % count) for i in range(ends)])
        from_above = lax.ppermute(heads, axis, [((i + 1) % count, i) for i in range(ends)])
        cells = [
            jnp.concatenate([below, c, above], axis=dim)
            for below, c, above in zip(from_below, cells, from_above)
        ]
    return cells


def extended_packed(em_image, level_set, info):
    cells = [em_image, level_set, info]
    widths = [2 + STEPS, STEPS, 1]
    for axis, dim in (("group", 0), ("dev", 1)):
        count = lax.axis_size(axis)
        ends = count - 1
        parts = []
        for end in (0, 1):
            pieces = []
            for c, w in zip(cells, widths):
                start = 0 if end == 0 else c.shape[dim] - w
                pieces.append(lax.slice_in_dim(c, start, start + w, axis=dim))
            parts.append(pieces)
        def sent(pieces, pairs):
            image_part = lax.ppermute(pieces[0], axis, pairs)
            flat = jnp.concatenate([pieces[1].reshape(-1), pieces[2].reshape(-1)])
            flat = lax.ppermute(flat, axis, pairs)
            size = pieces[1].size
            return [
                image_part,
                flat[:size].reshape(pieces[1].shape),
                flat[size:].reshape(pieces[2].shape),
            ]
        from_below = sent(parts[1], [(i, i + 1) for i in range(ends)])
        from_above = sent(parts[0], [(i + 1, i) for i in range(ends)])
        cells = [
            jnp.concatenate([below, c, above], axis=dim)
            for below, c, above in zip(from_below, cells, from_above)
        ]
    return cells


def region_step(lvl, edge, rate, code):
    centre = lvl[1:-1, 1:-1, 1:-1]
    shifted = (
        lvl[:-2, 1:-1, 1:-1],
        lvl[2:, 1:-1, 1:-1],
        lvl[1:-1, :-2, 1:-1],
        lvl[1:-1, 2:, 1:-1],
        lvl[1:-1, 1:-1, :-2],
        lvl[1:-1, 1:-1, 2:],
    )
    minus_x, plus_x, minus_y, plus_y, minus_z, plus_z = (
        jnp.where((code >> side) & 1 == 1, value, centre) for side, value in enumerate(shifted)
    )
    laplace = plus_x + minus_x + (plus_y + minus_y) + (plus_z + minus_z) - 6.0 * centre
    diff_x = (plus_x - minus_x) * 0.5
    diff_y = (plus_y - minus_y) * 0.5
    diff_z = (plus_z - minus_z) * 0.5
    gradient = diff_x * diff_x + diff_y * diff_y + diff_z * diff_z
    force = smoothing * laplace + rate
    updated = centre + edge * force * jnp.sqrt(1.0 + gradient)
    return jnp.pad(updated, ((0, 0), (0, 0), (1, 1)))


def per_device(em_image, level_set, speeds, brick_of_band, neighbours, speed_index):
    partners = lax.axis_size("dev")
    bricks_here = BXN * BYN * BZN
    choose = speed_index[:, None] == jnp.arange(speeds.shape[0])[None, :]
    rates_here = jnp.sum(jnp.where(choose, speeds[None, :], 0.0), axis=1)
    info = jnp.concatenate(
        [(neighbours >= 0).astype(jnp.float32), rates_here[:, None]], axis=1
    ).reshape(BXN, BYN, BZN, 7)
    margin, wide_level, wide_info = extended_packed(em_image, level_set, info)
    window = jnp.pad(margin.astype(jnp.float32), ((0, 0), (0, 0), (3, 3)))
    edge = time_step * edge_map(window)
    span_x, span_y, span_z = wide_level.shape
    lead = BX - STEPS
    weights = jnp.asarray([1 << side for side in range(6)] + [0], jnp.int32)
    brick_code = jnp.sum(jnp.where(wide_info > 0.5, weights, 0), axis=-1)
    def spread(per_brick):
        xe = lax.broadcasted_iota(jnp.int32, (span_x, BYN + 2, BZN), 0) + lead
        along_x = per_brick[BXN + 1][None]
        for bx in range(BXN, -1, -1):
            along_x = jnp.where(xe < (bx + 1) * BX, per_brick[bx][None], along_x)
        ye = lax.broadcasted_iota(jnp.int32, (span_x, span_y, BZN), 1) + lead
        table = along_x[:, BYN + 1][:, None]
        for by in range(BYN, -1, -1):
            table = jnp.where(ye < (by + 1) * BY, along_x[:, by][:, None], table)
        zi = lax.broadcasted_iota(jnp.int32, wide_level.shape, 2)
        value = table[:, :, BZN - 1][..., None]
        for bz in range(BZN - 2, -1, -1):
            value = jnp.where(zi < (bz + 1) * BZ, table[:, :, bz][..., None], value)
        return value
    rate = spread(wide_info[..., 6])
    place = (
        lax.broadcasted_iota(jnp.int32, wide_level.shape, 0) + lead,
        lax.broadcasted_iota(jnp.int32, wide_level.shape, 1) + lead,
        lax.broadcasted_iota(jnp.int32, wide_level.shape, 2),
    )
    sizes = (BX, BX, BY, BY, BZ, BZ)
    code = spread(brick_code)
    for side in range(6):
        pos = place[side // 2] % sizes[side]
        inner = pos != (0 if side % 2 == 0 else sizes[side] - 1)
        code = code | (inner.astype(jnp.int32) << side)
    lvl = jnp.pad(wide_level, ((0, 0), (0, 0), (1, 1)))
    for repeat in range(STEPS):
        lo = repeat + 1
        hi_x = span_x - repeat - 1
        hi_y = span_y - repeat - 1
        lvl = region_step(lvl, edge[lo - 1 : hi_x - 1, lo - 1 : hi_y - 1], rate[lo:hi_x, lo:hi_y], code[lo:hi_x, lo:hi_y])
    band_here = brick_of_band.shape[0]
    lower = jnp.concatenate([neighbours[1:, 4], neighbours[:1, 4]])
    upper = jnp.concatenate([neighbours[-1:, 5], neighbours[:-1, 5]])
    first_in_z = jnp.arange(bricks_here, dtype=jnp.int32) % BZN == 0
    band_of = jnp.where(first_in_z, lower, upper)
    in_band = band_of >= 0
    owner_dev = band_of // band_here % partners
    source_dev = brick_of_band // bricks_here % partners
    matches = (owner_dev[None, :] == jnp.arange(partners)[:, None]) & in_band[None, :]
    chosen = jnp.sum(jnp.where(matches, jnp.arange(bricks_here)[None, :], 0), axis=1)
    lvl = lvl[:, :, 1:-1]
    view = lvl.reshape(BXN, BX, BYN, BY, BZN, BZ)
    sending = view.at[chosen // (BYN * BZN), :, chosen // BZN % BYN, :, chosen % BZN, :].get(
        mode="promise_in_bounds"
    )
    arrived = lax.all_to_all(sending, "dev", split_axis=0, concat_axis=0, tiled=True)
    return arrived.at[source_dev].get(mode="promise_in_bounds")


def solution(mesh):
    placed = (
        P("group", "dev", None),
        P("group", "dev", None),
        P(),
        P(("group", "dev")),
        P(("group", "dev"), None),
        P(("group", "dev")),
    )
    return jax.shard_map(
        per_device,
        mesh=mesh,
        in_specs=placed,
        out_specs=P(("group", "dev"), None, None, None),
        check_vma=False,
    )
```
